128 devices in a mesh: seq: 16 (over x_lo, z, core), batch: 8 (over y, x_hi).
Axes of the slice: x: 4 (x_hi: 2, x_lo: 2; x = x_hi * 2 + x_lo), y: 4, z: 4, core: 2. Of those that a mesh axis runs over, the one named last changes fastest.
Arguments:
- activations: bfloat16 [2, 8192, 1536], P(None, ('seq', 'batch')), may hold values from -6 to 6
- conv_gain: float32 [1536], replicated, may hold values from 0.25 to 1.75
- conv_weight: bfloat16 [5, 1536, 1536], P(None, 'batch'), may hold values from -0.0625 to 0.0625
- attention_gain: float32 [1536], replicated, may hold values from 0.25 to 1.75
- query_weight: bfloat16 [1536, 1536], P('batch'), may hold values from -3 to 3
- key_weight: bfloat16 [1536, 1536], P('batch'), may hold values from -3 to 3
- value_weight: bfloat16 [1536, 1536], P('batch'), may hold values from -0.15625 to 0.15625
- output_weight: bfloat16 [1536, 1536], P('batch'), may hold values from -0.15625 to 0.15625
Outputs:
- block_out: bfloat16 [2, 8192, 1536], P(None, ('seq', 'batch'))
The draws below stay inside these ranges and needn't reach their ends.
All inputs are finite; a program needn't handle non-finite values.
Results may differ from the reference program's by a relative error of at most 0.015.
Values may be sent and summed in bfloat16 or wider, within the bound.
No kernel may reach another device: no remote copies, remote signals or barrier semaphores. Data moves between devices by JAX's collectives and lax.ppermute only.
A program may use at most 128 MiB of HBM per device.

```python
import math
import jax
import jax.numpy as jnp
from jax import lax

D = 1536
HEADS = 8
HD = 192
KW = 5
SAMPLES = 2
LENGTH = 8192


def attention_pair(key):
    base = jax.random.fold_in(key, 7)
    spread = 1.75 / math.sqrt(D)
    query_part = jax.random.normal(jax.random.fold_in(base, 1), (D, D), jnp.float32) * spread
    key_part = jax.random.normal(jax.random.fold_in(base, 2), (D, D), jnp.float32) * spread
    query_part = jnp.clip(query_part, -3.0, 3.0)
    key_part = jnp.clip(key_part, -3.0, 3.0)
    return (query_part, key_part)


def draw_query_weight(key, part):
    return attention_pair(key)[0].astype(jnp.bfloat16)


def draw_key_weight(key, part):
    return attention_pair(key)[1].astype(jnp.bfloat16)


def shard_levels(stream_key, dims, shards, least, top_value):
    def one(dim, blocks):
        heights = jax.random.uniform(jax.random.fold_in(jax.random.fold_in(stream_key, 6), dim), (blocks,), jnp.float32, least / len(shards), top_value / len(shards))
        return jnp.repeat(jnp.exp(heights), dims[dim] // blocks).reshape((-1,) + (1,) * (len(dims) - dim - 1))

    loudness = one(*shards[0])
    for cut in shards[1:]:
        loudness = loudness * one(*cut)
    return loudness


def normal_values(rng, dims, scale, reach, cuts=(), kind=jnp.bfloat16):
    drawn = jax.random.normal(rng, dims, jnp.float32) * scale
    if len(cuts) > 0:
        drawn = shard_levels(rng, dims, cuts, -0.22, 0.18) * drawn
    return jnp.clip(drawn, min=-reach, max=reach).astype(kind)


def setup_inputs(seed: int = 0) -> dict:
    streams_of = jax.random.split(jax.random.key(seed), 9)
    activations = normal_values(streams_of[0], (SAMPLES, LENGTH, D), 1.0, 6.0, ((1, 128),))
    conv_gain = jnp.clip(1.0 + 0.15 * jax.random.normal(streams_of[1], (D,), jnp.float32), 0.25, 1.75)
    conv_weight = normal_values(streams_of[2], (KW, D, D), (KW * D) ** -0.5, 0.0625, ((1, 8),))
    attention_gain = jnp.clip(1.0 + 0.15 * jax.random.normal(streams_of[3], (D,), jnp.float32), 0.25, 1.75)
    query_weight = draw_query_weight(jax.random.fold_in(streams_of[8], 71), 0)
    key_weight = draw_key_weight(jax.random.fold_in(streams_of[8], 71), 0)
    value_weight = normal_values(streams_of[6], (D, D), D ** -0.5, 0.15625, ((0, 8),))
    output_weight = normal_values(streams_of[7], (D, D), D ** -0.5, 0.15625, ((0, 8),))
    return {"activations": activations, "conv_gain": conv_gain, "conv_weight": conv_weight, "attention_gain": attention_gain, "query_weight": query_weight, "key_weight": key_weight, "value_weight": value_weight, "output_weight": output_weight}


def normalize(values, gain):
    scale = lax.rsqrt(lax.optimization_barrier(jnp.mean(values * values, axis=-1, keepdims=True)) + 1e-06)
    return values * scale * gain

def project_rows(normed, weight):
    return jnp.dot(normed.reshape(-1, D), weight.T, preferred_element_type=jnp.float32)

def reference(activations, conv_gain, conv_weight, attention_gain, query_weight, key_weight, value_weight, output_weight):
    flank_rows = KW // 2
    x_float = activations.astype(jnp.float32)
    active = jax.nn.gelu(normalize(x_float, conv_gain)).astype(jnp.bfloat16)
    padded = jnp.pad(active, ((0, 0), (flank_rows, flank_rows), (0, 0)))
    conv_sum = jnp.zeros((SAMPLES * LENGTH, D), jnp.float32)
    for offset in range(KW):
        window = padded[:, offset:offset + LENGTH].reshape(-1, D)
        conv_sum = conv_sum + jnp.dot(window, conv_weight[offset].T, preferred_element_type=jnp.float32)
    hidden = (x_float + conv_sum.reshape(SAMPLES, LENGTH, D)).astype(jnp.bfloat16)
    normed = normalize(hidden.astype(jnp.float32), attention_gain).astype(jnp.bfloat16)
    head_shape = (SAMPLES, LENGTH, HEADS, HD)
    queries = (project_rows(normed, query_weight) * HD ** (-0.5)).astype(jnp.bfloat16).reshape(head_shape)
    key_rows = project_rows(normed, key_weight).astype(jnp.bfloat16).reshape(head_shape)
    value_rows = project_rows(normed, value_weight).astype(jnp.bfloat16).reshape(head_shape)
    block_rows = math.gcd(LENGTH, 512)
    block_count = LENGTH // block_rows
    zero_index = jnp.int32(0)

    def attend_tile(tile_id):
        sample = (tile_id // (HEADS * block_count)).astype(jnp.int32)
        head = (tile_id // block_count % HEADS).astype(jnp.int32)
        block = (tile_id % block_count).astype(jnp.int32)
        first = (block * block_rows).astype(jnp.int32)
        query_tile = lax.dynamic_slice(queries, (sample, first, head, zero_index), (1, block_rows, 1, HD)).reshape(block_rows, HD)
        key_tile = lax.dynamic_slice(key_rows, (sample, zero_index, head, zero_index), (1, LENGTH, 1, HD)).reshape(LENGTH, HD)
        value_tile = lax.dynamic_slice(value_rows, (sample, zero_index, head, zero_index), (1, LENGTH, 1, HD)).reshape(LENGTH, HD)
        scores = jnp.dot(query_tile, key_tile.T, preferred_element_type=jnp.float32)
        peak = lax.optimization_barrier(jnp.max(scores, axis=-1, keepdims=True))
        expd = jnp.exp(scores - peak)
        weight_sum = lax.optimization_barrier(jnp.sum(expd, axis=-1, keepdims=True))
        summed = jnp.dot(expd.astype(jnp.bfloat16), value_tile, preferred_element_type=jnp.float32)
        return (summed / weight_sum).astype(jnp.bfloat16)
    tile_ids = jnp.arange(SAMPLES * HEADS * block_count, dtype=jnp.int32)
    tiles = lax.map(attend_tile, tile_ids)
    attended = tiles.reshape(SAMPLES, HEADS, block_count, block_rows, HD)
    attended = jnp.transpose(attended, (0, 2, 3, 1, 4)).reshape(SAMPLES * LENGTH, D)
    branch = jnp.dot(attended, output_weight, preferred_element_type=jnp.float32)
    return (hidden.astype(jnp.float32) + branch.reshape(SAMPLES, LENGTH, D)).astype(jnp.bfloat16)
```

```python
import math

import jax
import jax.numpy as jnp
from jax import lax
from jax.sharding import PartitionSpec as P

HD = 192


def with_halo(cells, sides, width):
    for axis, dim in sides:
        count = lax.axis_size(axis)
        ends = count - 1
        head = lax.slice_in_dim(cells, 0, width, axis=dim)
        tail = lax.slice_in_dim(cells, cells.shape[dim] - width, cells.shape[dim], axis=dim)
        cells = jnp.concatenate(
            [
                lax.ppermute(tail, axis, [(i, (i + 1) % count) for i in range(ends)]),
                cells,
                lax.ppermute(head, axis, [((i + 1) % count, i) for i in range(ends)]),
            ],
            axis=dim,
        )
    return cells


def gather_batch(block, axis):
    count = lax.axis_size("batch")
    copies = jnp.broadcast_to(block[None], (count,) + block.shape)
    arrived = jnp.moveaxis(lax.all_to_all(copies, "batch", 0, 0, tiled=False), 0, axis)
    return arrived.reshape(block.shape[:axis] + (count * block.shape[axis],) + block.shape[axis + 1 :])


def normalize(rows_in, gain):
    values = rows_in.astype(jnp.float32)
    scale = lax.rsqrt(jnp.mean(values * values, axis=-1, keepdims=True) + 1e-06)
    return values * scale * gain


def shards(
    activations,
    conv_gain,
    conv_weight,
    attention_gain,
    query_weight,
    key_weight,
    value_weight,
    output_weight,
):
    sample_count, own_rows, full_width = activations.shape
    tap_count, local_out, _ = conv_weight.shape
    flank_rows = tap_count // 2
    gathered_in = gather_batch(activations, 1)
    seq_rows = gathered_in.shape[1]
    active = jax.nn.gelu(normalize(gathered_in, conv_gain)).astype(jnp.bfloat16)
    framed = with_halo(active, (("seq", 1),), flank_rows)
    conv_sum = jnp.zeros((sample_count, local_out, seq_rows), jnp.float32)
    for offset in range(tap_count):
        conv_sum = conv_sum + jnp.einsum(
            "std,ed->set",
            framed[:, offset : offset + seq_rows],
            conv_weight[offset],
            preferred_element_type=jnp.float32,
        )
    column_start = lax.axis_index("batch") * local_out
    own_columns = lax.dynamic_slice_in_dim(gathered_in, column_start, local_out, 2)
    residual = jnp.transpose(own_columns, (0, 2, 1)).astype(jnp.float32)
    hidden_part = (residual + conv_sum).astype(jnp.bfloat16)
    hidden_full = gather_batch(hidden_part, 1)
    hidden_float = hidden_full.astype(jnp.float32)
    norm_scale = lax.rsqrt(jnp.mean(hidden_float * hidden_float, axis=1, keepdims=True) + 1e-06)
    normed = (hidden_float * norm_scale * attention_gain[None, :, None]).astype(jnp.bfloat16)
    queries = (
        jnp.einsum("sdt,ed->set", normed, query_weight, preferred_element_type=jnp.float32)
        * HD ** (-0.5)
    ).astype(jnp.bfloat16)
    key_rows = jnp.einsum(
        "sdt,ed->set", normed, key_weight, preferred_element_type=jnp.float32
    ).astype(jnp.bfloat16)
    value_rows = jnp.einsum(
        "sdt,ed->set", normed, value_weight, preferred_element_type=jnp.float32
    ).astype(jnp.bfloat16)
    heads_here = query_weight.shape[0] // HD
    query_heads = queries.reshape(sample_count, heads_here, HD, seq_rows)
    start_max = jnp.full((sample_count, heads_here, seq_rows), -jnp.inf, jnp.float32)
    start_sum = jnp.zeros((sample_count, heads_here, seq_rows), jnp.float32)
    start_acc = jnp.zeros((sample_count, heads_here, HD, seq_rows), jnp.float32)
    key_tile = lax.all_gather(key_rows, "seq", axis=2, tiled=True)
    value_tile = lax.all_gather(value_rows, "seq", axis=2, tiled=True)
    key_count = key_tile.shape[2]
    block_rows = math.gcd(key_count, 512)

    def consume(block_index, running):
        running_max, weight_sum, summed = running
        begin = block_index * block_rows
        key_block = lax.dynamic_slice_in_dim(key_tile, begin, block_rows, 2).reshape(
            sample_count, heads_here, HD, block_rows
        )
        value_block = lax.dynamic_slice_in_dim(value_tile, begin, block_rows, 2).reshape(
            sample_count, heads_here, HD, block_rows
        )
        scores = jnp.einsum(
            "shdq,shdk->shqk", query_heads, key_block, preferred_element_type=jnp.float32
        )
        new_max = jnp.maximum(running_max, jnp.max(scores, axis=-1))
        weights = jnp.exp(scores - new_max[..., None])
        rescale = jnp.exp(running_max - new_max)
        weight_sum = weight_sum * rescale + jnp.sum(weights, axis=-1)
        summed = summed * rescale[:, :, None, :] + jnp.einsum(
            "shqk,shdk->shdq",
            weights.astype(jnp.bfloat16),
            value_block,
            preferred_element_type=jnp.float32,
        )
        return (new_max, weight_sum, summed)

    final_max, weight_sum, summed = lax.fori_loop(
        0, key_count // block_rows, consume, (start_max, start_sum, start_acc)
    )
    attended = (
        (summed / weight_sum[:, :, None, :])
        .astype(jnp.bfloat16)
        .reshape(sample_count, heads_here * HD, seq_rows)
    )
    row_start = lax.axis_index("batch") * own_rows
    own_hidden = jnp.transpose(
        lax.dynamic_slice_in_dim(hidden_full, row_start, own_rows, 2), (0, 2, 1)
    ).astype(jnp.float32)
    batch_count = lax.axis_size("batch")
    partial_rows = jnp.einsum(
        "set,ef->tsf", attended, output_weight, preferred_element_type=jnp.float32
    ).astype(jnp.bfloat16)
    partial_rows = partial_rows.reshape(batch_count, own_rows, sample_count, full_width)
    share_rows = jnp.sum(
        lax.all_to_all(partial_rows, "batch", 0, 0, tiled=False).astype(jnp.float32), axis=0
    )
    branch_rows = jnp.transpose(share_rows, (1, 0, 2))
    result = own_hidden + branch_rows
    return result.astype(jnp.bfloat16)


def solution(mesh):
    placed = (
        P(None, ("seq", "batch"), None),
        P(),
        P(None, "batch", None),
        P(),
        P("batch", None),
        P("batch", None),
        P("batch", None),
        P("batch", None),
    )
    return jax.shard_map(
        shards,
        mesh=mesh,
        in_specs=placed,
        out_specs=P(None, ("seq", "batch"), None),
        check_vma=False,
    )
```

```python
import math

import jax
import jax.numpy as jnp
from jax import lax
from jax.sharding import PartitionSpec as P

HD = 192


def with_halo(cells, sides, width):
    for axis, dim in sides:
        count = lax.axis_size(axis)
        ends = count - 1
        head = lax.slice_in_dim(cells, 0, width, axis=dim)
        tail = lax.slice_in_dim(cells, cells.shape[dim] - width, cells.shape[dim], axis=dim)
        cells = jnp.concatenate(
            [
                lax.ppermute(tail, axis, [(i, (i + 1) % count) for i in range(ends)]),
                cells,
                lax.ppermute(head, axis, [((i + 1) % count, i) for i in range(ends)]),
            ],
            axis=dim,
        )
    return cells


def gather_batch(block, axis):
    count = lax.axis_size("batch")
    copies = jnp.broadcast_to(block[None], (count,) + block.shape)
    arrived = jnp.moveaxis(lax.all_to_all(copies, "batch", 0, 0, tiled=False), 0, axis)
    return arrived.reshape(block.shape[:axis] + (count * block.shape[axis],) + block.shape[axis + 1 :])


def normalize(rows_in, gain):
    values = rows_in.astype(jnp.float32)
    scale = lax.rsqrt(jnp.mean(values * values, axis=-1, keepdims=True) + 1e-06)
    return values * scale * gain


def one_sample(
    activations,
    conv_gain,
    conv_weight,
    attention_gain,
    query_weight,
    key_weight,
    value_weight,
    output_weight,
):
    sample_count, own_rows, full_width = activations.shape
    tap_count, local_out, _ = conv_weight.shape
    flank_rows = tap_count // 2
    gathered_in = gather_batch(activations, 1)
    seq_rows = gathered_in.shape[1]
    active = jax.nn.gelu(normalize(gathered_in, conv_gain)).astype(jnp.bfloat16)
    framed = with_halo(active, (("seq", 1),), flank_rows)
    conv_sum = jnp.zeros((sample_count, local_out, seq_rows), jnp.float32)
    for offset in range(tap_count):
        conv_sum = conv_sum + jnp.einsum(
            "std,ed->set",
            framed[:, offset : offset + seq_rows],
            conv_weight[offset],
            preferred_element_type=jnp.float32,
        )
    column_start = lax.axis_index("batch") * local_out
    own_columns = lax.dynamic_slice_in_dim(gathered_in, column_start, local_out, 2)
    residual = jnp.transpose(own_columns, (0, 2, 1)).astype(jnp.float32)
    hidden_part = (residual + conv_sum).astype(jnp.bfloat16)
    hidden_full = gather_batch(hidden_part, 1)
    hidden_float = hidden_full.astype(jnp.float32)
    norm_scale = lax.rsqrt(jnp.mean(hidden_float * hidden_float, axis=1, keepdims=True) + 1e-06)
    normed = (hidden_float * norm_scale * attention_gain[None, :, None]).astype(jnp.bfloat16)
    queries = (
        jnp.einsum("sdt,ed->set", normed, query_weight, preferred_element_type=jnp.float32)
        * HD ** (-0.5)
    ).astype(jnp.bfloat16)
    key_rows = jnp.einsum(
        "sdt,ed->set", normed, key_weight, preferred_element_type=jnp.float32
    ).astype(jnp.bfloat16)
    value_rows = jnp.einsum(
        "sdt,ed->set", normed, value_weight, preferred_element_type=jnp.float32
    ).astype(jnp.bfloat16)
    heads_here = query_weight.shape[0] // HD
    query_heads = queries.reshape(sample_count, heads_here, HD, seq_rows)
    start_max = jnp.full((sample_count, heads_here, seq_rows), -jnp.inf, jnp.float32)
    start_sum = jnp.zeros((sample_count, heads_here, seq_rows), jnp.float32)
    start_acc = jnp.zeros((sample_count, heads_here, HD, seq_rows), jnp.float32)
    key_tile = lax.all_gather(key_rows, "seq", axis=2, tiled=True)
    value_tile = lax.all_gather(value_rows, "seq", axis=2, tiled=True)
    key_count = key_tile.shape[2]
    block_rows = math.gcd(key_count, 512)

    def consume(block_index, running):
        running_max, weight_sum, summed = running
        begin = block_index * block_rows
        key_block = lax.dynamic_slice_in_dim(key_tile, begin, block_rows, 2).reshape(
            sample_count, heads_here, HD, block_rows
        )
        value_block = lax.dynamic_slice_in_dim(value_tile, begin, block_rows, 2).reshape(
            sample_count, heads_here, HD, block_rows
        )
        scores = jnp.einsum(
            "shdq,shdk->shqk", query_heads, key_block, preferred_element_type=jnp.float32
        )
        new_max = jnp.maximum(running_max, jnp.max(scores, axis=-1))
        weights = jnp.exp(scores - new_max[..., None])
        rescale = jnp.exp(running_max - new_max)
        weight_sum = weight_sum * rescale + jnp.sum(weights, axis=-1)
        summed = summed * rescale[:, :, None, :] + jnp.einsum(
            "shqk,shdk->shdq",
            weights.astype(jnp.bfloat16),
            value_block,
            preferred_element_type=jnp.float32,
        )
        return (new_max, weight_sum, summed)

    final_max, weight_sum, summed = lax.fori_loop(
        0, key_count // block_rows, consume, (start_max, start_sum, start_acc)
    )
    attended = (
        (summed / weight_sum[:, :, None, :])
        .astype(jnp.bfloat16)
        .reshape(sample_count, heads_here * HD, seq_rows)
    )
    row_start = lax.axis_index("batch") * own_rows
    own_hidden = jnp.transpose(
        lax.dynamic_slice_in_dim(hidden_full, row_start, own_rows, 2), (0, 2, 1)
    ).astype(jnp.float32)
    batch_count = lax.axis_size("batch")
    partial_rows = jnp.einsum(
        "set,ef->tsf", attended, output_weight, preferred_element_type=jnp.float32
    ).astype(jnp.bfloat16)
    partial_rows = partial_rows.reshape(batch_count, own_rows, sample_count, full_width)
    share_rows = jnp.sum(
        lax.all_to_all(partial_rows, "batch", 0, 0, tiled=False).astype(jnp.float32), axis=0
    )
    branch_rows = jnp.transpose(share_rows, (1, 0, 2))
    result = own_hidden + branch_rows
    return result.astype(jnp.bfloat16)


def shards(activations, *weights):
    pieces = [
        one_sample(activations[sample : sample + 1], *weights)
        for sample in range(activations.shape[0])
    ]
    return jnp.concatenate(pieces, axis=0)


def solution(mesh):
    placed = (
        P(None, ("seq", "batch"), None),
        P(),
        P(None, "batch", None),
        P(),
        P("batch", None),
        P("batch", None),
        P("batch", None),
        P("batch", None),
    )
    return jax.shard_map(
        shards,
        mesh=mesh,
        in_specs=placed,
        out_specs=P(None, ("seq", "batch"), None),
        check_vma=False,
    )
```

```python
import math

import jax
import jax.numpy as jnp
from jax import lax
from jax.experimental import pallas as pl
from jax.experimental.pallas import tpu as pltpu
from jax.sharding import PartitionSpec as P

HD = 192


def with_halo(cells, sides, width):
    for axis, dim in sides:
        count = lax.axis_size(axis)
        ends = count - 1
        head = lax.slice_in_dim(cells, 0, width, axis=dim)
        tail = lax.slice_in_dim(cells, cells.shape[dim] - width, cells.shape[dim], axis=dim)
        cells = jnp.concatenate(
            [
                lax.ppermute(tail, axis, [(i, (i + 1) % count) for i in range(ends)]),
                cells,
                lax.ppermute(head, axis, [((i + 1) % count, i) for i in range(ends)]),
            ],
            axis=dim,
        )
    return cells


def gather_batch(block, axis):
    count = lax.axis_size("batch")
    copies = jnp.broadcast_to(block[None], (count,) + block.shape)
    arrived = jnp.moveaxis(lax.all_to_all(copies, "batch", 0, 0, tiled=False), 0, axis)
    return arrived.reshape(block.shape[:axis] + (count * block.shape[axis],) + block.shape[axis + 1 :])


def flash_step(query_ref, key_ref, value_ref, out_ref, peak_ref, total_ref, summed_ref):
    block = pl.program_id(1)

    @pl.when(block == 0)
    def _():
        peak_ref[...] = jnp.full(peak_ref.shape, -jnp.inf, jnp.float32)
        total_ref[...] = jnp.zeros(total_ref.shape, jnp.float32)
        summed_ref[...] = jnp.zeros(summed_ref.shape, jnp.float32)

    scores = jnp.dot(query_ref[0], key_ref[0], preferred_element_type=jnp.float32)
    old_peak = peak_ref[...]
    new_peak = jnp.maximum(old_peak, jnp.max(scores, axis=1, keepdims=True))
    weights = jnp.exp(scores - new_peak)
    rescale = jnp.exp(old_peak - new_peak)
    total_ref[...] = total_ref[...] * rescale + jnp.sum(weights, axis=1, keepdims=True)
    summed_ref[...] = summed_ref[...] * rescale + jnp.dot(
        weights.astype(jnp.bfloat16), value_ref[0], preferred_element_type=jnp.float32
    )
    peak_ref[...] = new_peak

    @pl.when(block == pl.num_programs(1) - 1)
    def _():
        out_ref[0] = (summed_ref[...] / total_ref[...]).astype(out_ref.dtype)


def flash_attention(queries, keys, values, key_block=1024):
    sample_count, query_count, head_width = queries.shape
    key_count = keys.shape[2]
    key_block = math.gcd(key_count, key_block)
    return pl.pallas_call(
        flash_step,
        grid=(sample_count, key_count // key_block),
        in_specs=[
            pl.BlockSpec((1, query_count, head_width), lambda s, k: (s, 0, 0)),
            pl.BlockSpec((1, head_width, key_block), lambda s, k: (s, 0, k)),
            pl.BlockSpec((1, key_block, head_width), lambda s, k: (s, k, 0)),
        ],
        out_specs=pl.BlockSpec((1, query_count, head_width), lambda s, k: (s, 0, 0)),
        out_shape=jax.ShapeDtypeStruct(queries.shape, jnp.bfloat16),
        scratch_shapes=[
            pltpu.VMEM((query_count, 1), jnp.float32),
            pltpu.VMEM((query_count, 1), jnp.float32),
            pltpu.VMEM((query_count, head_width), jnp.float32),
        ],
        compiler_params=pltpu.CompilerParams(dimension_semantics=("parallel", "arbitrary")),
    )(queries, keys, values)


def normalize(rows_in, gain):
    values = rows_in.astype(jnp.float32)
    scale = lax.rsqrt(jnp.mean(values * values, axis=-1, keepdims=True) + 1e-06)
    return values * scale * gain


def shards(
    activations,
    conv_gain,
    conv_weight,
    attention_gain,
    query_weight,
    key_weight,
    value_weight,
    output_weight,
):
    sample_count, own_rows, full_width = activations.shape
    tap_count, local_out, _ = conv_weight.shape
    flank_rows = tap_count // 2
    gathered_in = gather_batch(activations, 1)
    seq_rows = gathered_in.shape[1]
    active = jax.nn.gelu(normalize(gathered_in, conv_gain)).astype(jnp.bfloat16)
    framed = with_halo(active, (("seq", 1),), flank_rows)
    conv_sum = jnp.zeros((sample_count, local_out, seq_rows), jnp.float32)
    for offset in range(tap_count):
        conv_sum = conv_sum + jnp.einsum(
            "std,ed->set",
            framed[:, offset : offset + seq_rows],
            conv_weight[offset],
            preferred_element_type=jnp.float32,
        )
    column_start = lax.axis_index("batch") * local_out
    own_columns = lax.dynamic_slice_in_dim(gathered_in, column_start, local_out, 2)
    residual = jnp.transpose(own_columns, (0, 2, 1)).astype(jnp.float32)
    hidden_part = (residual + conv_sum).astype(jnp.bfloat16)
    hidden_full = gather_batch(hidden_part, 1)
    hidden_float = hidden_full.astype(jnp.float32)
    norm_scale = lax.rsqrt(jnp.mean(hidden_float * hidden_float, axis=1, keepdims=True) + 1e-06)
    normed = (hidden_float * norm_scale * attention_gain[None, :, None]).astype(jnp.bfloat16)
    queries = (
        jnp.einsum("sdt,ed->ste", normed, query_weight, preferred_element_type=jnp.float32)
        * HD ** (-0.5)
    ).astype(jnp.bfloat16)
    key_rows = jnp.einsum(
        "sdt,ed->set", normed, key_weight, preferred_element_type=jnp.float32
    ).astype(jnp.bfloat16)
    value_rows = jnp.einsum(
        "sdt,ed->ste", normed, value_weight, preferred_element_type=jnp.float32
    ).astype(jnp.bfloat16)
    key_tile = lax.all_gather(key_rows, "seq", axis=2, tiled=True)
    value_tile = lax.all_gather(value_rows, "seq", axis=1, tiled=True)
    attended = flash_attention(queries, key_tile, value_tile)
    row_start = lax.axis_index("batch") * own_rows
    own_hidden = jnp.transpose(
        lax.dynamic_slice_in_dim(hidden_full, row_start, own_rows, 2), (0, 2, 1)
    ).astype(jnp.float32)
    batch_count = lax.axis_size("batch")
    partial_rows = jnp.einsum(
        "ste,ef->tsf", attended, output_weight, preferred_element_type=jnp.float32
    ).astype(jnp.bfloat16)
    partial_rows = partial_rows.reshape(batch_count, own_rows, sample_count, full_width)
    share_rows = jnp.sum(
        lax.all_to_all(partial_rows, "batch", 0, 0, tiled=False).astype(jnp.float32), axis=0
    )
    branch_rows = jnp.transpose(share_rows, (1, 0, 2))
    result = own_hidden + branch_rows
    return result.astype(jnp.bfloat16)


def solution(mesh):
    placed = (
        P(None, ("seq", "batch"), None),
        P(),
        P(None, "batch", None),
        P(),
        P("batch", None),
        P("batch", None),
        P("batch", None),
        P("batch", None),
    )
    return jax.shard_map(
        shards,
        mesh=mesh,
        in_specs=placed,
        out_specs=P(None, ("seq", "batch"), None),
        check_vma=False,
    )
```

```python
import math

import jax
import jax.numpy as jnp
from jax import lax
from jax.experimental import pallas as pl
from jax.experimental.pallas import tpu as pltpu
from jax.sharding import PartitionSpec as P

HD = 192


def with_halo(cells, sides, width):
    for axis, dim in sides:
        count = lax.axis_size(axis)
        ends = count - 1
        head = lax.slice_in_dim(cells, 0, width, axis=dim)
        tail = lax.slice_in_dim(cells, cells.shape[dim] - width, cells.shape[dim], axis=dim)
        cells = jnp.concatenate(
            [
                lax.ppermute(tail, axis, [(i, (i + 1) % count) for i in range(ends)]),
                cells,
                lax.ppermute(head, axis, [((i + 1) % count, i) for i in range(ends)]),
            ],
            axis=dim,
        )
    return cells


def gather_batch(block, axis):
    count = lax.axis_size("batch")
    copies = jnp.broadcast_to(block[None], (count,) + block.shape)
    arrived = jnp.moveaxis(lax.all_to_all(copies, "batch", 0, 0, tiled=False), 0, axis)
    return arrived.reshape(block.shape[:axis] + (count * block.shape[axis],) + block.shape[axis + 1 :])


def flash_step(query_ref, key_ref, value_ref, out_ref, peak_ref, total_ref, summed_ref):
    block = pl.program_id(1)

    @pl.when(block == 0)
    def _():
        peak_ref[...] = jnp.full(peak_ref.shape, -jnp.inf, jnp.float32)
        total_ref[...] = jnp.zeros(total_ref.shape, jnp.float32)
        summed_ref[...] = jnp.zeros(summed_ref.shape, jnp.float32)

    scores = jnp.dot(query_ref[0], key_ref[0], preferred_element_type=jnp.float32)
    old_peak = peak_ref[...]
    new_peak = jnp.maximum(old_peak, jnp.max(scores, axis=1, keepdims=True))
    weights = jnp.exp(scores - new_peak)
    rescale = jnp.exp(old_peak - new_peak)
    total_ref[...] = total_ref[...] * rescale + jnp.sum(weights, axis=1, keepdims=True)
    summed_ref[...] = summed_ref[...] * rescale + jnp.dot(
        weights.astype(jnp.bfloat16), value_ref[0], preferred_element_type=jnp.float32
    )
    peak_ref[...] = new_peak

    @pl.when(block == pl.num_programs(1) - 1)
    def _():
        out_ref[0] = (summed_ref[...] / total_ref[...]).astype(out_ref.dtype)


def flash_attention(queries, keys, values, key_block=1024):
    sample_count, query_count, head_width = queries.shape
    key_count = keys.shape[2]
    key_block = math.gcd(key_count, key_block)
    return pl.pallas_call(
        flash_step,
        grid=(sample_count, key_count // key_block),
        in_specs=[
            pl.BlockSpec((1, query_count, head_width), lambda s, k: (s, 0, 0)),
            pl.BlockSpec((1, head_width, key_block), lambda s, k: (s, 0, k)),
            pl.BlockSpec((1, key_block, head_width), lambda s, k: (s, k, 0)),
        ],
        out_specs=pl.BlockSpec((1, query_count, head_width), lambda s, k: (s, 0, 0)),
        out_shape=jax.ShapeDtypeStruct(queries.shape, jnp.bfloat16),
        scratch_shapes=[
            pltpu.VMEM((query_count, 1), jnp.float32),
            pltpu.VMEM((query_count, 1), jnp.float32),
            pltpu.VMEM((query_count, head_width), jnp.float32),
        ],
        compiler_params=pltpu.CompilerParams(dimension_semantics=("parallel", "arbitrary")),
    )(queries, keys, values)


def normalize(rows_in, gain):
    values = rows_in.astype(jnp.float32)
    scale = lax.rsqrt(jnp.mean(values * values, axis=-1, keepdims=True) + 1e-06)
    return values * scale * gain


def shards(
    activations,
    conv_gain,
    conv_weight,
    attention_gain,
    query_weight,
    key_weight,
    value_weight,
    output_weight,
):
    sample_count, own_rows, full_width = activations.shape
    tap_count, local_out, _ = conv_weight.shape
    flank_rows = tap_count // 2
    gathered_in = gather_batch(activations, 1)
    seq_rows = gathered_in.shape[1]
    active = jax.nn.gelu(normalize(gathered_in, conv_gain)).astype(jnp.bfloat16)
    framed = with_halo(active, (("seq", 1),), flank_rows)
    conv_sum = jnp.zeros((sample_count, local_out, seq_rows), jnp.float32)
    for offset in range(tap_count):
        conv_sum = conv_sum + jnp.einsum(
            "std,ed->set",
            framed[:, offset : offset + seq_rows],
            conv_weight[offset],
            preferred_element_type=jnp.float32,
        )
    column_start = lax.axis_index("batch") * local_out
    own_columns = lax.dynamic_slice_in_dim(gathered_in, column_start, local_out, 2)
    residual = jnp.transpose(own_columns, (0, 2, 1)).astype(jnp.float32)
    hidden_part = (residual + conv_sum).astype(jnp.bfloat16)
    hidden_full = gather_batch(hidden_part, 1)
    hidden_float = hidden_full.astype(jnp.float32)
    norm_scale = lax.rsqrt(jnp.mean(hidden_float * hidden_float, axis=1, keepdims=True) + 1e-06)
    normed = (hidden_float * norm_scale * attention_gain[None, :, None]).astype(jnp.bfloat16)
    queries = (
        jnp.einsum("sdt,ed->ste", normed, query_weight, preferred_element_type=jnp.float32)
        * HD ** (-0.5)
    ).astype(jnp.bfloat16)
    key_rows = jnp.einsum(
        "sdt,ed->set", normed, key_weight, preferred_element_type=jnp.float32
    ).astype(jnp.bfloat16)
    value_rows = jnp.einsum(
        "sdt,ed->ste", normed, value_weight, preferred_element_type=jnp.float32
    ).astype(jnp.bfloat16)
    seq_count = lax.axis_size("seq")
    mine = lax.axis_index("seq") % 2
    pair = [(index, index ^ 1) for index in range(seq_count)]
    own_queries = lax.dynamic_index_in_dim(queries, mine, 0, keepdims=False)
    other_queries = lax.dynamic_index_in_dim(queries, 1 - mine, 0, keepdims=False)
    query_block = jnp.concatenate([own_queries, lax.ppermute(other_queries, "seq", pair)], 0)
    head_width = key_rows.shape[1]
    value_flat = value_rows.reshape(sample_count, head_width, seq_rows)
    outgoing = jnp.broadcast_to(
        jnp.stack([key_rows, value_flat], axis=1)[None],
        (seq_count // sample_count, sample_count, 2, head_width, seq_rows),
    ).reshape(seq_count, 2, head_width, seq_rows)
    incoming = lax.all_to_all(outgoing, "seq", 0, 0, tiled=False)
    key_tile = jnp.moveaxis(incoming[:, 0], 0, 1).reshape(1, head_width, seq_count * seq_rows)
    value_tile = incoming[:, 1].reshape(1, seq_count * seq_rows, head_width)
    attended = flash_attention(query_block[None], key_tile, value_tile)[0]
    row_start = lax.axis_index("batch") * own_rows
    own_hidden = jnp.transpose(
        lax.dynamic_slice_in_dim(hidden_full, row_start, own_rows, 2), (0, 2, 1)
    ).astype(jnp.float32)
    batch_count = lax.axis_size("batch")
    partial_rows = jnp.dot(attended, output_weight, preferred_element_type=jnp.float32)
    partial_rows = jnp.transpose(
        partial_rows.astype(jnp.bfloat16).reshape(2, batch_count, own_rows, full_width), (1, 0, 2, 3)
    )
    share_rows = jnp.sum(
        lax.all_to_all(partial_rows, "batch", 0, 0, tiled=False).astype(jnp.float32), axis=0
    )
    from_partner = lax.ppermute(share_rows[1], "seq", pair)
    branch_rows = jnp.where(
        mine == 0,
        jnp.stack([share_rows[0], from_partner]),
        jnp.stack([from_partner, share_rows[0]]),
    )
    result = own_hidden + branch_rows
    return result.astype(jnp.bfloat16)


def solution(mesh):
    placed = (
        P(None, ("seq", "batch"), None),
        P(),
        P(None, "batch", None),
        P(),
        P("batch", None),
        P("batch", None),
        P("batch", None),
        P("batch", None),
    )
    return jax.shard_map(
        shards,
        mesh=mesh,
        in_specs=placed,
        out_specs=P(None, ("seq", "batch"), None),
        check_vma=False,
    )
```

```python
import math

import jax
import jax.numpy as jnp
from jax import lax
from jax.experimental import pallas as pl
from jax.experimental.pallas import tpu as pltpu
from jax.sharding import PartitionSpec as P

HD = 192


def with_halo(cells, sides, width):
    for axis, dim in sides:
        count = lax.axis_size(axis)
        ends = count - 1
        head = lax.slice_in_dim(cells, 0, width, axis=dim)
        tail = lax.slice_in_dim(cells, cells.shape[dim] - width, cells.shape[dim], axis=dim)
        cells = jnp.concatenate(
            [
                lax.ppermute(tail, axis, [(i, (i + 1) % count) for i in range(ends)]),
                cells,
                lax.ppermute(head, axis, [((i + 1) % count, i) for i in range(ends)]),
            ],
            axis=dim,
        )
    return cells


def gather_batch(block, axis):
    count = lax.axis_size("batch")
    copies = jnp.broadcast_to(block[None], (count,) + block.shape)
    arrived = jnp.moveaxis(lax.all_to_all(copies, "batch", 0, 0, tiled=False), 0, axis)
    return arrived.reshape(block.shape[:axis] + (count * block.shape[axis],) + block.shape[axis + 1 :])


def flash_step(query_ref, kv_ref, out_ref, peak_ref, total_ref, summed_ref):
    block = pl.program_id(1)

    @pl.when(block == 0)
    def _():
        peak_ref[...] = jnp.full(peak_ref.shape, -jnp.inf, jnp.float32)
        total_ref[...] = jnp.zeros(total_ref.shape, jnp.float32)
        summed_ref[...] = jnp.zeros(summed_ref.shape, jnp.float32)

    query = query_ref[0]
    pieces = [
        jnp.dot(query, kv_ref[part, 0, 0], preferred_element_type=jnp.float32)
        for part in range(kv_ref.shape[0])
    ]
    old_peak = peak_ref[...]
    new_peak = old_peak
    for scores in pieces:
        new_peak = jnp.maximum(new_peak, jnp.max(scores, axis=1, keepdims=True))
    rescale = jnp.exp(old_peak - new_peak)
    total = total_ref[...] * rescale
    summed = summed_ref[...] * rescale
    for part, scores in enumerate(pieces):
        weights = jnp.exp(scores - new_peak)
        total = total + jnp.sum(weights, axis=1, keepdims=True)
        summed = summed + lax.dot_general(
            weights.astype(jnp.bfloat16),
            kv_ref[part, 0, 1],
            (((1,), (1,)), ((), ())),
            preferred_element_type=jnp.float32,
        )
    total_ref[...] = total
    summed_ref[...] = summed
    peak_ref[...] = new_peak

    @pl.when(block == pl.num_programs(1) - 1)
    def _():
        out_ref[0] = (summed_ref[...] / total_ref[...]).astype(out_ref.dtype)


def flash_attention(queries, kv_tile, sources_per_step=2):
    sample_count, query_count, head_width = queries.shape
    source_count, _, _, _, source_rows = kv_tile.shape
    sources_per_step = math.gcd(source_count, sources_per_step)
    return pl.pallas_call(
        flash_step,
        grid=(sample_count, source_count // sources_per_step),
        in_specs=[
            pl.BlockSpec((1, query_count, head_width), lambda s, k: (s, 0, 0)),
            pl.BlockSpec(
                (sources_per_step, 1, 2, head_width, source_rows), lambda s, k: (k, s, 0, 0, 0)
            ),
        ],
        out_specs=pl.BlockSpec((1, query_count, head_width), lambda s, k: (s, 0, 0)),
        out_shape=jax.ShapeDtypeStruct(queries.shape, jnp.bfloat16),
        scratch_shapes=[
            pltpu.VMEM((query_count, 1), jnp.float32),
            pltpu.VMEM((query_count, 1), jnp.float32),
            pltpu.VMEM((query_count, head_width), jnp.float32),
        ],
        compiler_params=pltpu.CompilerParams(dimension_semantics=("parallel", "arbitrary")),
    )(queries, kv_tile)


def normalize(rows_in, gain):
    values = rows_in.astype(jnp.float32)
    scale = lax.rsqrt(jnp.mean(values * values, axis=-1, keepdims=True) + 1e-06)
    return values * scale * gain


def shards(
    activations,
    conv_gain,
    conv_weight,
    attention_gain,
    query_weight,
    key_weight,
    value_weight,
    output_weight,
):
    sample_count, own_rows, full_width = activations.shape
    tap_count, local_out, _ = conv_weight.shape
    flank_rows = tap_count // 2
    gathered_in = gather_batch(activations, 1)
    seq_rows = gathered_in.shape[1]
    active = jax.nn.gelu(normalize(gathered_in, conv_gain)).astype(jnp.bfloat16)
    framed = with_halo(active, (("seq", 1),), flank_rows)
    conv_sum = jnp.zeros((sample_count, local_out, seq_rows), jnp.float32)
    for offset in range(tap_count):
        conv_sum = conv_sum + jnp.einsum(
            "std,ed->set",
            framed[:, offset : offset + seq_rows],
            conv_weight[offset],
            preferred_element_type=jnp.float32,
        )
    column_start = lax.axis_index("batch") * local_out
    own_columns = lax.dynamic_slice_in_dim(gathered_in, column_start, local_out, 2)
    residual = jnp.transpose(own_columns, (0, 2, 1)).astype(jnp.float32)
    hidden_part = (residual + conv_sum).astype(jnp.bfloat16)
    hidden_full = gather_batch(hidden_part, 1)
    hidden_float = hidden_full.astype(jnp.float32)
    norm_scale = lax.rsqrt(jnp.mean(hidden_float * hidden_float, axis=1, keepdims=True) + 1e-06)
    normed = (hidden_float * norm_scale * attention_gain[None, :, None]).astype(jnp.bfloat16)
    queries = (
        jnp.einsum("sdt,ed->ste", normed, query_weight, preferred_element_type=jnp.float32)
        * HD ** (-0.5)
    ).astype(jnp.bfloat16)
    key_rows = jnp.einsum(
        "sdt,ed->set", normed, key_weight, preferred_element_type=jnp.float32
    ).astype(jnp.bfloat16)
    value_rows = jnp.einsum(
        "sdt,ed->set", normed, value_weight, preferred_element_type=jnp.float32
    ).astype(jnp.bfloat16)
    kv_tile = lax.all_gather(jnp.stack([key_rows, value_rows], axis=1), "seq", axis=0)
    attended = flash_attention(queries, kv_tile)
    row_start = lax.axis_index("batch") * own_rows
    own_hidden = jnp.transpose(
        lax.dynamic_slice_in_dim(hidden_full, row_start, own_rows, 2), (0, 2, 1)
    ).astype(jnp.float32)
    batch_count = lax.axis_size("batch")
    partial_rows = jnp.einsum(
        "ste,ef->tsf", attended, output_weight, preferred_element_type=jnp.float32
    ).astype(jnp.bfloat16)
    partial_rows = partial_rows.reshape(batch_count, own_rows, sample_count, full_width)
    share_rows = jnp.sum(
        lax.all_to_all(partial_rows, "batch", 0, 0, tiled=False).astype(jnp.float32), axis=0
    )
    branch_rows = jnp.transpose(share_rows, (1, 0, 2))
    result = own_hidden + branch_rows
    return result.astype(jnp.bfloat16)


def solution(mesh):
    placed = (
        P(None, ("seq", "batch"), None),
        P(),
        P(None, "batch", None),
        P(),
        P("batch", None),
        P("batch", None),
        P("batch", None),
        P("batch", None),
    )
    return jax.shard_map(
        shards,
        mesh=mesh,
        in_specs=placed,
        out_specs=P(None, ("seq", "batch"), None),
        check_vma=False,
    )
```

```python
import math

import jax
import jax.numpy as jnp
from jax import lax
from jax.experimental import pallas as pl
from jax.experimental.pallas import tpu as pltpu
from jax.sharding import PartitionSpec as P

HD = 192


def with_halo(cells, sides, width):
    for axis, dim in sides:
        count = lax.axis_size(axis)
        ends = count - 1
        head = lax.slice_in_dim(cells, 0, width, axis=dim)
        tail = lax.slice_in_dim(cells, cells.shape[dim] - width, cells.shape[dim], axis=dim)
        cells = jnp.concatenate(
            [
                lax.ppermute(tail, axis, [(i, (i + 1) % count) for i in range(ends)]),
                cells,
                lax.ppermute(head, axis, [((i + 1) % count, i) for i in range(ends)]),
            ],
            axis=dim,
        )
    return cells


def gather_batch(block, axis):
    count = lax.axis_size("batch")
    copies = jnp.broadcast_to(block[None], (count,) + block.shape)
    arrived = jnp.moveaxis(lax.all_to_all(copies, "batch", 0, 0, tiled=False), 0, axis)
    return arrived.reshape(block.shape[:axis] + (count * block.shape[axis],) + block.shape[axis + 1 :])


def flash_step(query_ref, key_ref, value_ref, out_ref, peak_ref, total_ref, summed_ref):
    block = pl.program_id(1)

    @pl.when(block == 0)
    def _():
        peak_ref[...] = jnp.full(peak_ref.shape, -jnp.inf, jnp.float32)
        total_ref[...] = jnp.zeros(total_ref.shape, jnp.float32)
        summed_ref[...] = jnp.zeros(summed_ref.shape, jnp.float32)

    query = query_ref[0]
    pieces = [
        jnp.dot(query, key_ref[0, part, 0], preferred_element_type=jnp.float32)
        for part in range(key_ref.shape[1])
    ]
    old_peak = peak_ref[...]
    new_peak = old_peak
    for scores in pieces:
        new_peak = jnp.maximum(new_peak, jnp.max(scores, axis=1, keepdims=True))
    rescale = jnp.exp(old_peak - new_peak)
    total = total_ref[...] * rescale
    summed = summed_ref[...] * rescale
    for part, scores in enumerate(pieces):
        weights = jnp.exp(scores - new_peak)
        total = total + jnp.sum(weights, axis=1, keepdims=True)
        summed = summed + lax.dot_general(
            weights.astype(jnp.bfloat16),
            value_ref[0, part, 0],
            (((1,), (1,)), ((), ())),
            preferred_element_type=jnp.float32,
        )
    total_ref[...] = total
    summed_ref[...] = summed
    peak_ref[...] = new_peak

    @pl.when(block == pl.num_programs(1) - 1)
    def _():
        out_ref[0] = (summed_ref[...] / total_ref[...]).astype(out_ref.dtype)


def flash_attention(queries, kv_tile, sources_per_step=2):
    sample_count, query_count, head_width = queries.shape
    _, source_count, _, _, source_rows = kv_tile.shape
    sources_per_step = math.gcd(source_count, sources_per_step)
    return pl.pallas_call(
        flash_step,
        grid=(sample_count, source_count // sources_per_step),
        in_specs=[
            pl.BlockSpec((1, query_count, head_width), lambda s, k: (s, 0, 0)),
            pl.BlockSpec(
                (1, sources_per_step, 1, head_width, source_rows), lambda s, k: (0, k, s, 0, 0)
            ),
            pl.BlockSpec(
                (1, sources_per_step, 1, head_width, source_rows), lambda s, k: (1, k, s, 0, 0)
            ),
        ],
        out_specs=pl.BlockSpec((1, query_count, head_width), lambda s, k: (s, 0, 0)),
        out_shape=jax.ShapeDtypeStruct(queries.shape, jnp.bfloat16),
        scratch_shapes=[
            pltpu.VMEM((query_count, 1), jnp.float32),
            pltpu.VMEM((query_count, 1), jnp.float32),
            pltpu.VMEM((query_count, head_width), jnp.float32),
        ],
        compiler_params=pltpu.CompilerParams(dimension_semantics=("parallel", "arbitrary")),
    )(queries, kv_tile, kv_tile)


def normalize(rows_in, gain):
    values = rows_in.astype(jnp.float32)
    scale = lax.rsqrt(jnp.mean(values * values, axis=-1, keepdims=True) + 1e-06)
    return values * scale * gain


def shards(
    activations,
    conv_gain,
    conv_weight,
    attention_gain,
    query_weight,
    key_weight,
    value_weight,
    output_weight,
):
    sample_count, own_rows, full_width = activations.shape
    tap_count, local_out, _ = conv_weight.shape
    flank_rows = tap_count // 2
    gathered_in = gather_batch(activations, 1)
    seq_rows = gathered_in.shape[1]
    active = jax.nn.gelu(normalize(gathered_in, conv_gain)).astype(jnp.bfloat16)
    framed = with_halo(active, (("seq", 1),), flank_rows)
    conv_sum = jnp.zeros((sample_count, local_out, seq_rows), jnp.float32)
    for offset in range(tap_count):
        conv_sum = conv_sum + jnp.einsum(
            "std,ed->set",
            framed[:, offset : offset + seq_rows],
            conv_weight[offset],
            preferred_element_type=jnp.float32,
        )
    column_start = lax.axis_index("batch") * local_out
    own_columns = lax.dynamic_slice_in_dim(gathered_in, column_start, local_out, 2)
    residual = jnp.transpose(own_columns, (0, 2, 1)).astype(jnp.float32)
    hidden_part = (residual + conv_sum).astype(jnp.bfloat16)
    hidden_full = gather_batch(hidden_part, 1)
    hidden_float = hidden_full.astype(jnp.float32)
    norm_scale = lax.rsqrt(jnp.mean(hidden_float * hidden_float, axis=1, keepdims=True) + 1e-06)
    normed = (hidden_float * norm_scale * attention_gain[None, :, None]).astype(jnp.bfloat16)
    queries = (
        jnp.einsum("sdt,ed->ste", normed, query_weight, preferred_element_type=jnp.float32)
        * HD ** (-0.5)
    ).astype(jnp.bfloat16)
    key_rows = jnp.einsum(
        "sdt,ed->set", normed, key_weight, preferred_element_type=jnp.float32
    ).astype(jnp.bfloat16)
    value_rows = jnp.einsum(
        "sdt,ed->set", normed, value_weight, preferred_element_type=jnp.float32
    ).astype(jnp.bfloat16)
    kv_tile = lax.all_gather(jnp.stack([key_rows, value_rows]), "seq", axis=1)
    attended = flash_attention(queries, kv_tile)
    row_start = lax.axis_index("batch") * own_rows
    own_hidden = jnp.transpose(
        lax.dynamic_slice_in_dim(hidden_full, row_start, own_rows, 2), (0, 2, 1)
    ).astype(jnp.float32)
    batch_count = lax.axis_size("batch")
    partial_rows = jnp.einsum(
        "ste,ef->tsf", attended, output_weight, preferred_element_type=jnp.float32
    ).astype(jnp.bfloat16)
    partial_rows = partial_rows.reshape(batch_count, own_rows, sample_count, full_width)
    share_rows = jnp.sum(
        lax.all_to_all(partial_rows, "batch", 0, 0, tiled=False).astype(jnp.float32), axis=0
    )
    branch_rows = jnp.transpose(share_rows, (1, 0, 2))
    result = own_hidden + branch_rows
    return result.astype(jnp.bfloat16)


def solution(mesh):
    placed = (
        P(None, ("seq", "batch"), None),
        P(),
        P(None, "batch", None),
        P(),
        P("batch", None),
        P("batch", None),
        P("batch", None),
        P("batch", None),
    )
    return jax.shard_map(
        shards,
        mesh=mesh,
        in_specs=placed,
        out_specs=P(None, ("seq", "batch"), None),
        check_vma=False,
    )
```

```python
import math

import jax
import jax.numpy as jnp
from jax import lax
from jax.experimental import pallas as pl
from jax.experimental.pallas import tpu as pltpu
from jax.sharding import PartitionSpec as P

HD = 192


def with_halo(cells, sides, width):
    for axis, dim in sides:
        count = lax.axis_size(axis)
        ends = count - 1
        head = lax.slice_in_dim(cells, 0, width, axis=dim)
        tail = lax.slice_in_dim(cells, cells.shape[dim] - width, cells.shape[dim], axis=dim)
        cells = jnp.concatenate(
            [
                lax.ppermute(tail, axis, [(i, (i + 1) % count) for i in range(ends)]),
                cells,
                lax.ppermute(head, axis, [((i + 1) % count, i) for i in range(ends)]),
            ],
            axis=dim,
        )
    return cells


def gather_batch(block, axis):
    count = lax.axis_size("batch")
    copies = jnp.broadcast_to(block[None], (count,) + block.shape)
    arrived = jnp.moveaxis(lax.all_to_all(copies, "batch", 0, 0, tiled=False), 0, axis)
    return arrived.reshape(block.shape[:axis] + (count * block.shape[axis],) + block.shape[axis + 1 :])


def flash_step(query_ref, key_ref, value_ref, out_ref, peak_ref, total_ref, summed_ref):
    block = pl.program_id(1)

    @pl.when(block == 0)
    def _():
        peak_ref[...] = jnp.full(peak_ref.shape, -jnp.inf, jnp.float32)
        total_ref[...] = jnp.zeros(total_ref.shape, jnp.float32)
        summed_ref[...] = jnp.zeros(summed_ref.shape, jnp.float32)

    query = query_ref[0]
    pieces = [
        jnp.dot(query, key_ref[0, part, 0], preferred_element_type=jnp.float32)
        for part in range(key_ref.shape[1])
    ]
    old_peak = peak_ref[...]
    new_peak = old_peak
    for scores in pieces:
        new_peak = jnp.maximum(new_peak, jnp.max(scores, axis=1, keepdims=True))
    rescale = jnp.exp(old_peak - new_peak)
    total = total_ref[...] * rescale
    summed = summed_ref[...] * rescale
    for part, scores in enumerate(pieces):
        weights = jnp.exp(scores - new_peak)
        total = total + jnp.sum(weights, axis=1, keepdims=True)
        summed = summed + lax.dot_general(
            weights.astype(jnp.bfloat16),
            value_ref[0, part, 0],
            (((1,), (1,)), ((), ())),
            preferred_element_type=jnp.float32,
        )
    total_ref[...] = total
    summed_ref[...] = summed
    peak_ref[...] = new_peak

    @pl.when(block == pl.num_programs(1) - 1)
    def _():
        out_ref[0] = (summed_ref[...] / total_ref[...]).astype(out_ref.dtype)


def flash_attention(queries, kv_tile, sources_per_step=2):
    sample_count, query_count, head_width = queries.shape
    _, source_count, _, _, source_rows = kv_tile.shape
    sources_per_step = math.gcd(source_count, sources_per_step)
    return pl.pallas_call(
        flash_step,
        grid=(sample_count, source_count // sources_per_step),
        in_specs=[
            pl.BlockSpec((1, query_count, head_width), lambda s, k: (s, 0, 0)),
            pl.BlockSpec(
                (1, sources_per_step, 1, head_width, source_rows), lambda s, k: (0, k, s, 0, 0)
            ),
            pl.BlockSpec(
                (1, sources_per_step, 1, head_width, source_rows), lambda s, k: (1, k, s, 0, 0)
            ),
        ],
        out_specs=pl.BlockSpec((1, query_count, head_width), lambda s, k: (s, 0, 0)),
        out_shape=jax.ShapeDtypeStruct(queries.shape, jnp.bfloat16),
        scratch_shapes=[
            pltpu.VMEM((query_count, 1), jnp.float32),
            pltpu.VMEM((query_count, 1), jnp.float32),
            pltpu.VMEM((query_count, head_width), jnp.float32),
        ],
        compiler_params=pltpu.CompilerParams(dimension_semantics=("parallel", "arbitrary")),
    )(queries, kv_tile, kv_tile)


def normalize(rows_in, gain):
    values = rows_in.astype(jnp.float32)
    scale = lax.rsqrt(jnp.mean(values * values, axis=-1, keepdims=True) + 1e-06)
    return values * scale * gain


def one_sample(
    activations,
    conv_gain,
    conv_weight,
    attention_gain,
    query_weight,
    key_weight,
    value_weight,
    output_weight,
):
    sample_count, own_rows, full_width = activations.shape
    tap_count, local_out, _ = conv_weight.shape
    flank_rows = tap_count // 2
    gathered_in = gather_batch(activations, 1)
    seq_rows = gathered_in.shape[1]
    active = jax.nn.gelu(normalize(gathered_in, conv_gain)).astype(jnp.bfloat16)
    framed = with_halo(active, (("seq", 1),), flank_rows)
    conv_sum = jnp.zeros((sample_count, local_out, seq_rows), jnp.float32)
    for offset in range(tap_count):
        conv_sum = conv_sum + jnp.einsum(
            "std,ed->set",
            framed[:, offset : offset + seq_rows],
            conv_weight[offset],
            preferred_element_type=jnp.float32,
        )
    column_start = lax.axis_index("batch") * local_out
    own_columns = lax.dynamic_slice_in_dim(gathered_in, column_start, local_out, 2)
    residual = jnp.transpose(own_columns, (0, 2, 1)).astype(jnp.float32)
    hidden_part = (residual + conv_sum).astype(jnp.bfloat16)
    hidden_full = gather_batch(hidden_part, 1)
    hidden_float = hidden_full.astype(jnp.float32)
    norm_scale = lax.rsqrt(jnp.mean(hidden_float * hidden_float, axis=1, keepdims=True) + 1e-06)
    normed = (hidden_float * norm_scale * attention_gain[None, :, None]).astype(jnp.bfloat16)
    queries = (
        jnp.einsum("sdt,ed->ste", normed, query_weight, preferred_element_type=jnp.float32)
        * HD ** (-0.5)
    ).astype(jnp.bfloat16)
    key_rows = jnp.einsum(
        "sdt,ed->set", normed, key_weight, preferred_element_type=jnp.float32
    ).astype(jnp.bfloat16)
    value_rows = jnp.einsum(
        "sdt,ed->set", normed, value_weight, preferred_element_type=jnp.float32
    ).astype(jnp.bfloat16)
    kv_tile = lax.all_gather(jnp.stack([key_rows, value_rows]), "seq", axis=1)
    attended = flash_attention(queries, kv_tile)
    row_start = lax.axis_index("batch") * own_rows
    own_hidden = jnp.transpose(
        lax.dynamic_slice_in_dim(hidden_full, row_start, own_rows, 2), (0, 2, 1)
    ).astype(jnp.float32)
    batch_count = lax.axis_size("batch")
    partial_rows = jnp.einsum(
        "ste,ef->tsf", attended, output_weight, preferred_element_type=jnp.float32
    ).astype(jnp.bfloat16)
    partial_rows = partial_rows.reshape(batch_count, own_rows, sample_count, full_width)
    share_rows = jnp.sum(
        lax.all_to_all(partial_rows, "batch", 0, 0, tiled=False).astype(jnp.float32), axis=0
    )
    branch_rows = jnp.transpose(share_rows, (1, 0, 2))
    result = own_hidden + branch_rows
    return result.astype(jnp.bfloat16)


def shards(activations, *weights):
    pieces = [
        one_sample(activations[sample : sample + 1], *weights)
        for sample in range(activations.shape[0])
    ]
    return jnp.concatenate(pieces, axis=0)


def solution(mesh):
    placed = (
        P(None, ("seq", "batch"), None),
        P(),
        P(None, "batch", None),
        P(),
        P("batch", None),
        P("batch", None),
        P("batch", None),
        P("batch", None),
    )
    return jax.shard_map(
        shards,
        mesh=mesh,
        in_specs=placed,
        out_specs=P(None, ("seq", "batch"), None),
        check_vma=False,
    )
```

```python
import math

import jax
import jax.numpy as jnp
from jax import lax
from jax.experimental import pallas as pl
from jax.experimental.pallas import tpu as pltpu
from jax.sharding import PartitionSpec as P

HD = 192
SEQ = ("chip_x", "chip_z", "core")
BATCH = ("peer_y", "peer_x")
CHIPS = ("chip_x", "chip_z")


def with_halo(cells, sides, width):
    for axis, dim in sides:
        count = lax.axis_size(axis)
        ends = count - 1
        head = lax.slice_in_dim(cells, 0, width, axis=dim)
        tail = lax.slice_in_dim(cells, cells.shape[dim] - width, cells.shape[dim], axis=dim)
        cells = jnp.concatenate(
            [
                lax.ppermute(tail, axis, [(i, (i + 1) % count) for i in range(ends)]),
                cells,
                lax.ppermute(head, axis, [((i + 1) % count, i) for i in range(ends)]),
            ],
            axis=dim,
        )
    return cells


def gather_batch(block, axis):
    count = lax.axis_size(BATCH)
    copies = jnp.broadcast_to(block[None], (count,) + block.shape)
    arrived = jnp.moveaxis(lax.all_to_all(copies, BATCH, 0, 0, tiled=False), 0, axis)
    return arrived.reshape(block.shape[:axis] + (count * block.shape[axis],) + block.shape[axis + 1 :])


def flash_step(query_ref, key_ref, value_ref, out_ref, peak_ref, total_ref, summed_ref):
    block = pl.program_id(1)

    @pl.when(block == 0)
    def _():
        peak_ref[...] = jnp.full(peak_ref.shape, -jnp.inf, jnp.float32)
        total_ref[...] = jnp.zeros(total_ref.shape, jnp.float32)
        summed_ref[...] = jnp.zeros(summed_ref.shape, jnp.float32)

    query = query_ref[0]
    pieces = [
        jnp.dot(query, key_ref[0, part, 0], preferred_element_type=jnp.float32)
        for part in range(key_ref.shape[1])
    ]
    old_peak = peak_ref[...]
    new_peak = old_peak
    for scores in pieces:
        new_peak = jnp.maximum(new_peak, jnp.max(scores, axis=1, keepdims=True))
    rescale = jnp.exp(old_peak - new_peak)
    total = total_ref[...] * rescale
    summed = summed_ref[...] * rescale
    for part, scores in enumerate(pieces):
        weights = jnp.exp(scores - new_peak)
        total = total + jnp.sum(weights, axis=1, keepdims=True)
        summed = summed + lax.dot_general(
            weights.astype(jnp.bfloat16),
            value_ref[0, part, 0],
            (((1,), (1,)), ((), ())),
            preferred_element_type=jnp.float32,
        )
    total_ref[...] = total
    summed_ref[...] = summed
    peak_ref[...] = new_peak

    @pl.when(block == pl.num_programs(1) - 1)
    def _():
        out_ref[0] = (summed_ref[...] / total_ref[...]).astype(out_ref.dtype)


def flash_attention(queries, kv_tile, sources_per_step=2):
    sample_count, query_count, head_width = queries.shape
    _, source_count, _, _, source_rows = kv_tile.shape
    sources_per_step = math.gcd(source_count, sources_per_step)
    return pl.pallas_call(
        flash_step,
        grid=(sample_count, source_count // sources_per_step),
        in_specs=[
            pl.BlockSpec((1, query_count, head_width), lambda s, k: (s, 0, 0)),
            pl.BlockSpec(
                (1, sources_per_step, 1, head_width, source_rows), lambda s, k: (0, k, s, 0, 0)
            ),
            pl.BlockSpec(
                (1, sources_per_step, 1, head_width, source_rows), lambda s, k: (1, k, s, 0, 0)
            ),
        ],
        out_specs=pl.BlockSpec((1, query_count, head_width), lambda s, k: (s, 0, 0)),
        out_shape=jax.ShapeDtypeStruct(queries.shape, jnp.bfloat16),
        scratch_shapes=[
            pltpu.VMEM((query_count, 1), jnp.float32),
            pltpu.VMEM((query_count, 1), jnp.float32),
            pltpu.VMEM((query_count, head_width), jnp.float32),
        ],
        compiler_params=pltpu.CompilerParams(dimension_semantics=("parallel", "arbitrary")),
    )(queries, kv_tile, kv_tile)


def normalize(rows_in, gain):
    values = rows_in.astype(jnp.float32)
    scale = lax.rsqrt(jnp.mean(values * values, axis=-1, keepdims=True) + 1e-06)
    return values * scale * gain


def shards(
    activations,
    conv_gain,
    conv_weight,
    attention_gain,
    query_weight,
    key_weight,
    value_weight,
    output_weight,
):
    sample_count, own_rows, full_width = activations.shape
    tap_count, local_out, _ = conv_weight.shape
    flank_rows = tap_count // 2
    gathered_in = gather_batch(activations, 1)
    seq_rows = gathered_in.shape[1]
    active = jax.nn.gelu(normalize(gathered_in, conv_gain)).astype(jnp.bfloat16)
    framed = with_halo(active, ((SEQ, 1),), flank_rows)
    conv_sum = jnp.zeros((sample_count, local_out, seq_rows), jnp.float32)
    for offset in range(tap_count):
        conv_sum = conv_sum + jnp.einsum(
            "std,ed->set",
            framed[:, offset : offset + seq_rows],
            conv_weight[offset],
            preferred_element_type=jnp.float32,
        )
    column_start = lax.axis_index(BATCH) * local_out
    own_columns = lax.dynamic_slice_in_dim(gathered_in, column_start, local_out, 2)
    residual = jnp.transpose(own_columns, (0, 2, 1)).astype(jnp.float32)
    hidden_part = (residual + conv_sum).astype(jnp.bfloat16)
    hidden_full = gather_batch(hidden_part, 1)
    hidden_float = hidden_full.astype(jnp.float32)
    norm_scale = lax.rsqrt(jnp.mean(hidden_float * hidden_float, axis=1, keepdims=True) + 1e-06)
    normed = (hidden_float * norm_scale * attention_gain[None, :, None]).astype(jnp.bfloat16)
    queries = (
        jnp.einsum("sdt,ed->ste", normed, query_weight, preferred_element_type=jnp.float32)
        * HD ** (-0.5)
    ).astype(jnp.bfloat16)
    key_rows = jnp.einsum(
        "sdt,ed->set", normed, key_weight, preferred_element_type=jnp.float32
    ).astype(jnp.bfloat16)
    value_rows = jnp.einsum(
        "sdt,ed->set", normed, value_weight, preferred_element_type=jnp.float32
    ).astype(jnp.bfloat16)
    mine = lax.axis_index("core")
    swap = [(0, 1), (1, 0)]
    own_queries = lax.dynamic_index_in_dim(queries, mine, 0, keepdims=False)
    other_queries = lax.dynamic_index_in_dim(queries, 1 - mine, 0, keepdims=False)
    query_block = jnp.concatenate([own_queries, lax.ppermute(other_queries, "core", swap)], 0)
    kv_rows = jnp.stack([key_rows, value_rows])
    own_kv = lax.dynamic_index_in_dim(kv_rows, mine, 1, keepdims=False)
    other_kv = lax.dynamic_index_in_dim(kv_rows, 1 - mine, 1, keepdims=False)
    chip_kv = jnp.stack([own_kv, lax.ppermute(other_kv, "core", swap)], axis=1)
    kv_tile = lax.all_gather(chip_kv, CHIPS, axis=1)
    kv_tile = kv_tile.reshape((2, -1, 1) + kv_tile.shape[3:])
    attended = flash_attention(query_block[None], kv_tile)[0]
    row_start = lax.axis_index(BATCH) * own_rows
    own_hidden = jnp.transpose(
        lax.dynamic_slice_in_dim(hidden_full, row_start, own_rows, 2), (0, 2, 1)
    ).astype(jnp.float32)
    batch_count = lax.axis_size(BATCH)
    partial_rows = jnp.dot(attended, output_weight, preferred_element_type=jnp.float32)
    partial_rows = jnp.transpose(
        partial_rows.astype(jnp.bfloat16).reshape(2, batch_count, own_rows, full_width), (1, 0, 2, 3)
    )
    share_rows = jnp.sum(
        lax.all_to_all(partial_rows, BATCH, 0, 0, tiled=False).astype(jnp.float32), axis=0
    )
    from_partner = lax.ppermute(share_rows[1], "core", swap)
    branch_rows = jnp.where(
        mine == 0,
        jnp.stack([share_rows[0], from_partner]),
        jnp.stack([from_partner, share_rows[0]]),
    )
    result = own_hidden + branch_rows
    return result.astype(jnp.bfloat16)


def solution(mesh):
    fine = jax.sharding.Mesh(
        mesh.devices.reshape(2, mesh.shape["seq"] // 4, 2, mesh.shape["batch"] // 2, 2),
        SEQ + BATCH,
    )
    placed = (
        P(None, SEQ + BATCH, None),
        P(),
        P(None, BATCH, None),
        P(),
        P(BATCH, None),
        P(BATCH, None),
        P(BATCH, None),
        P(BATCH, None),
    )
    return jax.shard_map(
        shards,
        mesh=fine,
        in_specs=placed,
        out_specs=P(None, SEQ + BATCH, None),
        check_vma=False,
    )
```

```python
import math

import jax
import jax.numpy as jnp
from jax import lax
from jax.experimental import pallas as pl
from jax.experimental.pallas import tpu as pltpu
from jax.sharding import PartitionSpec as P

HD = 192


def with_halo(cells, sides, width):
    for axis, dim in sides:
        count = lax.axis_size(axis)
        ends = count - 1
        head = lax.slice_in_dim(cells, 0, width, axis=dim)
        tail = lax.slice_in_dim(cells, cells.shape[dim] - width, cells.shape[dim], axis=dim)
        cells = jnp.concatenate(
            [
                lax.ppermute(tail, axis, [(i, (i + 1) % count) for i in range(ends)]),
                cells,
                lax.ppermute(head, axis, [((i + 1) % count, i) for i in range(ends)]),
            ],
            axis=dim,
        )
    return cells


def gather_batch(block, axis):
    count = lax.axis_size("batch")
    copies = jnp.broadcast_to(block[None], (count,) + block.shape)
    arrived = jnp.moveaxis(lax.all_to_all(copies, "batch", 0, 0, tiled=False), 0, axis)
    return arrived.reshape(block.shape[:axis] + (count * block.shape[axis],) + block.shape[axis + 1 :])


def flash_step(query_ref, key_ref, value_ref, out_ref, peak_ref, total_ref, summed_ref):
    block = pl.program_id(1)

    @pl.when(block == 0)
    def _():
        peak_ref[...] = jnp.full(peak_ref.shape, -jnp.inf, jnp.float32)
        total_ref[...] = jnp.zeros(total_ref.shape, jnp.float32)
        summed_ref[...] = jnp.zeros(summed_ref.shape, jnp.float32)

    query = query_ref[0]
    pieces = [
        jnp.dot(query, key_ref[0, part, 0], preferred_element_type=jnp.float32)
        for part in range(key_ref.shape[1])
    ]
    old_peak = peak_ref[...]
    new_peak = old_peak
    for scores in pieces:
        new_peak = jnp.maximum(new_peak, jnp.max(scores, axis=1, keepdims=True))
    rescale = jnp.exp(old_peak - new_peak)
    total = total_ref[...] * rescale
    summed = summed_ref[...] * rescale
    for part, scores in enumerate(pieces):
        weights = jnp.exp(scores - new_peak)
        total = total + jnp.sum(weights, axis=1, keepdims=True)
        summed = summed + lax.dot_general(
            weights.astype(jnp.bfloat16),
            value_ref[0, part, 0],
            (((1,), (1,)), ((), ())),
            preferred_element_type=jnp.float32,
        )
    total_ref[...] = total
    summed_ref[...] = summed
    peak_ref[...] = new_peak

    @pl.when(block == pl.num_programs(1) - 1)
    def _():
        out_ref[0] = (summed_ref[...] / total_ref[...]).astype(out_ref.dtype)


def flash_attention(queries, kv_tile, sources_per_step=2):
    sample_count, query_count, head_width = queries.shape
    _, source_count, _, _, source_rows = kv_tile.shape
    sources_per_step = math.gcd(source_count, sources_per_step)
    return pl.pallas_call(
        flash_step,
        grid=(sample_count, source_count // sources_per_step),
        in_specs=[
            pl.BlockSpec((1, query_count, head_width), lambda s, k: (s, 0, 0)),
            pl.BlockSpec(
                (1, sources_per_step, 1, head_width, source_rows), lambda s, k: (0, k, s, 0, 0)
            ),
            pl.BlockSpec(
                (1, sources_per_step, 1, head_width, source_rows), lambda s, k: (1, k, s, 0, 0)
            ),
        ],
        out_specs=pl.BlockSpec((1, query_count, head_width), lambda s, k: (s, 0, 0)),
        out_shape=jax.ShapeDtypeStruct(queries.shape, jnp.bfloat16),
        scratch_shapes=[
            pltpu.VMEM((query_count, 1), jnp.float32),
            pltpu.VMEM((query_count, 1), jnp.float32),
            pltpu.VMEM((query_count, head_width), jnp.float32),
        ],
        compiler_params=pltpu.CompilerParams(dimension_semantics=("parallel", "arbitrary")),
    )(queries, kv_tile, kv_tile)


def normalize(rows_in, gain):
    values = rows_in.astype(jnp.float32)
    scale = lax.rsqrt(jnp.mean(values * values, axis=-1, keepdims=True) + 1e-06)
    return values * scale * gain


def shards(
    activations,
    conv_gain,
    conv_weight,
    attention_gain,
    query_weight,
    key_weight,
    value_weight,
    output_weight,
):
    sample_count, own_rows, full_width = activations.shape
    tap_count, local_out, _ = conv_weight.shape
    flank_rows = tap_count // 2
    full_output_weight = lax.all_gather(output_weight, "batch", axis=0, tiled=True)
    gathered_in = gather_batch(activations, 1)
    seq_rows = gathered_in.shape[1]
    active = jax.nn.gelu(normalize(gathered_in, conv_gain)).astype(jnp.bfloat16)
    framed = with_halo(active, (("seq", 1),), flank_rows)
    conv_sum = jnp.zeros((sample_count, local_out, seq_rows), jnp.float32)
    for offset in range(tap_count):
        conv_sum = conv_sum + jnp.einsum(
            "std,ed->set",
            framed[:, offset : offset + seq_rows],
            conv_weight[offset],
            preferred_element_type=jnp.float32,
        )
    column_start = lax.axis_index("batch") * local_out
    own_columns = lax.dynamic_slice_in_dim(gathered_in, column_start, local_out, 2)
    residual = jnp.transpose(own_columns, (0, 2, 1)).astype(jnp.float32)
    hidden_part = (residual + conv_sum).astype(jnp.bfloat16)
    hidden_full = gather_batch(hidden_part, 1)
    hidden_float = hidden_full.astype(jnp.float32)
    norm_scale = lax.rsqrt(jnp.mean(hidden_float * hidden_float, axis=1, keepdims=True) + 1e-06)
    normed = (hidden_float * norm_scale * attention_gain[None, :, None]).astype(jnp.bfloat16)
    queries = (
        jnp.einsum("sdt,ed->ste", normed, query_weight, preferred_element_type=jnp.float32)
        * HD ** (-0.5)
    ).astype(jnp.bfloat16)
    key_rows = jnp.einsum(
        "sdt,ed->set", normed, key_weight, preferred_element_type=jnp.float32
    ).astype(jnp.bfloat16)
    value_rows = jnp.einsum(
        "sdt,ed->set", normed, value_weight, preferred_element_type=jnp.float32
    ).astype(jnp.bfloat16)
    kv_rows, full_output_weight = lax.optimization_barrier(
        (jnp.stack([key_rows, value_rows]), full_output_weight)
    )
    kv_tile = lax.all_gather(kv_rows, "seq", axis=1)
    attended = flash_attention(queries, kv_tile)
    row_start = lax.axis_index("batch") * own_rows
    own_hidden = jnp.transpose(
        lax.dynamic_slice_in_dim(hidden_full, row_start, own_rows, 2), (0, 2, 1)
    ).astype(jnp.float32)
    batch_count = lax.axis_size("batch")
    head_width = attended.shape[2]
    outgoing = jnp.transpose(
        attended.reshape(sample_count, batch_count, own_rows, head_width), (1, 0, 2, 3)
    )
    arrived = lax.all_to_all(outgoing, "batch", 0, 0, tiled=False)
    heads_side_by_side = jnp.transpose(arrived, (1, 2, 0, 3)).reshape(
        sample_count, own_rows, batch_count * head_width
    )
    branch_rows = jnp.einsum(
        "std,df->stf", heads_side_by_side, full_output_weight, preferred_element_type=jnp.float32
    )
    result = own_hidden + branch_rows
    return result.astype(jnp.bfloat16)


def solution(mesh):
    placed = (
        P(None, ("seq", "batch"), None),
        P(),
        P(None, "batch", None),
        P(),
        P("batch", None),
        P("batch", None),
        P("batch", None),
        P("batch", None),
    )
    return jax.shard_map(
        shards,
        mesh=mesh,
        in_specs=placed,
        out_specs=P(None, ("seq", "batch"), None),
        check_vma=False,
    )
```

```python
import math

import jax
import jax.numpy as jnp
from jax import lax
from jax.experimental import pallas as pl
from jax.experimental.pallas import tpu as pltpu
from jax.sharding import PartitionSpec as P

HD = 192


def with_halo(cells, sides, width):
    for axis, dim in sides:
        count = lax.axis_size(axis)
        ends = count - 1
        head = lax.slice_in_dim(cells, 0, width, axis=dim)
        tail = lax.slice_in_dim(cells, cells.shape[dim] - width, cells.shape[dim], axis=dim)
        cells = jnp.concatenate(
            [
                lax.ppermute(tail, axis, [(i, (i + 1) % count) for i in range(ends)]),
                cells,
                lax.ppermute(head, axis, [((i + 1) % count, i) for i in range(ends)]),
            ],
            axis=dim,
        )
    return cells


def gather_batch(block, axis):
    count = lax.axis_size("batch")
    copies = jnp.broadcast_to(block[None], (count,) + block.shape)
    arrived = jnp.moveaxis(lax.all_to_all(copies, "batch", 0, 0, tiled=False), 0, axis)
    return arrived.reshape(block.shape[:axis] + (count * block.shape[axis],) + block.shape[axis + 1 :])


def flash_step(query_ref, key_ref, value_ref, out_ref, peak_ref, total_ref, summed_ref):
    block = pl.program_id(1)

    @pl.when(block == 0)
    def _():
        peak_ref[...] = jnp.full(peak_ref.shape, -jnp.inf, jnp.float32)
        total_ref[...] = jnp.zeros(total_ref.shape, jnp.float32)
        summed_ref[...] = jnp.zeros(summed_ref.shape, jnp.float32)

    query = query_ref[0]
    pieces = [
        jnp.dot(query, key_ref[0, part, 0], preferred_element_type=jnp.float32)
        for part in range(key_ref.shape[1])
    ]
    old_peak = peak_ref[...]
    new_peak = old_peak
    for scores in pieces:
        new_peak = jnp.maximum(new_peak, jnp.max(scores, axis=1, keepdims=True))
    rescale = jnp.exp(old_peak - new_peak)
    total = total_ref[...] * rescale
    summed = summed_ref[...] * rescale
    for part, scores in enumerate(pieces):
        weights = jnp.exp(scores - new_peak)
        total = total + jnp.sum(weights, axis=1, keepdims=True)
        summed = summed + lax.dot_general(
            weights.astype(jnp.bfloat16),
            value_ref[0, part, 0],
            (((1,), (1,)), ((), ())),
            preferred_element_type=jnp.float32,
        )
    total_ref[...] = total
    summed_ref[...] = summed
    peak_ref[...] = new_peak

    @pl.when(block == pl.num_programs(1) - 1)
    def _():
        out_ref[0] = (summed_ref[...] / total_ref[...]).astype(out_ref.dtype)


def flash_attention(queries, kv_tile, sample, sources_per_step=2):
    _, query_count, head_width = queries.shape
    _, source_count, _, _, source_rows = kv_tile.shape
    sources_per_step = math.gcd(source_count, sources_per_step)
    return pl.pallas_call(
        flash_step,
        grid=(1, source_count // sources_per_step),
        in_specs=[
            pl.BlockSpec((1, query_count, head_width), lambda s, k: (sample, 0, 0)),
            pl.BlockSpec(
                (1, sources_per_step, 1, head_width, source_rows),
                lambda s, k: (0, k, sample, 0, 0),
            ),
            pl.BlockSpec(
                (1, sources_per_step, 1, head_width, source_rows),
                lambda s, k: (1, k, sample, 0, 0),
            ),
        ],
        out_specs=pl.BlockSpec((1, query_count, head_width), lambda s, k: (0, 0, 0)),
        out_shape=jax.ShapeDtypeStruct((1, query_count, head_width), jnp.bfloat16),
        scratch_shapes=[
            pltpu.VMEM((query_count, 1), jnp.float32),
            pltpu.VMEM((query_count, 1), jnp.float32),
            pltpu.VMEM((query_count, head_width), jnp.float32),
        ],
        compiler_params=pltpu.CompilerParams(dimension_semantics=("parallel", "arbitrary")),
    )(queries, kv_tile, kv_tile)


def normalize(rows_in, gain):
    values = rows_in.astype(jnp.float32)
    scale = lax.rsqrt(jnp.mean(values * values, axis=-1, keepdims=True) + 1e-06)
    return values * scale * gain


def shards(
    activations,
    conv_gain,
    conv_weight,
    attention_gain,
    query_weight,
    key_weight,
    value_weight,
    output_weight,
):
    sample_count, own_rows, full_width = activations.shape
    tap_count, local_out, _ = conv_weight.shape
    flank_rows = tap_count // 2
    full_output_weight = lax.all_gather(output_weight, "batch", axis=0, tiled=True)
    gathered_in = gather_batch(activations, 1)
    seq_rows = gathered_in.shape[1]
    active = jax.nn.gelu(normalize(gathered_in, conv_gain)).astype(jnp.bfloat16)
    framed = with_halo(active, (("seq", 1),), flank_rows)
    conv_sum = jnp.zeros((sample_count, local_out, seq_rows), jnp.float32)
    for offset in range(tap_count):
        conv_sum = conv_sum + jnp.einsum(
            "std,ed->set",
            framed[:, offset : offset + seq_rows],
            conv_weight[offset],
            preferred_element_type=jnp.float32,
        )
    column_start = lax.axis_index("batch") * local_out
    own_columns = lax.dynamic_slice_in_dim(gathered_in, column_start, local_out, 2)
    residual = jnp.transpose(own_columns, (0, 2, 1)).astype(jnp.float32)
    hidden_part = (residual + conv_sum).astype(jnp.bfloat16)
    hidden_full = gather_batch(hidden_part, 1)
    hidden_float = hidden_full.astype(jnp.float32)
    norm_scale = lax.rsqrt(jnp.mean(hidden_float * hidden_float, axis=1, keepdims=True) + 1e-06)
    normed = (hidden_float * norm_scale * attention_gain[None, :, None]).astype(jnp.bfloat16)
    queries = (
        jnp.einsum("sdt,ed->ste", normed, query_weight, preferred_element_type=jnp.float32)
        * HD ** (-0.5)
    ).astype(jnp.bfloat16)
    key_rows = jnp.einsum(
        "sdt,ed->set", normed, key_weight, preferred_element_type=jnp.float32
    ).astype(jnp.bfloat16)
    value_rows = jnp.einsum(
        "sdt,ed->set", normed, value_weight, preferred_element_type=jnp.float32
    ).astype(jnp.bfloat16)
    kv_rows, full_output_weight = lax.optimization_barrier(
        (jnp.stack([key_rows, value_rows]), full_output_weight)
    )
    kv_tile = lax.all_gather(kv_rows, "seq", axis=1)
    row_start = lax.axis_index("batch") * own_rows
    own_hidden = jnp.transpose(
        lax.dynamic_slice_in_dim(hidden_full, row_start, own_rows, 2), (0, 2, 1)
    ).astype(jnp.float32)
    batch_count = lax.axis_size("batch")
    pieces = []
    for sample in range(sample_count):
        attended = flash_attention(queries, kv_tile, sample)[0]
        head_width = attended.shape[1]
        arrived = lax.all_to_all(
            attended.reshape(batch_count, own_rows, head_width), "batch", 0, 0, tiled=False
        )
        heads_side_by_side = jnp.transpose(arrived, (1, 0, 2)).reshape(
            own_rows, batch_count * head_width
        )
        branch_rows = jnp.dot(
            heads_side_by_side, full_output_weight, preferred_element_type=jnp.float32
        )
        pieces.append((own_hidden[sample] + branch_rows).astype(jnp.bfloat16))
    return jnp.stack(pieces)


def solution(mesh):
    placed = (
        P(None, ("seq", "batch"), None),
        P(),
        P(None, "batch", None),
        P(),
        P("batch", None),
        P("batch", None),
        P("batch", None),
        P("batch", None),
    )
    return jax.shard_map(
        shards,
        mesh=mesh,
        in_specs=placed,
        out_specs=P(None, ("seq", "batch"), None),
        check_vma=False,
    )
```

```python
import math

import jax
import jax.numpy as jnp
from jax import lax
from jax.experimental import pallas as pl
from jax.experimental.pallas import tpu as pltpu
from jax.sharding import PartitionSpec as P

HD = 192


def with_halo(cells, sides, width):
    for axis, dim in sides:
        count = lax.axis_size(axis)
        ends = count - 1
        head = lax.slice_in_dim(cells, 0, width, axis=dim)
        tail = lax.slice_in_dim(cells, cells.shape[dim] - width, cells.shape[dim], axis=dim)
        cells = jnp.concatenate(
            [
                lax.ppermute(tail, axis, [(i, (i + 1) % count) for i in range(ends)]),
                cells,
                lax.ppermute(head, axis, [((i + 1) % count, i) for i in range(ends)]),
            ],
            axis=dim,
        )
    return cells


def gather_batch(block, axis):
    count = lax.axis_size("batch")
    spread = block.shape[:axis] + (count,) + block.shape[axis:]
    copies = jnp.broadcast_to(jnp.expand_dims(block, axis), spread)
    arrived = lax.all_to_all(copies, "batch", axis, axis, tiled=False)
    return arrived.reshape(block.shape[:axis] + (count * block.shape[axis],) + block.shape[axis + 1 :])


def flash_step(query_ref, key_ref, value_ref, out_ref, peak_ref, total_ref, summed_ref):
    block = pl.program_id(1)

    @pl.when(block == 0)
    def _():
        peak_ref[...] = jnp.full(peak_ref.shape, -jnp.inf, jnp.float32)
        total_ref[...] = jnp.zeros(total_ref.shape, jnp.float32)
        summed_ref[...] = jnp.zeros(summed_ref.shape, jnp.float32)

    query = query_ref[0]
    pieces = [
        jnp.dot(query, key_ref[0, part, 0], preferred_element_type=jnp.float32)
        for part in range(key_ref.shape[1])
    ]
    old_peak = peak_ref[...]
    new_peak = old_peak
    for scores in pieces:
        new_peak = jnp.maximum(new_peak, jnp.max(scores, axis=1, keepdims=True))
    rescale = jnp.exp(old_peak - new_peak)
    total = total_ref[...] * rescale
    summed = summed_ref[...] * rescale
    for part, scores in enumerate(pieces):
        weights = jnp.exp(scores - new_peak)
        total = total + jnp.sum(weights, axis=1, keepdims=True)
        summed = summed + lax.dot_general(
            weights.astype(jnp.bfloat16),
            value_ref[0, part, 0],
            (((1,), (1,)), ((), ())),
            preferred_element_type=jnp.float32,
        )
    total_ref[...] = total
    summed_ref[...] = summed
    peak_ref[...] = new_peak

    @pl.when(block == pl.num_programs(1) - 1)
    def _():
        out_ref[0] = (summed_ref[...] / total_ref[...]).astype(out_ref.dtype)


def flash_attention(queries, kv_tile, sources_per_step=2):
    sample_count, query_count, head_width = queries.shape
    _, source_count, _, _, source_rows = kv_tile.shape
    sources_per_step = math.gcd(source_count, sources_per_step)
    return pl.pallas_call(
        flash_step,
        grid=(sample_count, source_count // sources_per_step),
        in_specs=[
            pl.BlockSpec((1, query_count, head_width), lambda s, k: (s, 0, 0)),
            pl.BlockSpec(
                (1, sources_per_step, 1, head_width, source_rows), lambda s, k: (0, k, s, 0, 0)
            ),
            pl.BlockSpec(
                (1, sources_per_step, 1, head_width, source_rows), lambda s, k: (1, k, s, 0, 0)
            ),
        ],
        out_specs=pl.BlockSpec((1, query_count, head_width), lambda s, k: (s, 0, 0)),
        out_shape=jax.ShapeDtypeStruct(queries.shape, jnp.bfloat16),
        scratch_shapes=[
            pltpu.VMEM((query_count, 1), jnp.float32),
            pltpu.VMEM((query_count, 1), jnp.float32),
            pltpu.VMEM((query_count, head_width), jnp.float32),
        ],
        compiler_params=pltpu.CompilerParams(dimension_semantics=("parallel", "arbitrary")),
    )(queries, kv_tile, kv_tile)


def normalize(rows_in, gain):
    values = rows_in.astype(jnp.float32)
    scale = lax.rsqrt(jnp.mean(values * values, axis=-1, keepdims=True) + 1e-06)
    return values * scale * gain


def shards(
    activations,
    conv_gain,
    conv_weight,
    attention_gain,
    query_weight,
    key_weight,
    value_weight,
    output_weight,
):
    sample_count, own_rows, full_width = activations.shape
    tap_count, local_out, _ = conv_weight.shape
    flank_rows = tap_count // 2
    full_output_weight = lax.all_gather(output_weight, "batch", axis=0, tiled=True)
    gathered_in = gather_batch(activations, 1)
    seq_rows = gathered_in.shape[1]
    active = lax.optimization_barrier(
        jax.nn.gelu(normalize(gathered_in, conv_gain)).astype(jnp.bfloat16)
    )
    framed = with_halo(active, (("seq", 1),), flank_rows)
    conv_sum = jnp.zeros((sample_count, local_out, seq_rows), jnp.float32)
    for offset in range(tap_count):
        conv_sum = conv_sum + jnp.einsum(
            "std,ed->set",
            framed[:, offset : offset + seq_rows],
            conv_weight[offset],
            preferred_element_type=jnp.float32,
        )
    column_start = lax.axis_index("batch") * local_out
    own_columns = lax.dynamic_slice_in_dim(gathered_in, column_start, local_out, 2)
    residual = jnp.transpose(own_columns, (0, 2, 1)).astype(jnp.float32)
    hidden_part = (residual + conv_sum).astype(jnp.bfloat16)
    hidden_full = gather_batch(hidden_part, 1)
    hidden_float = hidden_full.astype(jnp.float32)
    norm_scale = lax.rsqrt(jnp.mean(hidden_float * hidden_float, axis=1, keepdims=True) + 1e-06)
    normed = (hidden_float * norm_scale * attention_gain[None, :, None]).astype(jnp.bfloat16)
    queries = (
        jnp.einsum("sdt,ed->ste", normed, query_weight, preferred_element_type=jnp.float32)
        * HD ** (-0.5)
    ).astype(jnp.bfloat16)
    key_rows = jnp.einsum(
        "sdt,ed->set", normed, key_weight, preferred_element_type=jnp.float32
    ).astype(jnp.bfloat16)
    value_rows = jnp.einsum(
        "sdt,ed->set", normed, value_weight, preferred_element_type=jnp.float32
    ).astype(jnp.bfloat16)
    kv_rows, full_output_weight = lax.optimization_barrier(
        (jnp.stack([key_rows, value_rows]), full_output_weight)
    )
    kv_tile = lax.all_gather(kv_rows, "seq", axis=1)
    attended = flash_attention(queries, kv_tile)
    row_start = lax.axis_index("batch") * own_rows
    own_hidden = jnp.transpose(
        lax.dynamic_slice_in_dim(hidden_full, row_start, own_rows, 2), (0, 2, 1)
    ).astype(jnp.float32)
    batch_count = lax.axis_size("batch")
    head_width = attended.shape[2]
    outgoing = jnp.transpose(
        attended.reshape(sample_count, batch_count, own_rows, head_width), (1, 0, 2, 3)
    )
    arrived = lax.all_to_all(outgoing, "batch", 0, 0, tiled=False)
    heads_side_by_side = jnp.transpose(arrived, (1, 2, 0, 3)).reshape(
        sample_count, own_rows, batch_count * head_width
    )
    branch_rows = jnp.einsum(
        "std,df->stf", heads_side_by_side, full_output_weight, preferred_element_type=jnp.float32
    )
    result = own_hidden + branch_rows
    return result.astype(jnp.bfloat16)


def solution(mesh):
    placed = (
        P(None, ("seq", "batch"), None),
        P(),
        P(None, "batch", None),
        P(),
        P("batch", None),
        P("batch", None),
        P("batch", None),
        P("batch", None),
    )
    return jax.shard_map(
        shards,
        mesh=mesh,
        in_specs=placed,
        out_specs=P(None, ("seq", "batch"), None),
        check_vma=False,
    )
```

```python
import math

import jax
import jax.numpy as jnp
from jax import lax
from jax.experimental import pallas as pl
from jax.experimental.pallas import tpu as pltpu
from jax.sharding import PartitionSpec as P

HD = 192
SEQ = ("chip_x", "chip_z", "core")
BATCH = ("peer_y", "peer_x")
CHIPS = ("chip_x", "chip_z")


def with_halo(cells, sides, width):
    for axis, dim in sides:
        count = lax.axis_size(axis)
        ends = count - 1
        head = lax.slice_in_dim(cells, 0, width, axis=dim)
        tail = lax.slice_in_dim(cells, cells.shape[dim] - width, cells.shape[dim], axis=dim)
        cells = jnp.concatenate(
            [
                lax.ppermute(tail, axis, [(i, (i + 1) % count) for i in range(ends)]),
                cells,
                lax.ppermute(head, axis, [((i + 1) % count, i) for i in range(ends)]),
            ],
            axis=dim,
        )
    return cells


def gather_batch(block, axis):
    count = lax.axis_size(BATCH)
    spread = block.shape[:axis] + (count,) + block.shape[axis:]
    copies = jnp.broadcast_to(jnp.expand_dims(block, axis), spread)
    arrived = lax.all_to_all(copies, BATCH, axis, axis, tiled=False)
    return arrived.reshape(block.shape[:axis] + (count * block.shape[axis],) + block.shape[axis + 1 :])


def flash_step(query_ref, key_ref, value_ref, out_ref, peak_ref, total_ref, summed_ref):
    block = pl.program_id(1)

    @pl.when(block == 0)
    def _():
        peak_ref[...] = jnp.full(peak_ref.shape, -jnp.inf, jnp.float32)
        total_ref[...] = jnp.zeros(total_ref.shape, jnp.float32)
        summed_ref[...] = jnp.zeros(summed_ref.shape, jnp.float32)

    query = query_ref[0]
    pieces = [
        jnp.dot(query, key_ref[0, part, 0], preferred_element_type=jnp.float32)
        for part in range(key_ref.shape[1])
    ]
    old_peak = peak_ref[...]
    new_peak = old_peak
    for scores in pieces:
        new_peak = jnp.maximum(new_peak, jnp.max(scores, axis=1, keepdims=True))
    rescale = jnp.exp(old_peak - new_peak)
    total = total_ref[...] * rescale
    summed = summed_ref[...] * rescale
    for part, scores in enumerate(pieces):
        weights = jnp.exp(scores - new_peak)
        total = total + jnp.sum(weights, axis=1, keepdims=True)
        summed = summed + lax.dot_general(
            weights.astype(jnp.bfloat16),
            value_ref[0, part, 0],
            (((1,), (1,)), ((), ())),
            preferred_element_type=jnp.float32,
        )
    total_ref[...] = total
    summed_ref[...] = summed
    peak_ref[...] = new_peak

    @pl.when(block == pl.num_programs(1) - 1)
    def _():
        out_ref[0] = (summed_ref[...] / total_ref[...]).astype(out_ref.dtype)


def flash_attention(queries, kv_tile, sample, sources_per_step=2):
    _, query_count, head_width = queries.shape
    _, source_count, _, _, source_rows = kv_tile.shape
    sources_per_step = math.gcd(source_count, sources_per_step)
    return pl.pallas_call(
        flash_step,
        grid=(1, source_count // sources_per_step),
        in_specs=[
            pl.BlockSpec((1, query_count, head_width), lambda s, k: (sample, 0, 0)),
            pl.BlockSpec(
                (1, sources_per_step, 1, head_width, source_rows), lambda s, k: (0, k, 0, 0, 0)
            ),
            pl.BlockSpec(
                (1, sources_per_step, 1, head_width, source_rows), lambda s, k: (1, k, 0, 0, 0)
            ),
        ],
        out_specs=pl.BlockSpec((1, query_count, head_width), lambda s, k: (0, 0, 0)),
        out_shape=jax.ShapeDtypeStruct((1, query_count, head_width), jnp.bfloat16),
        scratch_shapes=[
            pltpu.VMEM((query_count, 1), jnp.float32),
            pltpu.VMEM((query_count, 1), jnp.float32),
            pltpu.VMEM((query_count, head_width), jnp.float32),
        ],
        compiler_params=pltpu.CompilerParams(dimension_semantics=("parallel", "arbitrary")),
    )(queries, kv_tile, kv_tile)


def normalize(rows_in, gain):
    values = rows_in.astype(jnp.float32)
    scale = lax.rsqrt(jnp.mean(values * values, axis=-1, keepdims=True) + 1e-06)
    return values * scale * gain


def shards(
    activations,
    conv_gain,
    conv_weight,
    attention_gain,
    query_weight,
    key_weight,
    value_weight,
    output_weight,
):
    sample_count, own_rows, full_width = activations.shape
    tap_count, local_out, _ = conv_weight.shape
    flank_rows = tap_count // 2
    full_output_weight = lax.all_gather(output_weight, BATCH, axis=0, tiled=True)
    gathered_in = gather_batch(activations, 1)
    seq_rows = gathered_in.shape[1]
    active = lax.optimization_barrier(
        jax.nn.gelu(normalize(gathered_in, conv_gain)).astype(jnp.bfloat16)
    )
    framed = with_halo(active, ((SEQ, 1),), flank_rows)
    conv_sum = jnp.zeros((sample_count, local_out, seq_rows), jnp.float32)
    for offset in range(tap_count):
        conv_sum = conv_sum + jnp.einsum(
            "std,ed->set",
            framed[:, offset : offset + seq_rows],
            conv_weight[offset],
            preferred_element_type=jnp.float32,
        )
    column_start = lax.axis_index(BATCH) * local_out
    own_columns = lax.dynamic_slice_in_dim(gathered_in, column_start, local_out, 2)
    residual = jnp.transpose(own_columns, (0, 2, 1)).astype(jnp.float32)
    hidden_part = (residual + conv_sum).astype(jnp.bfloat16)
    hidden_full = gather_batch(hidden_part, 1)
    hidden_float = hidden_full.astype(jnp.float32)
    norm_scale = lax.rsqrt(jnp.mean(hidden_float * hidden_float, axis=1, keepdims=True) + 1e-06)
    normed = (hidden_float * norm_scale * attention_gain[None, :, None]).astype(jnp.bfloat16)
    queries = (
        jnp.einsum("sdt,ed->ste", normed, query_weight, preferred_element_type=jnp.float32)
        * HD ** (-0.5)
    ).astype(jnp.bfloat16)
    key_rows = jnp.einsum(
        "sdt,ed->set", normed, key_weight, preferred_element_type=jnp.float32
    ).astype(jnp.bfloat16)
    value_rows = jnp.einsum(
        "sdt,ed->set", normed, value_weight, preferred_element_type=jnp.float32
    ).astype(jnp.bfloat16)
    kv_rows, full_output_weight = lax.optimization_barrier(
        (jnp.stack([key_rows, value_rows]), full_output_weight)
    )
    first_tile = lax.all_gather(kv_rows[:, :1], SEQ, axis=1)
    chip_count = lax.axis_size(CHIPS)
    second_rows = kv_rows[:, 1:]
    copies = jnp.broadcast_to(second_rows, (2, chip_count) + second_rows.shape[2:])
    same_core = lax.all_to_all(copies, CHIPS, 1, 1, tiled=False)
    other_core = lax.ppermute(same_core, "core", [(0, 1), (1, 0)])
    second_tile = jnp.concatenate([same_core, other_core], axis=1)[:, :, None]
    attended = jnp.concatenate(
        [flash_attention(queries, first_tile, 0), flash_attention(queries, second_tile, 1)]
    )
    row_start = lax.axis_index(BATCH) * own_rows
    own_hidden = jnp.transpose(
        lax.dynamic_slice_in_dim(hidden_full, row_start, own_rows, 2), (0, 2, 1)
    ).astype(jnp.float32)
    batch_count = lax.axis_size(BATCH)
    head_width = attended.shape[2]
    outgoing = jnp.transpose(
        attended.reshape(sample_count, batch_count, own_rows, head_width), (1, 0, 2, 3)
    )
    arrived = lax.all_to_all(outgoing, BATCH, 0, 0, tiled=False)
    heads_side_by_side = jnp.transpose(arrived, (1, 2, 0, 3)).reshape(
        sample_count, own_rows, batch_count * head_width
    )
    branch_rows = jnp.einsum(
        "std,df->stf", heads_side_by_side, full_output_weight, preferred_element_type=jnp.float32
    )
    result = own_hidden + branch_rows
    return result.astype(jnp.bfloat16)


def solution(mesh):
    fine = jax.sharding.Mesh(
        mesh.devices.reshape(2, mesh.shape["seq"] // 4, 2, mesh.shape["batch"] // 2, 2),
        SEQ + BATCH,
    )
    placed = (
        P(None, SEQ + BATCH, None),
        P(),
        P(None, BATCH, None),
        P(),
        P(BATCH, None),
        P(BATCH, None),
        P(BATCH, None),
        P(BATCH, None),
    )
    return jax.shard_map(
        shards,
        mesh=fine,
        in_specs=placed,
        out_specs=P(None, SEQ + BATCH, None),
        check_vma=False,
    )
```

```python
import math

import jax
import jax.numpy as jnp
from jax import lax
from jax.experimental import pallas as pl
from jax.experimental.pallas import tpu as pltpu
from jax.sharding import PartitionSpec as P

HD = 192


def with_halo(cells, sides, width):
    for axis, dim in sides:
        count = lax.axis_size(axis)
        ends = count - 1
        head = lax.slice_in_dim(cells, 0, width, axis=dim)
        tail = lax.slice_in_dim(cells, cells.shape[dim] - width, cells.shape[dim], axis=dim)
        cells = jnp.concatenate(
            [
                lax.ppermute(tail, axis, [(i, (i + 1) % count) for i in range(ends)]),
                cells,
                lax.ppermute(head, axis, [((i + 1) % count, i) for i in range(ends)]),
            ],
            axis=dim,
        )
    return cells


def gather_batch(block, axis):
    count = lax.axis_size("batch")
    spread = block.shape[:axis] + (count,) + block.shape[axis:]
    copies = jnp.broadcast_to(jnp.expand_dims(block, axis), spread)
    arrived = lax.all_to_all(copies, "batch", axis, axis, tiled=False)
    return arrived.reshape(block.shape[:axis] + (count * block.shape[axis],) + block.shape[axis + 1 :])


def flash_step(query_ref, key_ref, value_ref, out_ref, peak_ref, total_ref, summed_ref):
    block = pl.program_id(1)

    @pl.when(block == 0)
    def _():
        peak_ref[...] = jnp.full(peak_ref.shape, -jnp.inf, jnp.float32)
        total_ref[...] = jnp.zeros(total_ref.shape, jnp.float32)
        summed_ref[...] = jnp.zeros(summed_ref.shape, jnp.float32)

    query = query_ref[0]
    pieces = [
        jnp.dot(query, key_ref[0, part, 0], preferred_element_type=jnp.float32)
        for part in range(key_ref.shape[1])
    ]
    old_peak = peak_ref[...]
    new_peak = old_peak
    for scores in pieces:
        new_peak = jnp.maximum(new_peak, jnp.max(scores, axis=1, keepdims=True))
    rescale = jnp.exp(old_peak - new_peak)
    total = total_ref[...] * rescale
    summed = summed_ref[...] * rescale
    for part, scores in enumerate(pieces):
        weights = jnp.exp(scores - new_peak)
        total = total + jnp.sum(weights, axis=1, keepdims=True)
        summed = summed + lax.dot_general(
            weights.astype(jnp.bfloat16),
            value_ref[0, part, 0],
            (((1,), (1,)), ((), ())),
            preferred_element_type=jnp.float32,
        )
    total_ref[...] = total
    summed_ref[...] = summed
    peak_ref[...] = new_peak

    @pl.when(block == pl.num_programs(1) - 1)
    def _():
        out_ref[0] = (summed_ref[...] / total_ref[...]).astype(out_ref.dtype)


def flash_attention(queries, kv_tile, sources_per_step=4):
    sample_count, query_count, head_width = queries.shape
    _, source_count, _, _, source_rows = kv_tile.shape
    sources_per_step = math.gcd(source_count, sources_per_step)
    return pl.pallas_call(
        flash_step,
        grid=(sample_count, source_count // sources_per_step),
        in_specs=[
            pl.BlockSpec((1, query_count, head_width), lambda s, k: (s, 0, 0)),
            pl.BlockSpec(
                (1, sources_per_step, 1, head_width, source_rows), lambda s, k: (0, k, s, 0, 0)
            ),
            pl.BlockSpec(
                (1, sources_per_step, 1, head_width, source_rows), lambda s, k: (1, k, s, 0, 0)
            ),
        ],
        out_specs=pl.BlockSpec((1, query_count, head_width), lambda s, k: (s, 0, 0)),
        out_shape=jax.ShapeDtypeStruct(queries.shape, jnp.bfloat16),
        scratch_shapes=[
            pltpu.VMEM((query_count, 1), jnp.float32),
            pltpu.VMEM((query_count, 1), jnp.float32),
            pltpu.VMEM((query_count, head_width), jnp.float32),
        ],
        compiler_params=pltpu.CompilerParams(dimension_semantics=("parallel", "arbitrary")),
    )(queries, kv_tile, kv_tile)


def normalize(rows_in, gain):
    values = rows_in.astype(jnp.float32)
    scale = lax.rsqrt(jnp.mean(values * values, axis=-1, keepdims=True) + 1e-06)
    return values * scale * gain


def shards(
    activations,
    conv_gain,
    conv_weight,
    attention_gain,
    query_weight,
    key_weight,
    value_weight,
    output_weight,
):
    sample_count, own_rows, full_width = activations.shape
    tap_count, local_out, _ = conv_weight.shape
    flank_rows = tap_count // 2
    full_output_weight = lax.all_gather(output_weight, "batch", axis=0, tiled=True)
    gathered_in = gather_batch(activations, 1)
    seq_rows = gathered_in.shape[1]
    active = lax.optimization_barrier(
        jax.nn.gelu(normalize(gathered_in, conv_gain)).astype(jnp.bfloat16)
    )
    framed = with_halo(active, (("seq", 1),), flank_rows)
    conv_sum = jnp.zeros((sample_count, local_out, seq_rows), jnp.float32)
    for offset in range(tap_count):
        conv_sum = conv_sum + jnp.einsum(
            "std,ed->set",
            framed[:, offset : offset + seq_rows],
            conv_weight[offset],
            preferred_element_type=jnp.float32,
        )
    column_start = lax.axis_index("batch") * local_out
    own_columns = lax.dynamic_slice_in_dim(gathered_in, column_start, local_out, 2)
    residual = jnp.transpose(own_columns, (0, 2, 1)).astype(jnp.float32)
    hidden_part = (residual + conv_sum).astype(jnp.bfloat16)
    hidden_full = gather_batch(hidden_part, 1)
    hidden_float = hidden_full.astype(jnp.float32)
    norm_scale = lax.rsqrt(jnp.mean(hidden_float * hidden_float, axis=1, keepdims=True) + 1e-06)
    normed = (hidden_float * norm_scale * attention_gain[None, :, None]).astype(jnp.bfloat16)
    queries = (
        jnp.einsum("sdt,ed->ste", normed, query_weight, preferred_element_type=jnp.float32)
        * HD ** (-0.5)
    ).astype(jnp.bfloat16)
    key_rows = jnp.einsum(
        "sdt,ed->set", normed, key_weight, preferred_element_type=jnp.float32
    ).astype(jnp.bfloat16)
    value_rows = jnp.einsum(
        "sdt,ed->set", normed, value_weight, preferred_element_type=jnp.float32
    ).astype(jnp.bfloat16)
    kv_rows, full_output_weight = lax.optimization_barrier(
        (jnp.stack([key_rows, value_rows]), full_output_weight)
    )
    kv_tile = lax.all_gather(kv_rows, "seq", axis=1)
    attended = flash_attention(queries, kv_tile)
    row_start = lax.axis_index("batch") * own_rows
    own_hidden = jnp.transpose(
        lax.dynamic_slice_in_dim(hidden_full, row_start, own_rows, 2), (0, 2, 1)
    ).astype(jnp.float32)
    batch_count = lax.axis_size("batch")
    head_width = attended.shape[2]
    outgoing = jnp.transpose(
        attended.reshape(sample_count, batch_count, own_rows, head_width), (1, 0, 2, 3)
    )
    arrived = lax.all_to_all(outgoing, "batch", 0, 0, tiled=False)
    heads_side_by_side = jnp.transpose(arrived, (1, 2, 0, 3)).reshape(
        sample_count, own_rows, batch_count * head_width
    )
    branch_rows = jnp.einsum(
        "std,df->stf", heads_side_by_side, full_output_weight, preferred_element_type=jnp.float32
    )
    result = own_hidden + branch_rows
    return result.astype(jnp.bfloat16)


def solution(mesh):
    placed = (
        P(None, ("seq", "batch"), None),
        P(),
        P(None, "batch", None),
        P(),
        P("batch", None),
        P("batch", None),
        P("batch", None),
        P("batch", None),
    )
    return jax.shard_map(
        shards,
        mesh=mesh,
        in_specs=placed,
        out_specs=P(None, ("seq", "batch"), None),
        check_vma=False,
    )
```

```python
import math

import jax
import jax.numpy as jnp
from jax import lax
from jax.experimental import pallas as pl
from jax.experimental.pallas import tpu as pltpu
from jax.sharding import PartitionSpec as P

HD = 192
SEQ = ("chip_x", "chip_z", "core")
BATCH = ("peer_y", "peer_x")


def with_halo(cells, sides, width):
    for axis, dim in sides:
        count = lax.axis_size(axis)
        ends = count - 1
        head = lax.slice_in_dim(cells, 0, width, axis=dim)
        tail = lax.slice_in_dim(cells, cells.shape[dim] - width, cells.shape[dim], axis=dim)
        cells = jnp.concatenate(
            [
                lax.ppermute(tail, axis, [(i, (i + 1) % count) for i in range(ends)]),
                cells,
                lax.ppermute(head, axis, [((i + 1) % count, i) for i in range(ends)]),
            ],
            axis=dim,
        )
    return cells


def gather_batch(block, axis):
    count = lax.axis_size(BATCH)
    spread = block.shape[:axis] + (count,) + block.shape[axis:]
    copies = jnp.broadcast_to(jnp.expand_dims(block, axis), spread)
    arrived = lax.all_to_all(copies, BATCH, axis, axis, tiled=False)
    return arrived.reshape(block.shape[:axis] + (count * block.shape[axis],) + block.shape[axis + 1 :])


def flash_step(query_ref, key_ref, value_ref, out_ref, peak_ref, total_ref, summed_ref):
    block = pl.program_id(1)

    @pl.when(block == 0)
    def _():
        peak_ref[...] = jnp.full(peak_ref.shape, -jnp.inf, jnp.float32)
        total_ref[...] = jnp.zeros(total_ref.shape, jnp.float32)
        summed_ref[...] = jnp.zeros(summed_ref.shape, jnp.float32)

    query = query_ref[0]
    pieces = [
        jnp.dot(query, key_ref[0, part, 0], preferred_element_type=jnp.float32)
        for part in range(key_ref.shape[1])
    ]
    old_peak = peak_ref[...]
    new_peak = old_peak
    for scores in pieces:
        new_peak = jnp.maximum(new_peak, jnp.max(scores, axis=1, keepdims=True))
    rescale = jnp.exp(old_peak - new_peak)
    total = total_ref[...] * rescale
    summed = summed_ref[...] * rescale
    for part, scores in enumerate(pieces):
        weights = jnp.exp(scores - new_peak)
        total = total + jnp.sum(weights, axis=1, keepdims=True)
        summed = summed + lax.dot_general(
            weights.astype(jnp.bfloat16),
            value_ref[0, part, 0],
            (((1,), (1,)), ((), ())),
            preferred_element_type=jnp.float32,
        )
    total_ref[...] = total
    summed_ref[...] = summed
    peak_ref[...] = new_peak

    @pl.when(block == pl.num_programs(1) - 1)
    def _():
        out_ref[0] = (summed_ref[...] / total_ref[...]).astype(out_ref.dtype)


def flash_attention(queries, kv_tile, sources_per_step=4):
    sample_count, query_count, head_width = queries.shape
    _, source_count, _, _, source_rows = kv_tile.shape
    sources_per_step = math.gcd(source_count, sources_per_step)
    return pl.pallas_call(
        flash_step,
        grid=(sample_count, source_count // sources_per_step),
        in_specs=[
            pl.BlockSpec((1, query_count, head_width), lambda s, k: (s, 0, 0)),
            pl.BlockSpec(
                (1, sources_per_step, 1, head_width, source_rows), lambda s, k: (0, k, s, 0, 0)
            ),
            pl.BlockSpec(
                (1, sources_per_step, 1, head_width, source_rows), lambda s, k: (1, k, s, 0, 0)
            ),
        ],
        out_specs=pl.BlockSpec((1, query_count, head_width), lambda s, k: (s, 0, 0)),
        out_shape=jax.ShapeDtypeStruct(queries.shape, jnp.bfloat16),
        scratch_shapes=[
            pltpu.VMEM((query_count, 1), jnp.float32),
            pltpu.VMEM((query_count, 1), jnp.float32),
            pltpu.VMEM((query_count, head_width), jnp.float32),
        ],
        compiler_params=pltpu.CompilerParams(dimension_semantics=("parallel", "arbitrary")),
    )(queries, kv_tile, kv_tile)


def normalize(rows_in, gain):
    values = rows_in.astype(jnp.float32)
    scale = lax.rsqrt(jnp.mean(values * values, axis=-1, keepdims=True) + 1e-06)
    return values * scale * gain


def shards(
    activations,
    conv_gain,
    conv_weight,
    attention_gain,
    query_weight,
    key_weight,
    value_weight,
    output_weight,
):
    sample_count, own_rows, full_width = activations.shape
    tap_count, local_out, _ = conv_weight.shape
    flank_rows = tap_count // 2
    mine = lax.axis_index("core")
    half_width = full_width // 2
    own_half = lax.all_gather(
        lax.dynamic_slice_in_dim(output_weight, mine * half_width, half_width, 1),
        BATCH,
        axis=0,
        tiled=True,
    )
    gathered_in = gather_batch(activations, 1)
    seq_rows = gathered_in.shape[1]
    active = lax.optimization_barrier(
        jax.nn.gelu(normalize(gathered_in, conv_gain)).astype(jnp.bfloat16)
    )
    framed = with_halo(active, ((SEQ, 1),), flank_rows)
    conv_sum = jnp.zeros((sample_count, local_out, seq_rows), jnp.float32)
    for offset in range(tap_count):
        conv_sum = conv_sum + jnp.einsum(
            "std,ed->set",
            framed[:, offset : offset + seq_rows],
            conv_weight[offset],
            preferred_element_type=jnp.float32,
        )
    column_start = lax.axis_index(BATCH) * local_out
    own_columns = lax.dynamic_slice_in_dim(gathered_in, column_start, local_out, 2)
    residual = jnp.transpose(own_columns, (0, 2, 1)).astype(jnp.float32)
    hidden_part = (residual + conv_sum).astype(jnp.bfloat16)
    hidden_full = gather_batch(hidden_part, 1)
    hidden_float = hidden_full.astype(jnp.float32)
    norm_scale = lax.rsqrt(jnp.mean(hidden_float * hidden_float, axis=1, keepdims=True) + 1e-06)
    normed = (hidden_float * norm_scale * attention_gain[None, :, None]).astype(jnp.bfloat16)
    queries = (
        jnp.einsum("sdt,ed->ste", normed, query_weight, preferred_element_type=jnp.float32)
        * HD ** (-0.5)
    ).astype(jnp.bfloat16)
    key_rows = jnp.einsum(
        "sdt,ed->set", normed, key_weight, preferred_element_type=jnp.float32
    ).astype(jnp.bfloat16)
    value_rows = jnp.einsum(
        "sdt,ed->set", normed, value_weight, preferred_element_type=jnp.float32
    ).astype(jnp.bfloat16)
    kv_rows, own_half = lax.optimization_barrier((jnp.stack([key_rows, value_rows]), own_half))
    kv_tile = lax.all_gather(kv_rows, SEQ, axis=1)
    attended = flash_attention(queries, kv_tile)
    row_start = lax.axis_index(BATCH) * own_rows
    own_hidden = jnp.transpose(
        lax.dynamic_slice_in_dim(hidden_full, row_start, own_rows, 2), (0, 2, 1)
    ).astype(jnp.float32)
    batch_count = lax.axis_size(BATCH)
    head_width = attended.shape[2]
    outgoing = jnp.transpose(
        attended.reshape(sample_count, batch_count, own_rows, head_width), (1, 0, 2, 3)
    )
    arrived = lax.all_to_all(outgoing, BATCH, 0, 0, tiled=False)
    heads_side_by_side = jnp.transpose(arrived, (1, 2, 0, 3)).reshape(
        sample_count, own_rows, batch_count * head_width
    )
    other_half = lax.ppermute(own_half, "core", [(0, 1), (1, 0)])
    own_part = jnp.einsum(
        "std,df->stf", heads_side_by_side, own_half, preferred_element_type=jnp.float32
    )
    other_part = jnp.einsum(
        "std,df->stf", heads_side_by_side, other_half, preferred_element_type=jnp.float32
    )
    branch_rows = jnp.where(
        mine == 0,
        jnp.concatenate([own_part, other_part], axis=2),
        jnp.concatenate([other_part, own_part], axis=2),
    )
    result = own_hidden + branch_rows
    return result.astype(jnp.bfloat16)


def solution(mesh):
    fine = jax.sharding.Mesh(
        mesh.devices.reshape(2, mesh.shape["seq"] // 4, 2, mesh.shape["batch"] // 2, 2),
        SEQ + BATCH,
    )
    placed = (
        P(None, SEQ + BATCH, None),
        P(),
        P(None, BATCH, None),
        P(),
        P(BATCH, None),
        P(BATCH, None),
        P(BATCH, None),
        P(BATCH, None),
    )
    return jax.shard_map(
        shards,
        mesh=fine,
        in_specs=placed,
        out_specs=P(None, SEQ + BATCH, None),
        check_vma=False,
    )
```

```python
import math

import jax
import jax.numpy as jnp
from jax import lax
from jax.experimental import pallas as pl
from jax.experimental.pallas import tpu as pltpu
from jax.sharding import PartitionSpec as P

HD = 192
SEQ = ("chip_x", "chip_z", "core")
BATCH = ("peer_y", "peer_x")


def with_halo(cells, sides, width):
    for axis, dim in sides:
        count = lax.axis_size(axis)
        ends = count - 1
        head = lax.slice_in_dim(cells, 0, width, axis=dim)
        tail = lax.slice_in_dim(cells, cells.shape[dim] - width, cells.shape[dim], axis=dim)
        cells = jnp.concatenate(
            [
                lax.ppermute(tail, axis, [(i, (i + 1) % count) for i in range(ends)]),
                cells,
                lax.ppermute(head, axis, [((i + 1) % count, i) for i in range(ends)]),
            ],
            axis=dim,
        )
    return cells


def gather_batch(block, axis):
    count = lax.axis_size(BATCH)
    spread = block.shape[:axis] + (count,) + block.shape[axis:]
    copies = jnp.broadcast_to(jnp.expand_dims(block, axis), spread)
    arrived = lax.all_to_all(copies, BATCH, axis, axis, tiled=False)
    return arrived.reshape(block.shape[:axis] + (count * block.shape[axis],) + block.shape[axis + 1 :])


def flash_step(query_ref, key_ref, value_ref, out_ref, peak_ref, total_ref, summed_ref):
    block = pl.program_id(1)

    @pl.when(block == 0)
    def _():
        peak_ref[...] = jnp.full(peak_ref.shape, -jnp.inf, jnp.float32)
        total_ref[...] = jnp.zeros(total_ref.shape, jnp.float32)
        summed_ref[...] = jnp.zeros(summed_ref.shape, jnp.float32)

    query = query_ref[0]
    pieces = [
        jnp.dot(query, key_ref[0, part, 0], preferred_element_type=jnp.float32)
        for part in range(key_ref.shape[1])
    ]
    old_peak = peak_ref[...]
    new_peak = old_peak
    for scores in pieces:
        new_peak = jnp.maximum(new_peak, jnp.max(scores, axis=1, keepdims=True))
    rescale = jnp.exp(old_peak - new_peak)
    total = total_ref[...] * rescale
    summed = summed_ref[...] * rescale
    for part, scores in enumerate(pieces):
        weights = jnp.exp(scores - new_peak)
        total = total + jnp.sum(weights, axis=1, keepdims=True)
        summed = summed + lax.dot_general(
            weights.astype(jnp.bfloat16),
            value_ref[0, part, 0],
            (((1,), (1,)), ((), ())),
            preferred_element_type=jnp.float32,
        )
    total_ref[...] = total
    summed_ref[...] = summed
    peak_ref[...] = new_peak

    @pl.when(block == pl.num_programs(1) - 1)
    def _():
        out_ref[0] = (summed_ref[...] / total_ref[...]).astype(out_ref.dtype)


def flash_attention(queries, kv_tile, sources_per_step=8):
    sample_count, query_count, head_width = queries.shape
    _, source_count, _, _, source_rows = kv_tile.shape
    sources_per_step = math.gcd(source_count, sources_per_step)
    return pl.pallas_call(
        flash_step,
        grid=(sample_count, source_count // sources_per_step),
        in_specs=[
            pl.BlockSpec((1, query_count, head_width), lambda s, k: (s, 0, 0)),
            pl.BlockSpec(
                (1, sources_per_step, 1, head_width, source_rows), lambda s, k: (0, k, s, 0, 0)
            ),
            pl.BlockSpec(
                (1, sources_per_step, 1, head_width, source_rows), lambda s, k: (1, k, s, 0, 0)
            ),
        ],
        out_specs=pl.BlockSpec((1, query_count, head_width), lambda s, k: (s, 0, 0)),
        out_shape=jax.ShapeDtypeStruct(queries.shape, jnp.bfloat16),
        scratch_shapes=[
            pltpu.VMEM((query_count, 1), jnp.float32),
            pltpu.VMEM((query_count, 1), jnp.float32),
            pltpu.VMEM((query_count, head_width), jnp.float32),
        ],
        compiler_params=pltpu.CompilerParams(dimension_semantics=("parallel", "arbitrary")),
    )(queries, kv_tile, kv_tile)


def normalize(rows_in, gain):
    values = rows_in.astype(jnp.float32)
    scale = lax.rsqrt(jnp.mean(values * values, axis=-1, keepdims=True) + 1e-06)
    return values * scale * gain


def shards(
    activations,
    conv_gain,
    conv_weight,
    attention_gain,
    query_weight,
    key_weight,
    value_weight,
    output_weight,
):
    sample_count, own_rows, full_width = activations.shape
    tap_count, local_out, _ = conv_weight.shape
    flank_rows = tap_count // 2
    mine = lax.axis_index("core")
    half_width = full_width // 2
    own_half = lax.all_gather(
        lax.dynamic_slice_in_dim(output_weight, mine * half_width, half_width, 1),
        BATCH,
        axis=0,
        tiled=True,
    )
    gathered_in = gather_batch(activations, 1)
    seq_rows = gathered_in.shape[1]
    active = lax.optimization_barrier(
        jax.nn.gelu(normalize(gathered_in, conv_gain)).astype(jnp.bfloat16)
    )
    framed = with_halo(active, ((SEQ, 1),), flank_rows)
    conv_sum = jnp.zeros((sample_count, local_out, seq_rows), jnp.float32)
    for offset in range(tap_count):
        conv_sum = conv_sum + jnp.einsum(
            "std,ed->set",
            framed[:, offset : offset + seq_rows],
            conv_weight[offset],
            preferred_element_type=jnp.float32,
        )
    column_start = lax.axis_index(BATCH) * local_out
    own_columns = lax.dynamic_slice_in_dim(gathered_in, column_start, local_out, 2)
    residual = jnp.transpose(own_columns, (0, 2, 1)).astype(jnp.float32)
    hidden_part, own_half = lax.optimization_barrier(
        ((residual + conv_sum).astype(jnp.bfloat16), own_half)
    )
    hidden_full = gather_batch(hidden_part, 1)
    hidden_float = hidden_full.astype(jnp.float32)
    norm_scale = lax.rsqrt(jnp.mean(hidden_float * hidden_float, axis=1, keepdims=True) + 1e-06)
    normed = (hidden_float * norm_scale * attention_gain[None, :, None]).astype(jnp.bfloat16)
    queries = (
        jnp.einsum("sdt,ed->ste", normed, query_weight, preferred_element_type=jnp.float32)
        * HD ** (-0.5)
    ).astype(jnp.bfloat16)
    key_rows = jnp.einsum(
        "sdt,ed->set", normed, key_weight, preferred_element_type=jnp.float32
    ).astype(jnp.bfloat16)
    value_rows = jnp.einsum(
        "sdt,ed->set", normed, value_weight, preferred_element_type=jnp.float32
    ).astype(jnp.bfloat16)
    kv_rows = jnp.stack([key_rows, value_rows])
    kv_tile = lax.all_gather(kv_rows, SEQ, axis=1)
    attended = flash_attention(queries, kv_tile)
    row_start = lax.axis_index(BATCH) * own_rows
    own_hidden = jnp.transpose(
        lax.dynamic_slice_in_dim(hidden_full, row_start, own_rows, 2), (0, 2, 1)
    ).astype(jnp.float32)
    batch_count = lax.axis_size(BATCH)
    head_width = attended.shape[2]
    outgoing = jnp.transpose(
        attended.reshape(sample_count, batch_count, own_rows, head_width), (1, 0, 2, 3)
    )
    arrived = lax.all_to_all(outgoing, BATCH, 0, 0, tiled=False)
    heads_side_by_side = jnp.transpose(arrived, (1, 2, 0, 3)).reshape(
        sample_count, own_rows, batch_count * head_width
    )
    other_half = lax.ppermute(own_half, "core", [(0, 1), (1, 0)])
    own_part = jnp.einsum(
        "std,df->stf", heads_side_by_side, own_half, preferred_element_type=jnp.float32
    )
    other_part = jnp.einsum(
        "std,df->stf", heads_side_by_side, other_half, preferred_element_type=jnp.float32
    )
    branch_rows = jnp.where(
        mine == 0,
        jnp.concatenate([own_part, other_part], axis=2),
        jnp.concatenate([other_part, own_part], axis=2),
    )
    result = own_hidden + branch_rows
    return result.astype(jnp.bfloat16)


def solution(mesh):
    fine = jax.sharding.Mesh(
        mesh.devices.reshape(2, mesh.shape["seq"] // 4, 2, mesh.shape["batch"] // 2, 2),
        SEQ + BATCH,
    )
    placed = (
        P(None, SEQ + BATCH, None),
        P(),
        P(None, BATCH, None),
        P(),
        P(BATCH, None),
        P(BATCH, None),
        P(BATCH, None),
        P(BATCH, None),
    )
    return jax.shard_map(
        shards,
        mesh=fine,
        in_specs=placed,
        out_specs=P(None, SEQ + BATCH, None),
        check_vma=False,
    )
```

```python
import math

import jax
import jax.numpy as jnp
from jax import lax
from jax.experimental import pallas as pl
from jax.experimental.pallas import tpu as pltpu
from jax.sharding import PartitionSpec as P

HD = 192
SEQ = ("chip_x", "chip_z", "core")
BATCH = ("peer_y", "peer_x")


def with_halo(cells, sides, width):
    for axis, dim in sides:
        count = lax.axis_size(axis)
        ends = count - 1
        head = lax.slice_in_dim(cells, 0, width, axis=dim)
        tail = lax.slice_in_dim(cells, cells.shape[dim] - width, cells.shape[dim], axis=dim)
        cells = jnp.concatenate(
            [
                lax.ppermute(tail, axis, [(i, (i + 1) % count) for i in range(ends)]),
                cells,
                lax.ppermute(head, axis, [((i + 1) % count, i) for i in range(ends)]),
            ],
            axis=dim,
        )
    return cells


def gather_batch(block, axis):
    count = lax.axis_size(BATCH)
    spread = block.shape[:axis] + (count,) + block.shape[axis:]
    copies = jnp.broadcast_to(jnp.expand_dims(block, axis), spread)
    arrived = lax.all_to_all(copies, BATCH, axis, axis, tiled=False)
    return arrived.reshape(block.shape[:axis] + (count * block.shape[axis],) + block.shape[axis + 1 :])


def flash_step(query_ref, key_ref, value_ref, out_ref, peak_ref, total_ref, summed_ref):
    block = pl.program_id(1)

    @pl.when(block == 0)
    def _():
        peak_ref[...] = jnp.full(peak_ref.shape, -jnp.inf, jnp.float32)
        total_ref[...] = jnp.zeros(total_ref.shape, jnp.float32)
        summed_ref[...] = jnp.zeros(summed_ref.shape, jnp.float32)

    query = query_ref[0]
    pieces = [
        jnp.dot(query, key_ref[0, part, 0], preferred_element_type=jnp.float32)
        for part in range(key_ref.shape[1])
    ]
    old_peak = peak_ref[...]
    new_peak = old_peak
    for scores in pieces:
        new_peak = jnp.maximum(new_peak, jnp.max(scores, axis=1, keepdims=True))
    rescale = jnp.exp(old_peak - new_peak)
    total = total_ref[...] * rescale
    summed = summed_ref[...] * rescale
    for part, scores in enumerate(pieces):
        weights = jnp.exp(scores - new_peak)
        total = total + jnp.sum(weights, axis=1, keepdims=True)
        summed = summed + lax.dot_general(
            weights.astype(jnp.bfloat16),
            value_ref[0, part, 0],
            (((1,), (1,)), ((), ())),
            preferred_element_type=jnp.float32,
        )
    total_ref[...] = total
    summed_ref[...] = summed
    peak_ref[...] = new_peak

    @pl.when(block == pl.num_programs(1) - 1)
    def _():
        out_ref[0] = (summed_ref[...] / total_ref[...]).astype(out_ref.dtype)


def flash_attention(queries, kv_tile, sources_per_step=8):
    sample_count, query_count, head_width = queries.shape
    _, source_count, _, _, source_rows = kv_tile.shape
    sources_per_step = math.gcd(source_count, sources_per_step)
    return pl.pallas_call(
        flash_step,
        grid=(sample_count, source_count // sources_per_step),
        in_specs=[
            pl.BlockSpec((1, query_count, head_width), lambda s, k: (s, 0, 0)),
            pl.BlockSpec(
                (1, sources_per_step, 1, head_width, source_rows), lambda s, k: (0, k, s, 0, 0)
            ),
            pl.BlockSpec(
                (1, sources_per_step, 1, head_width, source_rows), lambda s, k: (1, k, s, 0, 0)
            ),
        ],
        out_specs=pl.BlockSpec((1, query_count, head_width), lambda s, k: (s, 0, 0)),
        out_shape=jax.ShapeDtypeStruct(queries.shape, jnp.bfloat16),
        scratch_shapes=[
            pltpu.VMEM((query_count, 1), jnp.float32),
            pltpu.VMEM((query_count, 1), jnp.float32),
            pltpu.VMEM((query_count, head_width), jnp.float32),
        ],
        compiler_params=pltpu.CompilerParams(dimension_semantics=("parallel", "arbitrary")),
    )(queries, kv_tile, kv_tile)


def normalize(rows_in, gain):
    values = rows_in.astype(jnp.float32)
    scale = lax.rsqrt(jnp.mean(values * values, axis=-1, keepdims=True) + 1e-06)
    return values * scale * gain


def shards(
    activations,
    conv_gain,
    conv_weight,
    attention_gain,
    query_weight,
    key_weight,
    value_weight,
    output_weight,
):
    sample_count, own_rows, full_width = activations.shape
    tap_count, local_out, _ = conv_weight.shape
    flank_rows = tap_count // 2
    mine = lax.axis_index("core")
    half_width = full_width // 2
    own_half = lax.all_gather(
        lax.dynamic_slice_in_dim(output_weight, mine * half_width, half_width, 1),
        BATCH,
        axis=0,
        tiled=True,
    )
    gathered_in = gather_batch(activations, 1)
    seq_rows = gathered_in.shape[1]
    active = lax.optimization_barrier(
        jax.nn.gelu(normalize(gathered_in, conv_gain)).astype(jnp.bfloat16)
    )
    framed = with_halo(active, ((SEQ, 1),), flank_rows)
    conv_sum = jnp.zeros((sample_count, local_out, seq_rows), jnp.float32)
    for offset in range(tap_count):
        conv_sum = conv_sum + jnp.einsum(
            "std,ed->set",
            framed[:, offset : offset + seq_rows],
            conv_weight[offset],
            preferred_element_type=jnp.float32,
        )
    column_start = lax.axis_index(BATCH) * local_out
    own_columns = lax.dynamic_slice_in_dim(gathered_in, column_start, local_out, 2)
    residual = jnp.transpose(own_columns, (0, 2, 1)).astype(jnp.float32)
    hidden_part = (residual + conv_sum).astype(jnp.bfloat16)
    hidden_full, own_half = lax.optimization_barrier((gather_batch(hidden_part, 1), own_half))
    hidden_float = hidden_full.astype(jnp.float32)
    norm_scale = lax.rsqrt(jnp.mean(hidden_float * hidden_float, axis=1, keepdims=True) + 1e-06)
    normed = (hidden_float * norm_scale * attention_gain[None, :, None]).astype(jnp.bfloat16)
    queries = (
        jnp.einsum("sdt,ed->ste", normed, query_weight, preferred_element_type=jnp.float32)
        * HD ** (-0.5)
    ).astype(jnp.bfloat16)
    key_rows = jnp.einsum(
        "sdt,ed->set", normed, key_weight, preferred_element_type=jnp.float32
    ).astype(jnp.bfloat16)
    value_rows = jnp.einsum(
        "sdt,ed->set", normed, value_weight, preferred_element_type=jnp.float32
    ).astype(jnp.bfloat16)
    kv_rows = jnp.stack([key_rows, value_rows])
    kv_tile = lax.all_gather(kv_rows, SEQ, axis=1)
    attended = flash_attention(queries, kv_tile)
    row_start = lax.axis_index(BATCH) * own_rows
    own_hidden = jnp.transpose(
        lax.dynamic_slice_in_dim(hidden_full, row_start, own_rows, 2), (0, 2, 1)
    ).astype(jnp.float32)
    batch_count = lax.axis_size(BATCH)
    head_width = attended.shape[2]
    outgoing = jnp.transpose(
        attended.reshape(sample_count, batch_count, own_rows, head_width), (1, 0, 2, 3)
    )
    arrived = lax.all_to_all(outgoing, BATCH, 0, 0, tiled=False)
    heads_side_by_side = jnp.transpose(arrived, (1, 2, 0, 3)).reshape(
        sample_count, own_rows, batch_count * head_width
    )
    other_half = lax.ppermute(own_half, "core", [(0, 1), (1, 0)])
    own_part = jnp.einsum(
        "std,df->stf", heads_side_by_side, own_half, preferred_element_type=jnp.float32
    )
    other_part = jnp.einsum(
        "std,df->stf", heads_side_by_side, other_half, preferred_element_type=jnp.float32
    )
    branch_rows = jnp.where(
        mine == 0,
        jnp.concatenate([own_part, other_part], axis=2),
        jnp.concatenate([other_part, own_part], axis=2),
    )
    result = own_hidden + branch_rows
    return result.astype(jnp.bfloat16)


def solution(mesh):
    fine = jax.sharding.Mesh(
        mesh.devices.reshape(2, mesh.shape["seq"] // 4, 2, mesh.shape["batch"] // 2, 2),
        SEQ + BATCH,
    )
    placed = (
        P(None, SEQ + BATCH, None),
        P(),
        P(None, BATCH, None),
        P(),
        P(BATCH, None),
        P(BATCH, None),
        P(BATCH, None),
        P(BATCH, None),
    )
    return jax.shard_map(
        shards,
        mesh=fine,
        in_specs=placed,
        out_specs=P(None, SEQ + BATCH, None),
        check_vma=False,
    )
```

```python
import math

import jax
import jax.numpy as jnp
from jax import lax
from jax.experimental import pallas as pl
from jax.experimental.pallas import tpu as pltpu
from jax.sharding import PartitionSpec as P

HD = 192
SEQ = ("chip_x", "chip_z", "core")
BATCH = ("peer_y", "peer_x")


def with_halo(cells, sides, width):
    for axis, dim in sides:
        count = lax.axis_size(axis)
        ends = count - 1
        head = lax.slice_in_dim(cells, 0, width, axis=dim)
        tail = lax.slice_in_dim(cells, cells.shape[dim] - width, cells.shape[dim], axis=dim)
        cells = jnp.concatenate(
            [
                lax.ppermute(tail, axis, [(i, (i + 1) % count) for i in range(ends)]),
                cells,
                lax.ppermute(head, axis, [((i + 1) % count, i) for i in range(ends)]),
            ],
            axis=dim,
        )
    return cells


def gather_batch(block, axis):
    count = lax.axis_size(BATCH)
    spread = block.shape[:axis] + (count,) + block.shape[axis:]
    copies = jnp.broadcast_to(jnp.expand_dims(block, axis), spread)
    arrived = lax.all_to_all(copies, BATCH, axis, axis, tiled=False)
    return arrived.reshape(block.shape[:axis] + (count * block.shape[axis],) + block.shape[axis + 1 :])


def flash_step(query_ref, key_ref, value_ref, out_ref, peak_ref, total_ref, summed_ref):
    block = pl.program_id(1)

    @pl.when(block == 0)
    def _():
        peak_ref[...] = jnp.full(peak_ref.shape, -jnp.inf, jnp.float32)
        total_ref[...] = jnp.zeros(total_ref.shape, jnp.float32)
        summed_ref[...] = jnp.zeros(summed_ref.shape, jnp.float32)

    query = query_ref[0]
    pieces = [
        jnp.dot(query, key_ref[0, part, 0], preferred_element_type=jnp.float32)
        for part in range(key_ref.shape[1])
    ]
    old_peak = peak_ref[...]
    new_peak = old_peak
    for scores in pieces:
        new_peak = jnp.maximum(new_peak, jnp.max(scores, axis=1, keepdims=True))
    rescale = jnp.exp(old_peak - new_peak)
    total = total_ref[...] * rescale
    summed = summed_ref[...] * rescale
    for part, scores in enumerate(pieces):
        weights = jnp.exp(scores - new_peak)
        total = total + jnp.sum(weights, axis=1, keepdims=True)
        summed = summed + lax.dot_general(
            weights.astype(jnp.bfloat16),
            value_ref[0, part, 0],
            (((1,), (1,)), ((), ())),
            preferred_element_type=jnp.float32,
        )
    total_ref[...] = total
    summed_ref[...] = summed
    peak_ref[...] = new_peak

    @pl.when(block == pl.num_programs(1) - 1)
    def _():
        finished = (summed_ref[...] / total_ref[...]).astype(out_ref.dtype)
        out_ref[:, 0] = finished.reshape(out_ref.shape[0], out_ref.shape[2], out_ref.shape[3])


def flash_attention(queries, kv_tile, peers, sources_per_step=8):
    sample_count, query_count, head_width = queries.shape
    _, source_count, _, _, source_rows = kv_tile.shape
    sources_per_step = math.gcd(source_count, sources_per_step)
    return pl.pallas_call(
        flash_step,
        grid=(sample_count, source_count // sources_per_step),
        in_specs=[
            pl.BlockSpec((1, query_count, head_width), lambda s, k: (s, 0, 0)),
            pl.BlockSpec(
                (1, sources_per_step, 1, head_width, source_rows), lambda s, k: (0, k, s, 0, 0)
            ),
            pl.BlockSpec(
                (1, sources_per_step, 1, head_width, source_rows), lambda s, k: (1, k, s, 0, 0)
            ),
        ],
        out_specs=pl.BlockSpec(
            (peers, 1, query_count // peers, head_width), lambda s, k: (0, s, 0, 0)
        ),
        out_shape=jax.ShapeDtypeStruct(
            (peers, sample_count, query_count // peers, head_width), jnp.bfloat16
        ),
        scratch_shapes=[
            pltpu.VMEM((query_count, 1), jnp.float32),
            pltpu.VMEM((query_count, 1), jnp.float32),
            pltpu.VMEM((query_count, head_width), jnp.float32),
        ],
        compiler_params=pltpu.CompilerParams(dimension_semantics=("parallel", "arbitrary")),
    )(queries, kv_tile, kv_tile)


def normalize(rows_in, gain):
    values = rows_in.astype(jnp.float32)
    scale = lax.rsqrt(jnp.mean(values * values, axis=-1, keepdims=True) + 1e-06)
    return values * scale * gain


def shards(
    activations,
    conv_gain,
    conv_weight,
    attention_gain,
    query_weight,
    key_weight,
    value_weight,
    output_weight,
):
    sample_count, own_rows, full_width = activations.shape
    tap_count, local_out, _ = conv_weight.shape
    flank_rows = tap_count // 2
    mine = lax.axis_index("core")
    half_width = full_width // 2
    own_half = lax.all_gather(
        lax.dynamic_slice_in_dim(output_weight, mine * half_width, half_width, 1),
        BATCH,
        axis=0,
        tiled=True,
    )
    gathered_in = gather_batch(activations, 1)
    seq_rows = gathered_in.shape[1]
    active = lax.optimization_barrier(
        jax.nn.gelu(normalize(gathered_in, conv_gain)).astype(jnp.bfloat16)
    )
    framed = with_halo(active, ((SEQ, 1),), flank_rows)
    conv_sum = jnp.zeros((sample_count, local_out, seq_rows), jnp.float32)
    for offset in range(tap_count):
        conv_sum = conv_sum + jnp.einsum(
            "std,ed->set",
            framed[:, offset : offset + seq_rows],
            conv_weight[offset],
            preferred_element_type=jnp.float32,
        )
    column_start = lax.axis_index(BATCH) * local_out
    own_columns = lax.dynamic_slice_in_dim(gathered_in, column_start, local_out, 2)
    residual = jnp.transpose(own_columns, (0, 2, 1)).astype(jnp.float32)
    hidden_part = (residual + conv_sum).astype(jnp.bfloat16)
    hidden_full, own_half = lax.optimization_barrier((gather_batch(hidden_part, 1), own_half))
    hidden_float = hidden_full.astype(jnp.float32)
    norm_scale = lax.rsqrt(jnp.mean(hidden_float * hidden_float, axis=1, keepdims=True) + 1e-06)
    normed = (hidden_float * norm_scale * attention_gain[None, :, None]).astype(jnp.bfloat16)
    queries = (
        jnp.einsum("sdt,ed->ste", normed, query_weight, preferred_element_type=jnp.float32)
        * HD ** (-0.5)
    ).astype(jnp.bfloat16)
    key_rows = jnp.einsum(
        "sdt,ed->set", normed, key_weight, preferred_element_type=jnp.float32
    ).astype(jnp.bfloat16)
    value_rows = jnp.einsum(
        "sdt,ed->set", normed, value_weight, preferred_element_type=jnp.float32
    ).astype(jnp.bfloat16)
    kv_rows = jnp.stack([key_rows, value_rows])
    kv_tile = lax.all_gather(kv_rows, SEQ, axis=1)
    batch_count = lax.axis_size(BATCH)
    attended = flash_attention(queries, kv_tile, batch_count)
    row_start = lax.axis_index(BATCH) * own_rows
    own_hidden = jnp.transpose(
        lax.dynamic_slice_in_dim(hidden_full, row_start, own_rows, 2), (0, 2, 1)
    ).astype(jnp.float32)
    head_width = attended.shape[3]
    arrived = lax.all_to_all(attended, BATCH, 0, 0, tiled=False)
    other_half = lax.ppermute(own_half, "core", [(0, 1), (1, 0)])
    own_part = jnp.einsum(
        "hstd,hdf->stf",
        arrived,
        own_half.reshape(batch_count, head_width, -1),
        preferred_element_type=jnp.float32,
    )
    other_part = jnp.einsum(
        "hstd,hdf->stf",
        arrived,
        other_half.reshape(batch_count, head_width, -1),
        preferred_element_type=jnp.float32,
    )
    branch_rows = jnp.where(
        mine == 0,
        jnp.concatenate([own_part, other_part], axis=2),
        jnp.concatenate([other_part, own_part], axis=2),
    )
    result = own_hidden + branch_rows
    return result.astype(jnp.bfloat16)


def solution(mesh):
    fine = jax.sharding.Mesh(
        mesh.devices.reshape(2, mesh.shape["seq"] // 4, 2, mesh.shape["batch"] // 2, 2),
        SEQ + BATCH,
    )
    placed = (
        P(None, SEQ + BATCH, None),
        P(),
        P(None, BATCH, None),
        P(),
        P(BATCH, None),
        P(BATCH, None),
        P(BATCH, None),
        P(BATCH, None),
    )
    return jax.shard_map(
        shards,
        mesh=fine,
        in_specs=placed,
        out_specs=P(None, SEQ + BATCH, None),
        check_vma=False,
    )
```

```python
import math

import jax
import jax.numpy as jnp
from jax import lax
from jax.experimental import pallas as pl
from jax.experimental.pallas import tpu as pltpu
from jax.sharding import PartitionSpec as P

HD = 192
SEQ = ("chip_x", "chip_z", "core")
BATCH = ("peer_y", "peer_x")


def with_halo(cells, raw, activate, axis, width):
    count = lax.axis_size(axis)
    ends = count - 1
    head = raw[:, :width]
    tail = raw[:, raw.shape[1] - width :]
    before = lax.ppermute(tail, axis, [(i, (i + 1) % count) for i in range(ends)])
    after = lax.ppermute(head, axis, [((i + 1) % count, i) for i in range(ends)])
    return jnp.concatenate([activate(before), cells, activate(after)], axis=1)


def gather_batch(block, axis):
    count = lax.axis_size(BATCH)
    spread = block.shape[:axis] + (count,) + block.shape[axis:]
    copies = jnp.broadcast_to(jnp.expand_dims(block, axis), spread)
    arrived = lax.all_to_all(copies, BATCH, axis, axis, tiled=False)
    return arrived.reshape(block.shape[:axis] + (count * block.shape[axis],) + block.shape[axis + 1 :])


def flash_step(query_ref, key_ref, value_ref, out_ref, peak_ref, total_ref, summed_ref):
    block = pl.program_id(1)

    @pl.when(block == 0)
    def _():
        peak_ref[...] = jnp.full(peak_ref.shape, -jnp.inf, jnp.float32)
        total_ref[...] = jnp.zeros(total_ref.shape, jnp.float32)
        summed_ref[...] = jnp.zeros(summed_ref.shape, jnp.float32)

    query = query_ref[0]
    pieces = [
        jnp.dot(query, key_ref[0, part, 0], preferred_element_type=jnp.float32)
        for part in range(key_ref.shape[1])
    ]
    old_peak = peak_ref[...]
    new_peak = old_peak
    for scores in pieces:
        new_peak = jnp.maximum(new_peak, jnp.max(scores, axis=1, keepdims=True))
    rescale = jnp.exp(old_peak - new_peak)
    total = total_ref[...] * rescale
    summed = summed_ref[...] * rescale
    for part, scores in enumerate(pieces):
        weights = jnp.exp(scores - new_peak)
        total = total + jnp.sum(weights, axis=1, keepdims=True)
        summed = summed + lax.dot_general(
            weights.astype(jnp.bfloat16),
            value_ref[0, part, 0],
            (((1,), (1,)), ((), ())),
            preferred_element_type=jnp.float32,
        )
    total_ref[...] = total
    summed_ref[...] = summed
    peak_ref[...] = new_peak

    @pl.when(block == pl.num_programs(1) - 1)
    def _():
        finished = (summed_ref[...] / total_ref[...]).astype(out_ref.dtype)
        out_ref[:, 0] = finished.reshape(out_ref.shape[0], out_ref.shape[2], out_ref.shape[3])


def flash_attention(queries, kv_tile, peers, sources_per_step=8):
    sample_count, query_count, head_width = queries.shape
    _, source_count, _, _, source_rows = kv_tile.shape
    sources_per_step = math.gcd(source_count, sources_per_step)
    return pl.pallas_call(
        flash_step,
        grid=(sample_count, source_count // sources_per_step),
        in_specs=[
            pl.BlockSpec((1, query_count, head_width), lambda s, k: (s, 0, 0)),
            pl.BlockSpec(
                (1, sources_per_step, 1, head_width, source_rows), lambda s, k: (0, k, s, 0, 0)
            ),
            pl.BlockSpec(
                (1, sources_per_step, 1, head_width, source_rows), lambda s, k: (1, k, s, 0, 0)
            ),
        ],
        out_specs=pl.BlockSpec(
            (peers, 1, query_count // peers, head_width), lambda s, k: (0, s, 0, 0)
        ),
        out_shape=jax.ShapeDtypeStruct(
            (peers, sample_count, query_count // peers, head_width), jnp.bfloat16
        ),
        scratch_shapes=[
            pltpu.VMEM((query_count, 1), jnp.float32),
            pltpu.VMEM((query_count, 1), jnp.float32),
            pltpu.VMEM((query_count, head_width), jnp.float32),
        ],
        compiler_params=pltpu.CompilerParams(dimension_semantics=("parallel", "arbitrary")),
    )(queries, kv_tile, kv_tile)


def normalize(rows_in, gain):
    values = rows_in.astype(jnp.float32)
    scale = lax.rsqrt(jnp.mean(values * values, axis=-1, keepdims=True) + 1e-06)
    return values * scale * gain


def shards(
    activations,
    conv_gain,
    conv_weight,
    attention_gain,
    query_weight,
    key_weight,
    value_weight,
    output_weight,
):
    sample_count, own_rows, full_width = activations.shape
    tap_count, local_out, _ = conv_weight.shape
    flank_rows = tap_count // 2
    mine = lax.axis_index("core")
    half_width = full_width // 2
    own_half = lax.all_gather(
        lax.dynamic_slice_in_dim(output_weight, mine * half_width, half_width, 1),
        BATCH,
        axis=0,
        tiled=True,
    )
    gathered_in = gather_batch(activations, 1)
    seq_rows = gathered_in.shape[1]
    def activate(rows_in):
        return jax.nn.gelu(normalize(rows_in, conv_gain)).astype(jnp.bfloat16)

    active = lax.optimization_barrier(activate(gathered_in))
    framed = with_halo(active, gathered_in, activate, SEQ, flank_rows)
    conv_sum = jnp.zeros((sample_count, local_out, seq_rows), jnp.float32)
    for offset in range(tap_count):
        conv_sum = conv_sum + jnp.einsum(
            "std,ed->set",
            framed[:, offset : offset + seq_rows],
            conv_weight[offset],
            preferred_element_type=jnp.float32,
        )
    column_start = lax.axis_index(BATCH) * local_out
    own_columns = lax.dynamic_slice_in_dim(gathered_in, column_start, local_out, 2)
    residual = jnp.transpose(own_columns, (0, 2, 1)).astype(jnp.float32)
    hidden_part = (residual + conv_sum).astype(jnp.bfloat16)
    hidden_full, own_half = lax.optimization_barrier((gather_batch(hidden_part, 1), own_half))
    hidden_float = hidden_full.astype(jnp.float32)
    norm_scale = lax.rsqrt(jnp.mean(hidden_float * hidden_float, axis=1, keepdims=True) + 1e-06)
    normed = (hidden_float * norm_scale * attention_gain[None, :, None]).astype(jnp.bfloat16)
    queries = (
        jnp.einsum("sdt,ed->ste", normed, query_weight, preferred_element_type=jnp.float32)
        * HD ** (-0.5)
    ).astype(jnp.bfloat16)
    key_rows = jnp.einsum(
        "sdt,ed->set", normed, key_weight, preferred_element_type=jnp.float32
    ).astype(jnp.bfloat16)
    value_rows = jnp.einsum(
        "sdt,ed->set", normed, value_weight, preferred_element_type=jnp.float32
    ).astype(jnp.bfloat16)
    kv_rows = jnp.stack([key_rows, value_rows])
    kv_tile = lax.all_gather(kv_rows, SEQ, axis=1)
    batch_count = lax.axis_size(BATCH)
    attended = flash_attention(queries, kv_tile, batch_count)
    row_start = lax.axis_index(BATCH) * own_rows
    own_hidden = jnp.transpose(
        lax.dynamic_slice_in_dim(hidden_full, row_start, own_rows, 2), (0, 2, 1)
    ).astype(jnp.float32)
    head_width = attended.shape[3]
    arrived = lax.all_to_all(attended, BATCH, 0, 0, tiled=False)
    other_half = lax.ppermute(own_half, "core", [(0, 1), (1, 0)])
    own_part = jnp.einsum(
        "hstd,hdf->stf",
        arrived,
        own_half.reshape(batch_count, head_width, -1),
        preferred_element_type=jnp.float32,
    )
    other_part = jnp.einsum(
        "hstd,hdf->stf",
        arrived,
        other_half.reshape(batch_count, head_width, -1),
        preferred_element_type=jnp.float32,
    )
    branch_rows = jnp.where(
        mine == 0,
        jnp.concatenate([own_part, other_part], axis=2),
        jnp.concatenate([other_part, own_part], axis=2),
    )
    result = own_hidden + branch_rows
    return result.astype(jnp.bfloat16)


def solution(mesh):
    fine = jax.sharding.Mesh(
        mesh.devices.reshape(2, mesh.shape["seq"] // 4, 2, mesh.shape["batch"] // 2, 2),
        SEQ + BATCH,
    )
    placed = (
        P(None, SEQ + BATCH, None),
        P(),
        P(None, BATCH, None),
        P(),
        P(BATCH, None),
        P(BATCH, None),
        P(BATCH, None),
        P(BATCH, None),
    )
    return jax.shard_map(
        shards,
        mesh=fine,
        in_specs=placed,
        out_specs=P(None, SEQ + BATCH, None),
        check_vma=False,
    )
```

```python
import math

import jax
import jax.numpy as jnp
from jax import lax
from jax.experimental import pallas as pl
from jax.experimental.pallas import tpu as pltpu
from jax.sharding import PartitionSpec as P

HD = 192
SEQ = ("chip_x", "chip_z", "core")
BATCH = ("peer_y", "peer_x")


def with_halo(cells, raw, activate, axis, width):
    count = lax.axis_size(axis)
    ends = count - 1
    head = raw[:, :width]
    tail = raw[:, raw.shape[1] - width :]
    before = lax.ppermute(tail, axis, [(i, (i + 1) % count) for i in range(ends)])
    after = lax.ppermute(head, axis, [((i + 1) % count, i) for i in range(ends)])
    return jnp.concatenate([activate(before), cells, activate(after)], axis=1)


def gather_batch(block, axis):
    count = lax.axis_size(BATCH)
    spread = block.shape[:axis] + (count,) + block.shape[axis:]
    copies = jnp.broadcast_to(jnp.expand_dims(block, axis), spread)
    arrived = lax.all_to_all(copies, BATCH, axis, axis, tiled=False)
    return arrived.reshape(block.shape[:axis] + (count * block.shape[axis],) + block.shape[axis + 1 :])


def flash_step(query_ref, key_ref, value_ref, out_ref, peak_ref, total_ref, summed_ref):
    block = pl.program_id(1)

    @pl.when(block == 0)
    def _():
        peak_ref[...] = jnp.full(peak_ref.shape, -jnp.inf, jnp.float32)
        total_ref[...] = jnp.zeros(total_ref.shape, jnp.float32)
        summed_ref[...] = jnp.zeros(summed_ref.shape, jnp.float32)

    query = query_ref[0]
    pieces = [
        jnp.dot(query, key_ref[0, part, 0], preferred_element_type=jnp.float32)
        for part in range(key_ref.shape[1])
    ]
    old_peak = peak_ref[...]
    new_peak = old_peak
    for scores in pieces:
        new_peak = jnp.maximum(new_peak, jnp.max(scores, axis=1, keepdims=True))
    rescale = jnp.exp(old_peak - new_peak)
    total = total_ref[...] * rescale
    summed = summed_ref[...] * rescale
    for part, scores in enumerate(pieces):
        weights = jnp.exp(scores - new_peak)
        total = total + jnp.sum(weights, axis=1, keepdims=True)
        summed = summed + lax.dot_general(
            weights.astype(jnp.bfloat16),
            value_ref[0, part, 0],
            (((1,), (1,)), ((), ())),
            preferred_element_type=jnp.float32,
        )
    total_ref[...] = total
    summed_ref[...] = summed
    peak_ref[...] = new_peak

    @pl.when(block == pl.num_programs(1) - 1)
    def _():
        finished = (summed_ref[...] / total_ref[...]).astype(out_ref.dtype)
        out_ref[:, 0] = finished.reshape(out_ref.shape[0], out_ref.shape[2], out_ref.shape[3])


def flash_attention(queries, kv_tile, peers, sources_per_step=8):
    sample_count, query_count, head_width = queries.shape
    _, source_count, _, _, source_rows = kv_tile.shape
    sources_per_step = math.gcd(source_count, sources_per_step)
    return pl.pallas_call(
        flash_step,
        grid=(sample_count, source_count // sources_per_step),
        in_specs=[
            pl.BlockSpec((1, query_count, head_width), lambda s, k: (s, 0, 0)),
            pl.BlockSpec(
                (1, sources_per_step, 1, head_width, source_rows), lambda s, k: (0, k, s, 0, 0)
            ),
            pl.BlockSpec(
                (1, sources_per_step, 1, head_width, source_rows), lambda s, k: (1, k, s, 0, 0)
            ),
        ],
        out_specs=pl.BlockSpec(
            (peers, 1, query_count // peers, head_width), lambda s, k: (0, s, 0, 0)
        ),
        out_shape=jax.ShapeDtypeStruct(
            (peers, sample_count, query_count // peers, head_width), jnp.bfloat16
        ),
        scratch_shapes=[
            pltpu.VMEM((query_count, 1), jnp.float32),
            pltpu.VMEM((query_count, 1), jnp.float32),
            pltpu.VMEM((query_count, head_width), jnp.float32),
        ],
        compiler_params=pltpu.CompilerParams(dimension_semantics=("parallel", "arbitrary")),
    )(queries, kv_tile, kv_tile)


def normalize(rows_in, gain):
    values = rows_in.astype(jnp.float32)
    scale = lax.rsqrt(jnp.mean(values * values, axis=-1, keepdims=True) + 1e-06)
    return values * scale * gain


def shards(
    activations,
    conv_gain,
    conv_weight,
    attention_gain,
    query_weight,
    key_weight,
    value_weight,
    output_weight,
):
    sample_count, own_rows, full_width = activations.shape
    tap_count, local_out, _ = conv_weight.shape
    flank_rows = tap_count // 2
    mine = lax.axis_index("core")
    half_width = full_width // 2
    own_half = lax.all_gather(
        lax.dynamic_slice_in_dim(output_weight, mine * half_width, half_width, 1),
        BATCH,
        axis=0,
        tiled=True,
    )
    gathered_in = gather_batch(activations, 1)
    seq_rows = gathered_in.shape[1]
    def activate(rows_in):
        return jax.nn.gelu(normalize(rows_in, conv_gain)).astype(jnp.bfloat16)

    active = lax.optimization_barrier(activate(gathered_in))
    framed = with_halo(active, gathered_in, activate, SEQ, flank_rows)
    conv_sum = jnp.zeros((sample_count, local_out, seq_rows), jnp.float32)
    for offset in range(tap_count):
        conv_sum = conv_sum + jnp.einsum(
            "std,ed->set",
            framed[:, offset : offset + seq_rows],
            conv_weight[offset],
            preferred_element_type=jnp.float32,
        )
    column_start = lax.axis_index(BATCH) * local_out
    own_columns = lax.dynamic_slice_in_dim(gathered_in, column_start, local_out, 2)
    residual = jnp.transpose(own_columns, (0, 2, 1)).astype(jnp.float32)
    hidden_part = (residual + conv_sum).astype(jnp.bfloat16)
    hidden_full, own_half = lax.optimization_barrier((gather_batch(hidden_part, 1), own_half))
    hidden_float = hidden_full.astype(jnp.float32)
    norm_scale = lax.rsqrt(jnp.mean(hidden_float * hidden_float, axis=1, keepdims=True) + 1e-06)
    normed = (hidden_float * norm_scale * attention_gain[None, :, None]).astype(jnp.bfloat16)
    queries = (
        jnp.einsum("sdt,ed->ste", normed, query_weight, preferred_element_type=jnp.float32)
        * HD ** (-0.5)
    ).astype(jnp.bfloat16)
    key_rows = jnp.einsum(
        "sdt,ed->set", normed, key_weight, preferred_element_type=jnp.float32
    ).astype(jnp.bfloat16)
    value_rows = jnp.einsum(
        "sdt,ed->set", normed, value_weight, preferred_element_type=jnp.float32
    ).astype(jnp.bfloat16)
    kv_rows = jnp.stack([key_rows, value_rows])
    row_start = lax.axis_index(BATCH) * own_rows
    own_hidden = jnp.transpose(
        lax.dynamic_slice_in_dim(hidden_full, row_start, own_rows, 2), (0, 2, 1)
    ).astype(jnp.float32)
    kv_tile, own_hidden = lax.optimization_barrier(
        (lax.all_gather(kv_rows, SEQ, axis=1), own_hidden)
    )
    batch_count = lax.axis_size(BATCH)
    attended = flash_attention(queries, kv_tile, batch_count)
    head_width = attended.shape[3]
    arrived = lax.all_to_all(attended, BATCH, 0, 0, tiled=False)
    other_half = lax.ppermute(own_half, "core", [(0, 1), (1, 0)])
    own_part = jnp.einsum(
        "hstd,hdf->stf",
        arrived,
        own_half.reshape(batch_count, head_width, -1),
        preferred_element_type=jnp.float32,
    )
    other_part = jnp.einsum(
        "hstd,hdf->stf",
        arrived,
        other_half.reshape(batch_count, head_width, -1),
        preferred_element_type=jnp.float32,
    )
    branch_rows = jnp.where(
        mine == 0,
        jnp.concatenate([own_part, other_part], axis=2),
        jnp.concatenate([other_part, own_part], axis=2),
    )
    result = own_hidden + branch_rows
    return result.astype(jnp.bfloat16)


def solution(mesh):
    fine = jax.sharding.Mesh(
        mesh.devices.reshape(2, mesh.shape["seq"] // 4, 2, mesh.shape["batch"] // 2, 2),
        SEQ + BATCH,
    )
    placed = (
        P(None, SEQ + BATCH, None),
        P(),
        P(None, BATCH, None),
        P(),
        P(BATCH, None),
        P(BATCH, None),
        P(BATCH, None),
        P(BATCH, None),
    )
    return jax.shard_map(
        shards,
        mesh=fine,
        in_specs=placed,
        out_specs=P(None, SEQ + BATCH, None),
        check_vma=False,
    )
```

```python
import math

import jax
import jax.numpy as jnp
from jax import lax
from jax.experimental import pallas as pl
from jax.experimental.pallas import tpu as pltpu
from jax.sharding import PartitionSpec as P

HD = 192
SEQ = ("chip_x", "chip_z", "core")
BATCH = ("peer_y", "peer_x")


def with_halo(cells, sides, width):
    for axis, dim in sides:
        count = lax.axis_size(axis)
        ends = count - 1
        head = lax.slice_in_dim(cells, 0, width, axis=dim)
        tail = lax.slice_in_dim(cells, cells.shape[dim] - width, cells.shape[dim], axis=dim)
        cells = jnp.concatenate(
            [
                lax.ppermute(tail, axis, [(i, (i + 1) % count) for i in range(ends)]),
                cells,
                lax.ppermute(head, axis, [((i + 1) % count, i) for i in range(ends)]),
            ],
            axis=dim,
        )
    return cells


def gather_batch(block, axis):
    count = lax.axis_size(BATCH)
    spread = block.shape[:axis] + (count,) + block.shape[axis:]
    copies = jnp.broadcast_to(jnp.expand_dims(block, axis), spread)
    arrived = lax.all_to_all(copies, BATCH, axis, axis, tiled=False)
    return arrived.reshape(block.shape[:axis] + (count * block.shape[axis],) + block.shape[axis + 1 :])


def flash_step(query_ref, key_ref, value_ref, out_ref, peak_ref, total_ref, summed_ref):
    block = pl.program_id(1)

    @pl.when(block == 0)
    def _():
        peak_ref[...] = jnp.full(peak_ref.shape, -jnp.inf, jnp.float32)
        total_ref[...] = jnp.zeros(total_ref.shape, jnp.float32)
        summed_ref[...] = jnp.zeros(summed_ref.shape, jnp.float32)

    query = query_ref[0]
    pieces = [
        jnp.dot(query, key_ref[0, part, 0], preferred_element_type=jnp.float32)
        for part in range(key_ref.shape[1])
    ]
    old_peak = peak_ref[...]
    new_peak = old_peak
    for scores in pieces:
        new_peak = jnp.maximum(new_peak, jnp.max(scores, axis=1, keepdims=True))
    rescale = jnp.exp(old_peak - new_peak)
    total = total_ref[...] * rescale
    summed = summed_ref[...] * rescale
    for part, scores in enumerate(pieces):
        weights = jnp.exp(scores - new_peak)
        total = total + jnp.sum(weights, axis=1, keepdims=True)
        summed = summed + lax.dot_general(
            weights.astype(jnp.bfloat16),
            value_ref[0, part, 0],
            (((1,), (1,)), ((), ())),
            preferred_element_type=jnp.float32,
        )
    total_ref[...] = total
    summed_ref[...] = summed
    peak_ref[...] = new_peak

    @pl.when(block == pl.num_programs(1) - 1)
    def _():
        finished = (summed_ref[...] / total_ref[...]).astype(out_ref.dtype)
        out_ref[:, 0] = finished.reshape(out_ref.shape[0], out_ref.shape[2], out_ref.shape[3])


def flash_attention(queries, kv_tile, peers, sources_per_step=16):
    sample_count, query_count, head_width = queries.shape
    _, source_count, _, _, source_rows = kv_tile.shape
    sources_per_step = math.gcd(source_count, sources_per_step)
    return pl.pallas_call(
        flash_step,
        grid=(sample_count, source_count // sources_per_step),
        in_specs=[
            pl.BlockSpec((1, query_count, head_width), lambda s, k: (s, 0, 0)),
            pl.BlockSpec(
                (1, sources_per_step, 1, head_width, source_rows), lambda s, k: (0, k, s, 0, 0)
            ),
            pl.BlockSpec(
                (1, sources_per_step, 1, head_width, source_rows), lambda s, k: (1, k, s, 0, 0)
            ),
        ],
        out_specs=pl.BlockSpec(
            (peers, 1, query_count // peers, head_width), lambda s, k: (0, s, 0, 0)
        ),
        out_shape=jax.ShapeDtypeStruct(
            (peers, sample_count, query_count // peers, head_width), jnp.bfloat16
        ),
        scratch_shapes=[
            pltpu.VMEM((query_count, 1), jnp.float32),
            pltpu.VMEM((query_count, 1), jnp.float32),
            pltpu.VMEM((query_count, head_width), jnp.float32),
        ],
        compiler_params=pltpu.CompilerParams(dimension_semantics=("parallel", "arbitrary")),
    )(queries, kv_tile, kv_tile)


def normalize(rows_in, gain):
    values = rows_in.astype(jnp.float32)
    scale = lax.rsqrt(jnp.mean(values * values, axis=-1, keepdims=True) + 1e-06)
    return values * scale * gain


def shards(
    activations,
    conv_gain,
    conv_weight,
    attention_gain,
    query_weight,
    key_weight,
    value_weight,
    output_weight,
):
    sample_count, own_rows, full_width = activations.shape
    tap_count, local_out, _ = conv_weight.shape
    flank_rows = tap_count // 2
    mine = lax.axis_index("core")
    half_width = full_width // 2
    own_half = lax.all_gather(
        lax.dynamic_slice_in_dim(output_weight, mine * half_width, half_width, 1),
        BATCH,
        axis=0,
        tiled=True,
    )
    gathered_in = gather_batch(activations, 1)
    seq_rows = gathered_in.shape[1]
    active = lax.optimization_barrier(
        jax.nn.gelu(normalize(gathered_in, conv_gain)).astype(jnp.bfloat16)
    )
    framed = with_halo(active, ((SEQ, 1),), flank_rows)
    conv_sum = jnp.zeros((sample_count, local_out, seq_rows), jnp.float32)
    for offset in range(tap_count):
        conv_sum = conv_sum + jnp.einsum(
            "std,ed->set",
            framed[:, offset : offset + seq_rows],
            conv_weight[offset],
            preferred_element_type=jnp.float32,
        )
    column_start = lax.axis_index(BATCH) * local_out
    own_columns = lax.dynamic_slice_in_dim(gathered_in, column_start, local_out, 2)
    residual = jnp.transpose(own_columns, (0, 2, 1)).astype(jnp.float32)
    hidden_part = (residual + conv_sum).astype(jnp.bfloat16)
    hidden_full, own_half = lax.optimization_barrier((gather_batch(hidden_part, 1), own_half))
    hidden_float = hidden_full.astype(jnp.float32)
    norm_scale = lax.rsqrt(jnp.mean(hidden_float * hidden_float, axis=1, keepdims=True) + 1e-06)
    normed = (hidden_float * norm_scale * attention_gain[None, :, None]).astype(jnp.bfloat16)
    queries = (
        jnp.einsum("sdt,ed->ste", normed, query_weight, preferred_element_type=jnp.float32)
        * HD ** (-0.5)
    ).astype(jnp.bfloat16)
    key_rows = jnp.einsum(
        "sdt,ed->set", normed, key_weight, preferred_element_type=jnp.float32
    ).astype(jnp.bfloat16)
    value_rows = jnp.einsum(
        "sdt,ed->set", normed, value_weight, preferred_element_type=jnp.float32
    ).astype(jnp.bfloat16)
    kv_rows = jnp.stack([key_rows, value_rows])
    kv_tile = lax.all_gather(kv_rows, SEQ, axis=1)
    batch_count = lax.axis_size(BATCH)
    attended = flash_attention(queries, kv_tile, batch_count)
    row_start = lax.axis_index(BATCH) * own_rows
    own_hidden = jnp.transpose(
        lax.dynamic_slice_in_dim(hidden_full, row_start, own_rows, 2), (0, 2, 1)
    ).astype(jnp.float32)
    head_width = attended.shape[3]
    arrived = lax.all_to_all(attended, BATCH, 0, 0, tiled=False)
    other_half = lax.ppermute(own_half, "core", [(0, 1), (1, 0)])
    own_part = jnp.einsum(
        "hstd,hdf->stf",
        arrived,
        own_half.reshape(batch_count, head_width, -1),
        preferred_element_type=jnp.float32,
    )
    other_part = jnp.einsum(
        "hstd,hdf->stf",
        arrived,
        other_half.reshape(batch_count, head_width, -1),
        preferred_element_type=jnp.float32,
    )
    branch_rows = jnp.where(
        mine == 0,
        jnp.concatenate([own_part, other_part], axis=2),
        jnp.concatenate([other_part, own_part], axis=2),
    )
    result = own_hidden + branch_rows
    return result.astype(jnp.bfloat16)


def solution(mesh):
    fine = jax.sharding.Mesh(
        mesh.devices.reshape(2, mesh.shape["seq"] // 4, 2, mesh.shape["batch"] // 2, 2),
        SEQ + BATCH,
    )
    placed = (
        P(None, SEQ + BATCH, None),
        P(),
        P(None, BATCH, None),
        P(),
        P(BATCH, None),
        P(BATCH, None),
        P(BATCH, None),
        P(BATCH, None),
    )
    return jax.shard_map(
        shards,
        mesh=fine,
        in_specs=placed,
        out_specs=P(None, SEQ + BATCH, None),
        check_vma=False,
    )
```

```python
import math

import jax
import jax.numpy as jnp
from jax import lax
from jax.experimental import pallas as pl
from jax.experimental.pallas import tpu as pltpu
from jax.sharding import PartitionSpec as P

HD = 192
SEQ = ("chip_x", "chip_z", "core")
BATCH = ("peer_y", "peer_x")


def with_halo(cells, sides, width):
    for axis, dim in sides:
        count = lax.axis_size(axis)
        ends = count - 1
        head = lax.slice_in_dim(cells, 0, width, axis=dim)
        tail = lax.slice_in_dim(cells, cells.shape[dim] - width, cells.shape[dim], axis=dim)
        cells = jnp.concatenate(
            [
                lax.ppermute(tail, axis, [(i, (i + 1) % count) for i in range(ends)]),
                cells,
                lax.ppermute(head, axis, [((i + 1) % count, i) for i in range(ends)]),
            ],
            axis=dim,
        )
    return cells


def gather_batch(block, axis):
    count = lax.axis_size(BATCH)
    spread = block.shape[:axis] + (count,) + block.shape[axis:]
    copies = jnp.broadcast_to(jnp.expand_dims(block, axis), spread)
    arrived = lax.all_to_all(copies, BATCH, axis, axis, tiled=False)
    return arrived.reshape(block.shape[:axis] + (count * block.shape[axis],) + block.shape[axis + 1 :])


def flash_step(query_ref, key_ref, value_ref, out_ref, peak_ref, total_ref, summed_ref):
    block = pl.program_id(1)

    @pl.when(block == 0)
    def _():
        peak_ref[...] = jnp.full(peak_ref.shape, -jnp.inf, jnp.float32)
        total_ref[...] = jnp.zeros(total_ref.shape, jnp.float32)
        summed_ref[...] = jnp.zeros(summed_ref.shape, jnp.float32)

    query = query_ref[0]
    pieces = [
        jnp.dot(query, key_ref[0, part, 0], preferred_element_type=jnp.float32)
        for part in range(key_ref.shape[1])
    ]
    old_peak = peak_ref[...]
    new_peak = old_peak
    for scores in pieces:
        new_peak = jnp.maximum(new_peak, jnp.max(scores, axis=1, keepdims=True))
    rescale = jnp.exp(old_peak - new_peak)
    total = total_ref[...] * rescale
    summed = summed_ref[...] * rescale
    for part, scores in enumerate(pieces):
        weights = jnp.exp(scores - new_peak)
        total = total + jnp.sum(weights, axis=1, keepdims=True)
        summed = summed + lax.dot_general(
            weights.astype(jnp.bfloat16),
            value_ref[0, part, 0],
            (((1,), (1,)), ((), ())),
            preferred_element_type=jnp.float32,
        )
    total_ref[...] = total
    summed_ref[...] = summed
    peak_ref[...] = new_peak

    @pl.when(block == pl.num_programs(1) - 1)
    def _():
        finished = (summed_ref[...] / total_ref[...]).astype(out_ref.dtype)
        out_ref[:, 0] = finished.reshape(out_ref.shape[0], out_ref.shape[2], out_ref.shape[3])


def flash_attention(queries, kv_tile, peers, sources_per_step=8):
    sample_count, query_count, head_width = queries.shape
    _, source_count, _, _, source_rows = kv_tile.shape
    sources_per_step = math.gcd(source_count, sources_per_step)
    return pl.pallas_call(
        flash_step,
        grid=(sample_count, source_count // sources_per_step),
        in_specs=[
            pl.BlockSpec((1, query_count, head_width), lambda s, k: (s, 0, 0)),
            pl.BlockSpec(
                (1, sources_per_step, 1, head_width, source_rows), lambda s, k: (0, k, s, 0, 0)
            ),
            pl.BlockSpec(
                (1, sources_per_step, 1, head_width, source_rows), lambda s, k: (1, k, s, 0, 0)
            ),
        ],
        out_specs=pl.BlockSpec(
            (peers, 1, query_count // peers, head_width), lambda s, k: (0, s, 0, 0)
        ),
        out_shape=jax.ShapeDtypeStruct(
            (peers, sample_count, query_count // peers, head_width), jnp.bfloat16
        ),
        scratch_shapes=[
            pltpu.VMEM((query_count, 1), jnp.float32),
            pltpu.VMEM((query_count, 1), jnp.float32),
            pltpu.VMEM((query_count, head_width), jnp.float32),
        ],
        compiler_params=pltpu.CompilerParams(dimension_semantics=("parallel", "arbitrary")),
    )(queries, kv_tile, kv_tile)


def normalize(rows_in, gain):
    values = rows_in.astype(jnp.float32)
    scale = lax.rsqrt(jnp.mean(values * values, axis=-1, keepdims=True) + 1e-06)
    return values * scale * gain


def shards(
    activations,
    conv_gain,
    conv_weight,
    attention_gain,
    query_weight,
    key_weight,
    value_weight,
    output_weight,
):
    sample_count, own_rows, full_width = activations.shape
    tap_count, local_out, _ = conv_weight.shape
    flank_rows = tap_count // 2
    mine = lax.axis_index("core")
    half_width = full_width // 2
    own_half = lax.all_gather(
        lax.dynamic_slice_in_dim(output_weight, mine * half_width, half_width, 1),
        BATCH,
        axis=0,
        tiled=True,
    )
    gathered_in = gather_batch(activations, 1)
    seq_rows = gathered_in.shape[1]
    active = lax.optimization_barrier(
        jax.nn.gelu(normalize(gathered_in, conv_gain)).astype(jnp.bfloat16)
    )
    framed = with_halo(active, ((SEQ, 1),), flank_rows)
    conv_sum = jnp.zeros((sample_count, local_out, seq_rows), jnp.float32)
    for offset in range(tap_count):
        conv_sum = conv_sum + jnp.einsum(
            "std,ed->set",
            framed[:, offset : offset + seq_rows],
            conv_weight[offset],
            preferred_element_type=jnp.float32,
        )
    column_start = lax.axis_index(BATCH) * local_out
    own_columns = lax.dynamic_slice_in_dim(gathered_in, column_start, local_out, 2)
    residual = jnp.transpose(own_columns, (0, 2, 1)).astype(jnp.float32)
    hidden_part = (residual + conv_sum).astype(jnp.bfloat16)
    hidden_full, own_half = lax.optimization_barrier((gather_batch(hidden_part, 1), own_half))
    hidden_float = hidden_full.astype(jnp.float32)
    norm_scale = lax.rsqrt(jnp.mean(hidden_float * hidden_float, axis=1, keepdims=True) + 1e-06)
    normed = (hidden_float * norm_scale * attention_gain[None, :, None]).astype(jnp.bfloat16)
    queries = (
        jnp.einsum("sdt,ed->ste", normed, query_weight, preferred_element_type=jnp.float32)
        * HD ** (-0.5)
    ).astype(jnp.bfloat16)
    key_rows = jnp.einsum(
        "sdt,ed->set", normed, key_weight, preferred_element_type=jnp.float32
    ).astype(jnp.bfloat16)
    value_rows = jnp.einsum(
        "sdt,ed->set", normed, value_weight, preferred_element_type=jnp.float32
    ).astype(jnp.bfloat16)
    kv_rows = jnp.stack([key_rows, value_rows])
    kv_tile = lax.all_gather(kv_rows, SEQ, axis=1)
    batch_count = lax.axis_size(BATCH)
    attended = flash_attention(queries, kv_tile, batch_count)
    row_start = lax.axis_index(BATCH) * own_rows
    own_hidden = jnp.transpose(
        lax.dynamic_slice_in_dim(hidden_full, row_start, own_rows, 2), (0, 2, 1)
    ).astype(jnp.float32)
    head_width = attended.shape[3]
    arrived = lax.all_to_all(attended, BATCH, 0, 0, tiled=False)
    other_half = lax.ppermute(own_half, "core", [(0, 1), (1, 0)])
    full_output_weight = jnp.where(
        mine == 0,
        jnp.concatenate([own_half, other_half], axis=1),
        jnp.concatenate([other_half, own_half], axis=1),
    )
    branch_rows = jnp.einsum(
        "hstd,hdf->stf",
        arrived,
        full_output_weight.reshape(batch_count, head_width, -1),
        preferred_element_type=jnp.float32,
    )
    result = own_hidden + branch_rows
    return result.astype(jnp.bfloat16)


def solution(mesh):
    fine = jax.sharding.Mesh(
        mesh.devices.reshape(2, mesh.shape["seq"] // 4, 2, mesh.shape["batch"] // 2, 2),
        SEQ + BATCH,
    )
    placed = (
        P(None, SEQ + BATCH, None),
        P(),
        P(None, BATCH, None),
        P(),
        P(BATCH, None),
        P(BATCH, None),
        P(BATCH, None),
        P(BATCH, None),
    )
    return jax.shard_map(
        shards,
        mesh=fine,
        in_specs=placed,
        out_specs=P(None, SEQ + BATCH, None),
        check_vma=False,
    )
```

```python
import math

import jax
import jax.numpy as jnp
from jax import lax
from jax.experimental import pallas as pl
from jax.experimental.pallas import tpu as pltpu
from jax.sharding import PartitionSpec as P

HD = 192
SEQ = ("chip_x", "chip_z", "core")
BATCH = ("peer_y", "peer_x")


def with_halo(cells, sides, width):
    for axis, dim in sides:
        count = lax.axis_size(axis)
        ends = count - 1
        head = lax.slice_in_dim(cells, 0, width, axis=dim)
        tail = lax.slice_in_dim(cells, cells.shape[dim] - width, cells.shape[dim], axis=dim)
        cells = jnp.concatenate(
            [
                lax.ppermute(tail, axis, [(i, (i + 1) % count) for i in range(ends)]),
                cells,
                lax.ppermute(head, axis, [((i + 1) % count, i) for i in range(ends)]),
            ],
            axis=dim,
        )
    return cells


def gather_batch(block, axis):
    count = lax.axis_size(BATCH)
    spread = block.shape[:axis] + (count,) + block.shape[axis:]
    copies = jnp.broadcast_to(jnp.expand_dims(block, axis), spread)
    arrived = lax.all_to_all(copies, BATCH, axis, axis, tiled=False)
    return arrived.reshape(block.shape[:axis] + (count * block.shape[axis],) + block.shape[axis + 1 :])


def flash_step(query_ref, key_ref, value_ref, out_ref, peak_ref, total_ref, summed_ref):
    block = pl.program_id(1)

    @pl.when(block == 0)
    def _():
        peak_ref[...] = jnp.full(peak_ref.shape, -jnp.inf, jnp.float32)
        total_ref[...] = jnp.zeros(total_ref.shape, jnp.float32)
        summed_ref[...] = jnp.zeros(summed_ref.shape, jnp.float32)

    query = query_ref[0]
    pieces = [
        jnp.dot(query, key_ref[0, part, 0], preferred_element_type=jnp.float32)
        for part in range(key_ref.shape[1])
    ]
    old_peak = peak_ref[...]
    new_peak = old_peak
    for scores in pieces:
        new_peak = jnp.maximum(new_peak, jnp.max(scores, axis=1, keepdims=True))
    rescale = jnp.exp(old_peak - new_peak)
    total = total_ref[...] * rescale
    summed = summed_ref[...] * rescale
    for part, scores in enumerate(pieces):
        weights = jnp.exp(scores - new_peak)
        total = total + jnp.sum(weights, axis=1, keepdims=True)
        summed = summed + lax.dot_general(
            weights.astype(jnp.bfloat16),
            value_ref[0, part, 0],
            (((1,), (1,)), ((), ())),
            preferred_element_type=jnp.float32,
        )
    total_ref[...] = total
    summed_ref[...] = summed
    peak_ref[...] = new_peak

    @pl.when(block == pl.num_programs(1) - 1)
    def _():
        finished = (summed_ref[...] / total_ref[...]).astype(out_ref.dtype)
        out_ref[:, 0] = finished.reshape(out_ref.shape[0], out_ref.shape[2], out_ref.shape[3])


def flash_attention(queries, kv_tile, peers, sources_per_step=8):
    sample_count, query_count, head_width = queries.shape
    _, source_count, _, _, source_rows = kv_tile.shape
    sources_per_step = math.gcd(source_count, sources_per_step)
    return pl.pallas_call(
        flash_step,
        grid=(sample_count, source_count // sources_per_step),
        in_specs=[
            pl.BlockSpec((1, query_count, head_width), lambda s, k: (s, 0, 0)),
            pl.BlockSpec(
                (1, sources_per_step, 1, head_width, source_rows), lambda s, k: (0, k, s, 0, 0)
            ),
            pl.BlockSpec(
                (1, sources_per_step, 1, head_width, source_rows), lambda s, k: (1, k, s, 0, 0)
            ),
        ],
        out_specs=pl.BlockSpec(
            (peers, 1, query_count // peers, head_width), lambda s, k: (0, s, 0, 0)
        ),
        out_shape=jax.ShapeDtypeStruct(
            (peers, sample_count, query_count // peers, head_width), jnp.bfloat16
        ),
        scratch_shapes=[
            pltpu.VMEM((query_count, 1), jnp.float32),
            pltpu.VMEM((query_count, 1), jnp.float32),
            pltpu.VMEM((query_count, head_width), jnp.float32),
        ],
        compiler_params=pltpu.CompilerParams(dimension_semantics=("parallel", "arbitrary")),
    )(queries, kv_tile, kv_tile)


def normalize(rows_in, gain):
    values = rows_in.astype(jnp.float32)
    scale = lax.rsqrt(jnp.mean(values * values, axis=-1, keepdims=True) + 1e-06)
    return values * scale * gain


def shards(
    activations,
    conv_gain,
    conv_weight,
    attention_gain,
    query_weight,
    key_weight,
    value_weight,
    output_weight,
):
    sample_count, own_rows, full_width = activations.shape
    tap_count, local_out, _ = conv_weight.shape
    flank_rows = tap_count // 2
    mine = lax.axis_index("core")
    half_width = full_width // 2
    own_half = lax.all_gather(
        lax.dynamic_slice_in_dim(output_weight, mine * half_width, half_width, 1),
        BATCH,
        axis=0,
        tiled=True,
    )
    gathered_in = gather_batch(activations, 1)
    seq_rows = gathered_in.shape[1]
    active = lax.optimization_barrier(
        jax.nn.gelu(normalize(gathered_in, conv_gain)).astype(jnp.bfloat16)
    )
    framed = with_halo(active, ((SEQ, 1),), flank_rows)
    conv_sum = jnp.zeros((sample_count, local_out, seq_rows), jnp.float32)
    for offset in range(tap_count):
        conv_sum = conv_sum + jnp.einsum(
            "std,ed->set",
            framed[:, offset : offset + seq_rows],
            conv_weight[offset],
            preferred_element_type=jnp.float32,
        )
    column_start = lax.axis_index(BATCH) * local_out
    own_columns = lax.dynamic_slice_in_dim(gathered_in, column_start, local_out, 2)
    residual = jnp.transpose(own_columns, (0, 2, 1)).astype(jnp.float32)
    hidden_part = (residual + conv_sum).astype(jnp.bfloat16)
    hidden_full, own_half = lax.optimization_barrier((gather_batch(hidden_part, 1), own_half))
    hidden_float = hidden_full.astype(jnp.float32)
    norm_scale = lax.rsqrt(jnp.mean(hidden_float * hidden_float, axis=1, keepdims=True) + 1e-06)
    normed = (hidden_float * norm_scale * attention_gain[None, :, None]).astype(jnp.bfloat16)
    queries = (
        jnp.einsum("sdt,ed->ste", normed, query_weight, preferred_element_type=jnp.float32)
        * HD ** (-0.5)
    ).astype(jnp.bfloat16)
    key_rows = jnp.einsum(
        "sdt,ed->set", normed, key_weight, preferred_element_type=jnp.float32
    ).astype(jnp.bfloat16)
    value_rows = jnp.einsum(
        "sdt,ed->set", normed, value_weight, preferred_element_type=jnp.float32
    ).astype(jnp.bfloat16)
    kv_rows = jnp.stack([key_rows, value_rows])
    kv_tile = lax.all_gather(kv_rows, SEQ, axis=1)
    batch_count = lax.axis_size(BATCH)
    attended = flash_attention(queries, kv_tile, batch_count)
    row_start = lax.axis_index(BATCH) * own_rows
    own_hidden = jnp.transpose(
        lax.dynamic_slice_in_dim(hidden_full, row_start, own_rows, 2), (0, 2, 1)
    ).astype(jnp.float32)
    head_width = attended.shape[3]
    peer = lax.axis_index(BATCH)
    by_shift = [lax.dynamic_index_in_dim(attended, peer, 0, keepdims=False)]
    for shift in range(1, batch_count):
        by_shift.append(
            lax.ppermute(
                lax.dynamic_index_in_dim(attended, (peer + shift) % batch_count, 0, keepdims=False),
                BATCH,
                [(index, (index + shift) % batch_count) for index in range(batch_count)],
            )
        )
    arrived = jnp.take(
        jnp.stack(by_shift), (peer - jnp.arange(batch_count)) % batch_count, axis=0
    )
    other_half = lax.ppermute(own_half, "core", [(0, 1), (1, 0)])
    own_part = jnp.einsum(
        "hstd,hdf->stf",
        arrived,
        own_half.reshape(batch_count, head_width, -1),
        preferred_element_type=jnp.float32,
    )
    other_part = jnp.einsum(
        "hstd,hdf->stf",
        arrived,
        other_half.reshape(batch_count, head_width, -1),
        preferred_element_type=jnp.float32,
    )
    branch_rows = jnp.where(
        mine == 0,
        jnp.concatenate([own_part, other_part], axis=2),
        jnp.concatenate([other_part, own_part], axis=2),
    )
    result = own_hidden + branch_rows
    return result.astype(jnp.bfloat16)


def solution(mesh):
    fine = jax.sharding.Mesh(
        mesh.devices.reshape(2, mesh.shape["seq"] // 4, 2, mesh.shape["batch"] // 2, 2),
        SEQ + BATCH,
    )
    placed = (
        P(None, SEQ + BATCH, None),
        P(),
        P(None, BATCH, None),
        P(),
        P(BATCH, None),
        P(BATCH, None),
        P(BATCH, None),
        P(BATCH, None),
    )
    return jax.shard_map(
        shards,
        mesh=fine,
        in_specs=placed,
        out_specs=P(None, SEQ + BATCH, None),
        check_vma=False,
    )
```

```python
import math

import jax
import jax.numpy as jnp
from jax import lax
from jax.experimental import pallas as pl
from jax.experimental.pallas import tpu as pltpu
from jax.sharding import PartitionSpec as P

HD = 192
SEQ = ("chip_x", "chip_z", "core")
BATCH = ("peer_y", "peer_x")


def with_halo(cells, sides, width):
    for axis, dim in sides:
        count = lax.axis_size(axis)
        ends = count - 1
        head = lax.slice_in_dim(cells, 0, width, axis=dim)
        tail = lax.slice_in_dim(cells, cells.shape[dim] - width, cells.shape[dim], axis=dim)
        cells = jnp.concatenate(
            [
                lax.ppermute(tail, axis, [(i, (i + 1) % count) for i in range(ends)]),
                cells,
                lax.ppermute(head, axis, [((i + 1) % count, i) for i in range(ends)]),
            ],
            axis=dim,
        )
    return cells


def gather_batch(block, axis):
    count = lax.axis_size(BATCH)
    spread = block.shape[:axis] + (count,) + block.shape[axis:]
    copies = jnp.broadcast_to(jnp.expand_dims(block, axis), spread)
    arrived = lax.all_to_all(copies, BATCH, axis, axis, tiled=False)
    return arrived.reshape(block.shape[:axis] + (count * block.shape[axis],) + block.shape[axis + 1 :])


def flash_step(query_ref, key_ref, value_ref, out_ref, peak_ref, total_ref, summed_ref):
    block = pl.program_id(2)

    @pl.when(block == 0)
    def _():
        peak_ref[...] = jnp.full(peak_ref.shape, -jnp.inf, jnp.float32)
        total_ref[...] = jnp.zeros(total_ref.shape, jnp.float32)
        summed_ref[...] = jnp.zeros(summed_ref.shape, jnp.float32)

    query = query_ref[0]
    pieces = [
        jnp.dot(query, key_ref[0, part, 0], preferred_element_type=jnp.float32)
        for part in range(key_ref.shape[1])
    ]
    old_peak = peak_ref[...]
    new_peak = old_peak
    for scores in pieces:
        new_peak = jnp.maximum(new_peak, jnp.max(scores, axis=1, keepdims=True))
    rescale = jnp.exp(old_peak - new_peak)
    total = total_ref[...] * rescale
    summed = summed_ref[...] * rescale
    for part, scores in enumerate(pieces):
        weights = jnp.exp(scores - new_peak)
        total = total + jnp.sum(weights, axis=1, keepdims=True)
        summed = summed + lax.dot_general(
            weights.astype(jnp.bfloat16),
            value_ref[0, part, 0],
            (((1,), (1,)), ((), ())),
            preferred_element_type=jnp.float32,
        )
    total_ref[...] = total
    summed_ref[...] = summed
    peak_ref[...] = new_peak

    @pl.when(block == pl.num_programs(2) - 1)
    def _():
        finished = (summed_ref[...] / total_ref[...]).astype(out_ref.dtype)
        out_ref[:, 0] = finished.reshape(out_ref.shape[0], out_ref.shape[2], out_ref.shape[3])


def flash_attention(queries, kv_tile, peers, sources_per_step=16, query_splits=2):
    sample_count, query_count, head_width = queries.shape
    _, source_count, _, _, source_rows = kv_tile.shape
    sources_per_step = math.gcd(source_count, sources_per_step)
    query_splits = math.gcd(peers, query_splits)
    query_block = query_count // query_splits
    peer_block = peers // query_splits
    return pl.pallas_call(
        flash_step,
        grid=(sample_count, query_splits, source_count // sources_per_step),
        in_specs=[
            pl.BlockSpec((1, query_block, head_width), lambda s, q, k: (s, q, 0)),
            pl.BlockSpec(
                (1, sources_per_step, 1, head_width, source_rows),
                lambda s, q, k: (0, k, s, 0, 0),
            ),
            pl.BlockSpec(
                (1, sources_per_step, 1, head_width, source_rows),
                lambda s, q, k: (1, k, s, 0, 0),
            ),
        ],
        out_specs=pl.BlockSpec(
            (peer_block, 1, query_count // peers, head_width), lambda s, q, k: (q, s, 0, 0)
        ),
        out_shape=jax.ShapeDtypeStruct(
            (peers, sample_count, query_count // peers, head_width), jnp.bfloat16
        ),
        scratch_shapes=[
            pltpu.VMEM((query_block, 1), jnp.float32),
            pltpu.VMEM((query_block, 1), jnp.float32),
            pltpu.VMEM((query_block, head_width), jnp.float32),
        ],
        compiler_params=pltpu.CompilerParams(
            dimension_semantics=("parallel", "parallel", "arbitrary")
        ),
    )(queries, kv_tile, kv_tile)


def normalize(rows_in, gain):
    values = rows_in.astype(jnp.float32)
    scale = lax.rsqrt(jnp.mean(values * values, axis=-1, keepdims=True) + 1e-06)
    return values * scale * gain


def shards(
    activations,
    conv_gain,
    conv_weight,
    attention_gain,
    query_weight,
    key_weight,
    value_weight,
    output_weight,
):
    sample_count, own_rows, full_width = activations.shape
    tap_count, local_out, _ = conv_weight.shape
    flank_rows = tap_count // 2
    mine = lax.axis_index("core")
    half_width = full_width // 2
    own_half = lax.all_gather(
        lax.dynamic_slice_in_dim(output_weight, mine * half_width, half_width, 1),
        BATCH,
        axis=0,
        tiled=True,
    )
    gathered_in = gather_batch(activations, 1)
    seq_rows = gathered_in.shape[1]
    active = lax.optimization_barrier(
        jax.nn.gelu(normalize(gathered_in, conv_gain)).astype(jnp.bfloat16)
    )
    framed = with_halo(active, ((SEQ, 1),), flank_rows)
    conv_sum = jnp.zeros((sample_count, local_out, seq_rows), jnp.float32)
    for offset in range(tap_count):
        conv_sum = conv_sum + jnp.einsum(
            "std,ed->set",
            framed[:, offset : offset + seq_rows],
            conv_weight[offset],
            preferred_element_type=jnp.float32,
        )
    column_start = lax.axis_index(BATCH) * local_out
    own_columns = lax.dynamic_slice_in_dim(gathered_in, column_start, local_out, 2)
    residual = jnp.transpose(own_columns, (0, 2, 1)).astype(jnp.float32)
    hidden_part = (residual + conv_sum).astype(jnp.bfloat16)
    hidden_full, own_half = lax.optimization_barrier((gather_batch(hidden_part, 1), own_half))
    hidden_float = hidden_full.astype(jnp.float32)
    norm_scale = lax.rsqrt(jnp.mean(hidden_float * hidden_float, axis=1, keepdims=True) + 1e-06)
    normed = (hidden_float * norm_scale * attention_gain[None, :, None]).astype(jnp.bfloat16)
    queries = (
        jnp.einsum("sdt,ed->ste", normed, query_weight, preferred_element_type=jnp.float32)
        * HD ** (-0.5)
    ).astype(jnp.bfloat16)
    key_rows = jnp.einsum(
        "sdt,ed->set", normed, key_weight, preferred_element_type=jnp.float32
    ).astype(jnp.bfloat16)
    value_rows = jnp.einsum(
        "sdt,ed->set", normed, value_weight, preferred_element_type=jnp.float32
    ).astype(jnp.bfloat16)
    kv_rows = jnp.stack([key_rows, value_rows])
    kv_tile = lax.all_gather(kv_rows, SEQ, axis=1)
    batch_count = lax.axis_size(BATCH)
    attended = flash_attention(queries, kv_tile, batch_count)
    row_start = lax.axis_index(BATCH) * own_rows
    own_hidden = jnp.transpose(
        lax.dynamic_slice_in_dim(hidden_full, row_start, own_rows, 2), (0, 2, 1)
    ).astype(jnp.float32)
    head_width = attended.shape[3]
    arrived = lax.all_to_all(attended, BATCH, 0, 0, tiled=False)
    other_half = lax.ppermute(own_half, "core", [(0, 1), (1, 0)])
    own_part = jnp.einsum(
        "hstd,hdf->stf",
        arrived,
        own_half.reshape(batch_count, head_width, -1),
        preferred_element_type=jnp.float32,
    )
    other_part = jnp.einsum(
        "hstd,hdf->stf",
        arrived,
        other_half.reshape(batch_count, head_width, -1),
        preferred_element_type=jnp.float32,
    )
    branch_rows = jnp.where(
        mine == 0,
        jnp.concatenate([own_part, other_part], axis=2),
        jnp.concatenate([other_part, own_part], axis=2),
    )
    result = own_hidden + branch_rows
    return result.astype(jnp.bfloat16)


def solution(mesh):
    fine = jax.sharding.Mesh(
        mesh.devices.reshape(2, mesh.shape["seq"] // 4, 2, mesh.shape["batch"] // 2, 2),
        SEQ + BATCH,
    )
    placed = (
        P(None, SEQ + BATCH, None),
        P(),
        P(None, BATCH, None),
        P(),
        P(BATCH, None),
        P(BATCH, None),
        P(BATCH, None),
        P(BATCH, None),
    )
    return jax.shard_map(
        shards,
        mesh=fine,
        in_specs=placed,
        out_specs=P(None, SEQ + BATCH, None),
        check_vma=False,
    )
```

```python
import math

import jax
import jax.numpy as jnp
from jax import lax
from jax.experimental import pallas as pl
from jax.experimental.pallas import tpu as pltpu
from jax.sharding import PartitionSpec as P

HD = 192
SEQ = ("chip_x", "chip_z", "core")
BATCH = ("peer_y", "peer_x")


def with_halo(cells, raw, activate, axis, width):
    count = lax.axis_size(axis)
    ends = count - 1
    head = raw[:, :width]
    tail = raw[:, raw.shape[1] - width :]
    before = lax.ppermute(tail, axis, [(i, (i + 1) % count) for i in range(ends)])
    after = lax.ppermute(head, axis, [((i + 1) % count, i) for i in range(ends)])
    return jnp.concatenate([activate(before), cells, activate(after)], axis=1)


def gather_batch(block, axis):
    count = lax.axis_size(BATCH)
    spread = block.shape[:axis] + (count,) + block.shape[axis:]
    copies = jnp.broadcast_to(jnp.expand_dims(block, axis), spread)
    arrived = lax.all_to_all(copies, BATCH, axis, axis, tiled=False)
    return arrived.reshape(block.shape[:axis] + (count * block.shape[axis],) + block.shape[axis + 1 :])


def flash_step(query_ref, key_ref, value_ref, out_ref, peak_ref, total_ref, summed_ref):
    block = pl.program_id(1)

    @pl.when(block == 0)
    def _():
        peak_ref[...] = jnp.full(peak_ref.shape, -jnp.inf, jnp.float32)
        total_ref[...] = jnp.zeros(total_ref.shape, jnp.float32)
        summed_ref[...] = jnp.zeros(summed_ref.shape, jnp.float32)

    query = query_ref[0]
    pieces = [
        jnp.dot(query, key_ref[0, part, 0], preferred_element_type=jnp.float32)
        for part in range(key_ref.shape[1])
    ]
    old_peak = peak_ref[...]
    new_peak = old_peak
    for scores in pieces:
        new_peak = jnp.maximum(new_peak, jnp.max(scores, axis=1, keepdims=True))
    rescale = jnp.exp(old_peak - new_peak)
    total = total_ref[...] * rescale
    summed = summed_ref[...] * rescale
    for part, scores in enumerate(pieces):
        weights = jnp.exp(scores - new_peak)
        total = total + jnp.sum(weights, axis=1, keepdims=True)
        summed = summed + lax.dot_general(
            weights.astype(jnp.bfloat16),
            value_ref[0, part, 0],
            (((1,), (1,)), ((), ())),
            preferred_element_type=jnp.float32,
        )
    total_ref[...] = total
    summed_ref[...] = summed
    peak_ref[...] = new_peak

    @pl.when(block == pl.num_programs(1) - 1)
    def _():
        finished = (summed_ref[...] / total_ref[...]).astype(out_ref.dtype)
        out_ref[:, 0] = finished.reshape(out_ref.shape[0], out_ref.shape[2], out_ref.shape[3])


def flash_attention(queries, kv_tile, peers, sources_per_step=8):
    sample_count, query_count, head_width = queries.shape
    _, source_count, _, _, source_rows = kv_tile.shape
    sources_per_step = math.gcd(source_count, sources_per_step)
    return pl.pallas_call(
        flash_step,
        grid=(sample_count, source_count // sources_per_step),
        in_specs=[
            pl.BlockSpec((1, query_count, head_width), lambda s, k: (s, 0, 0)),
            pl.BlockSpec(
                (1, sources_per_step, 1, head_width, source_rows), lambda s, k: (0, k, s, 0, 0)
            ),
            pl.BlockSpec(
                (1, sources_per_step, 1, head_width, source_rows), lambda s, k: (1, k, s, 0, 0)
            ),
        ],
        out_specs=pl.BlockSpec(
            (peers, 1, query_count // peers, head_width), lambda s, k: (0, s, 0, 0)
        ),
        out_shape=jax.ShapeDtypeStruct(
            (peers, sample_count, query_count // peers, head_width), jnp.bfloat16
        ),
        scratch_shapes=[
            pltpu.VMEM((query_count, 1), jnp.float32),
            pltpu.VMEM((query_count, 1), jnp.float32),
            pltpu.VMEM((query_count, head_width), jnp.float32),
        ],
        compiler_params=pltpu.CompilerParams(dimension_semantics=("parallel", "arbitrary")),
    )(queries, kv_tile, kv_tile)


def normalize(rows_in, gain):
    values = rows_in.astype(jnp.float32)
    scale = lax.rsqrt(jnp.mean(values * values, axis=-1, keepdims=True) + 1e-06)
    return values * scale * gain


def shards(
    activations,
    conv_gain,
    conv_weight,
    attention_gain,
    query_weight,
    key_weight,
    value_weight,
    output_weight,
):
    sample_count, own_rows, full_width = activations.shape
    tap_count, local_out, _ = conv_weight.shape
    flank_rows = tap_count // 2
    mine = lax.axis_index("core")
    half_width = full_width // 2
    own_half = lax.all_gather(
        lax.dynamic_slice_in_dim(output_weight, mine * half_width, half_width, 1),
        BATCH,
        axis=0,
        tiled=True,
    )
    gathered_in = gather_batch(activations, 1)
    seq_rows = gathered_in.shape[1]
    def activate(rows_in):
        return jax.nn.gelu(normalize(rows_in, conv_gain)).astype(jnp.bfloat16)

    active = lax.optimization_barrier(activate(gathered_in))
    framed = with_halo(active, gathered_in, activate, SEQ, flank_rows)
    conv_sum = jnp.zeros((sample_count, local_out, seq_rows), jnp.float32)
    for offset in range(tap_count):
        conv_sum = conv_sum + jnp.einsum(
            "std,ed->set",
            framed[:, offset : offset + seq_rows],
            conv_weight[offset],
            preferred_element_type=jnp.float32,
        )
    column_start = lax.axis_index(BATCH) * local_out
    own_columns = lax.dynamic_slice_in_dim(gathered_in, column_start, local_out, 2)
    residual = jnp.transpose(own_columns, (0, 2, 1)).astype(jnp.float32)
    hidden_part = (residual + conv_sum).astype(jnp.bfloat16)
    hidden_full, own_half = lax.optimization_barrier((gather_batch(hidden_part, 1), own_half))
    hidden_float = hidden_full.astype(jnp.float32)
    norm_scale = lax.rsqrt(jnp.mean(hidden_float * hidden_float, axis=1, keepdims=True) + 1e-06)
    normed = (hidden_float * norm_scale * attention_gain[None, :, None]).astype(jnp.bfloat16)
    queries = (
        jnp.einsum("sdt,ed->ste", normed, query_weight, preferred_element_type=jnp.float32)
        * HD ** (-0.5)
    ).astype(jnp.bfloat16)
    key_rows = jnp.einsum(
        "sdt,ed->set", normed, key_weight, preferred_element_type=jnp.float32
    ).astype(jnp.bfloat16)
    value_rows = jnp.einsum(
        "sdt,ed->set", normed, value_weight, preferred_element_type=jnp.float32
    ).astype(jnp.bfloat16)
    kv_rows = jnp.stack([key_rows, value_rows])
    kv_tile = lax.all_gather(kv_rows, SEQ, axis=1)
    batch_count = lax.axis_size(BATCH)
    attended = flash_attention(queries, kv_tile, batch_count)
    row_start = lax.axis_index(BATCH) * own_rows
    own_hidden = jnp.transpose(
        lax.dynamic_slice_in_dim(hidden_full, row_start, own_rows, 2), (0, 2, 1)
    ).astype(jnp.float32)
    head_width = attended.shape[3]
    arrived = lax.all_to_all(attended, BATCH, 0, 0, tiled=False)
    other_half = lax.ppermute(own_half, "core", [(0, 1), (1, 0)])
    full_output_weight = jnp.where(
        mine == 0,
        jnp.concatenate([own_half, other_half], axis=1),
        jnp.concatenate([other_half, own_half], axis=1),
    )
    branch_rows = jnp.einsum(
        "hstd,hdf->stf",
        arrived,
        full_output_weight.reshape(batch_count, head_width, -1),
        preferred_element_type=jnp.float32,
    )
    result = own_hidden + branch_rows
    return result.astype(jnp.bfloat16)


def solution(mesh):
    fine = jax.sharding.Mesh(
        mesh.devices.reshape(2, mesh.shape["seq"] // 4, 2, mesh.shape["batch"] // 2, 2),
        SEQ + BATCH,
    )
    placed = (
        P(None, SEQ + BATCH, None),
        P(),
        P(None, BATCH, None),
        P(),
        P(BATCH, None),
        P(BATCH, None),
        P(BATCH, None),
        P(BATCH, None),
    )
    return jax.shard_map(
        shards,
        mesh=fine,
        in_specs=placed,
        out_specs=P(None, SEQ + BATCH, None),
        check_vma=False,
    )
```

```python
import math

import jax
import jax.numpy as jnp
from jax import lax
from jax.experimental import pallas as pl
from jax.experimental.pallas import tpu as pltpu
from jax.sharding import PartitionSpec as P

HD = 192
SEQ = ("chip_x", "chip_z", "core")
BATCH = ("peer_y", "peer_x")


def with_halo(cells, sides, width):
    for axis, dim in sides:
        count = lax.axis_size(axis)
        ends = count - 1
        head = lax.slice_in_dim(cells, 0, width, axis=dim)
        tail = lax.slice_in_dim(cells, cells.shape[dim] - width, cells.shape[dim], axis=dim)
        cells = jnp.concatenate(
            [
                lax.ppermute(tail, axis, [(i, (i + 1) % count) for i in range(ends)]),
                cells,
                lax.ppermute(head, axis, [((i + 1) % count, i) for i in range(ends)]),
            ],
            axis=dim,
        )
    return cells


def gather_batch(block, axis):
    count = lax.axis_size(BATCH)
    spread = block.shape[:axis] + (count,) + block.shape[axis:]
    copies = jnp.broadcast_to(jnp.expand_dims(block, axis), spread)
    arrived = lax.all_to_all(copies, BATCH, axis, axis, tiled=False)
    return arrived.reshape(block.shape[:axis] + (count * block.shape[axis],) + block.shape[axis + 1 :])


def flash_step(query_ref, key_ref, value_ref, out_ref, peak_ref, total_ref, summed_ref):
    block = pl.program_id(1)

    @pl.when(block == 0)
    def _():
        peak_ref[...] = jnp.full(peak_ref.shape, -jnp.inf, jnp.float32)
        total_ref[...] = jnp.zeros(total_ref.shape, jnp.float32)
        summed_ref[...] = jnp.zeros(summed_ref.shape, jnp.float32)

    query = query_ref[0]
    pieces = [
        jnp.dot(query, key_ref[0, part, 0], preferred_element_type=jnp.float32)
        for part in range(key_ref.shape[1])
    ]
    old_peak = peak_ref[...]
    new_peak = old_peak
    for scores in pieces:
        new_peak = jnp.maximum(new_peak, jnp.max(scores, axis=1, keepdims=True))
    rescale = jnp.exp(old_peak - new_peak)
    total = total_ref[...] * rescale
    summed = summed_ref[...] * rescale
    for part, scores in enumerate(pieces):
        weights = jnp.exp(scores - new_peak)
        total = total + jnp.sum(weights, axis=1, keepdims=True)
        summed = summed + lax.dot_general(
            weights.astype(jnp.bfloat16),
            value_ref[0, part, 0],
            (((1,), (1,)), ((), ())),
            preferred_element_type=jnp.float32,
        )
    total_ref[...] = total
    summed_ref[...] = summed
    peak_ref[...] = new_peak

    @pl.when(block == pl.num_programs(1) - 1)
    def _():
        finished = (summed_ref[...] / total_ref[...]).astype(out_ref.dtype)
        out_ref[:, 0] = finished.reshape(out_ref.shape[0], out_ref.shape[2], out_ref.shape[3])


def flash_attention(queries, kv_tile, peers, sources_per_step=4):
    sample_count, query_count, head_width = queries.shape
    _, source_count, _, _, source_rows = kv_tile.shape
    sources_per_step = math.gcd(source_count, sources_per_step)
    return pl.pallas_call(
        flash_step,
        grid=(sample_count, source_count // sources_per_step),
        in_specs=[
            pl.BlockSpec((1, query_count, head_width), lambda s, k: (s, 0, 0)),
            pl.BlockSpec(
                (1, sources_per_step, 1, head_width, source_rows), lambda s, k: (0, k, s, 0, 0)
            ),
            pl.BlockSpec(
                (1, sources_per_step, 1, head_width, source_rows), lambda s, k: (1, k, s, 0, 0)
            ),
        ],
        out_specs=pl.BlockSpec(
            (peers, 1, query_count // peers, head_width), lambda s, k: (0, s, 0, 0)
        ),
        out_shape=jax.ShapeDtypeStruct(
            (peers, sample_count, query_count // peers, head_width), jnp.bfloat16
        ),
        scratch_shapes=[
            pltpu.VMEM((query_count, 1), jnp.float32),
            pltpu.VMEM((query_count, 1), jnp.float32),
            pltpu.VMEM((query_count, head_width), jnp.float32),
        ],
        compiler_params=pltpu.CompilerParams(dimension_semantics=("parallel", "arbitrary")),
    )(queries, kv_tile, kv_tile)


def normalize(rows_in, gain):
    values = rows_in.astype(jnp.float32)
    scale = lax.rsqrt(jnp.mean(values * values, axis=-1, keepdims=True) + 1e-06)
    return values * scale * gain


def shards(
    activations,
    conv_gain,
    conv_weight,
    attention_gain,
    query_weight,
    key_weight,
    value_weight,
    output_weight,
):
    sample_count, own_rows, full_width = activations.shape
    tap_count, local_out, _ = conv_weight.shape
    flank_rows = tap_count // 2
    mine = lax.axis_index("core")
    half_width = full_width // 2
    own_half = lax.all_gather(
        lax.dynamic_slice_in_dim(output_weight, mine * half_width, half_width, 1),
        BATCH,
        axis=0,
        tiled=True,
    )
    gathered_in = gather_batch(activations, 1)
    seq_rows = gathered_in.shape[1]
    active = lax.optimization_barrier(
        jax.nn.gelu(normalize(gathered_in, conv_gain)).astype(jnp.bfloat16)
    )
    framed = with_halo(active, ((SEQ, 1),), flank_rows)
    conv_sum = jnp.zeros((sample_count, local_out, seq_rows), jnp.float32)
    for offset in range(tap_count):
        conv_sum = conv_sum + jnp.einsum(
            "std,ed->set",
            framed[:, offset : offset + seq_rows],
            conv_weight[offset],
            preferred_element_type=jnp.float32,
        )
    column_start = lax.axis_index(BATCH) * local_out
    own_columns = lax.dynamic_slice_in_dim(gathered_in, column_start, local_out, 2)
    residual = jnp.transpose(own_columns, (0, 2, 1)).astype(jnp.float32)
    hidden_part = (residual + conv_sum).astype(jnp.bfloat16)
    hidden_full, own_half = lax.optimization_barrier((gather_batch(hidden_part, 1), own_half))
    hidden_float = hidden_full.astype(jnp.float32)
    norm_scale = lax.rsqrt(jnp.mean(hidden_float * hidden_float, axis=1, keepdims=True) + 1e-06)
    normed = (hidden_float * norm_scale * attention_gain[None, :, None]).astype(jnp.bfloat16)
    queries = (
        jnp.einsum("sdt,ed->ste", normed, query_weight, preferred_element_type=jnp.float32)
        * HD ** (-0.5)
    ).astype(jnp.bfloat16)
    key_rows = jnp.einsum(
        "sdt,ed->set", normed, key_weight, preferred_element_type=jnp.float32
    ).astype(jnp.bfloat16)
    value_rows = jnp.einsum(
        "sdt,ed->set", normed, value_weight, preferred_element_type=jnp.float32
    ).astype(jnp.bfloat16)
    kv_rows = jnp.stack([key_rows, value_rows])
    kv_tile = lax.all_gather(kv_rows, SEQ, axis=1)
    batch_count = lax.axis_size(BATCH)
    attended = flash_attention(queries, kv_tile, batch_count)
    row_start = lax.axis_index(BATCH) * own_rows
    own_hidden = jnp.transpose(
        lax.dynamic_slice_in_dim(hidden_full, row_start, own_rows, 2), (0, 2, 1)
    ).astype(jnp.float32)
    head_width = attended.shape[3]
    arrived = lax.all_to_all(attended, BATCH, 0, 0, tiled=False)
    other_half = lax.ppermute(own_half, "core", [(0, 1), (1, 0)])
    own_part = jnp.einsum(
        "hstd,hdf->stf",
        arrived,
        own_half.reshape(batch_count, head_width, -1),
        preferred_element_type=jnp.float32,
    )
    other_part = jnp.einsum(
        "hstd,hdf->stf",
        arrived,
        other_half.reshape(batch_count, head_width, -1),
        preferred_element_type=jnp.float32,
    )
    branch_rows = jnp.where(
        mine == 0,
        jnp.concatenate([own_part, other_part], axis=2),
        jnp.concatenate([other_part, own_part], axis=2),
    )
    result = own_hidden + branch_rows
    return result.astype(jnp.bfloat16)


def solution(mesh):
    fine = jax.sharding.Mesh(
        mesh.devices.reshape(2, mesh.shape["seq"] // 4, 2, mesh.shape["batch"] // 2, 2),
        SEQ + BATCH,
    )
    placed = (
        P(None, SEQ + BATCH, None),
        P(),
        P(None, BATCH, None),
        P(),
        P(BATCH, None),
        P(BATCH, None),
        P(BATCH, None),
        P(BATCH, None),
    )
    return jax.shard_map(
        shards,
        mesh=fine,
        in_specs=placed,
        out_specs=P(None, SEQ + BATCH, None),
        check_vma=False,
    )
```

```python
import math

import jax
import jax.numpy as jnp
from jax import lax
from jax.experimental import pallas as pl
from jax.experimental.pallas import tpu as pltpu
from jax.sharding import PartitionSpec as P

HD = 192
SEQ = ("chip_x", "chip_z", "core")
BATCH = ("peer_y", "peer_x")


def with_halo(cells, sides, width):
    for axis, dim in sides:
        count = lax.axis_size(axis)
        ends = count - 1
        head = lax.slice_in_dim(cells, 0, width, axis=dim)
        tail = lax.slice_in_dim(cells, cells.shape[dim] - width, cells.shape[dim], axis=dim)
        cells = jnp.concatenate(
            [
                lax.ppermute(tail, axis, [(i, (i + 1) % count) for i in range(ends)]),
                cells,
                lax.ppermute(head, axis, [((i + 1) % count, i) for i in range(ends)]),
            ],
            axis=dim,
        )
    return cells


def gather_batch(block, axis):
    count = lax.axis_size(BATCH)
    spread = block.shape[:axis] + (count,) + block.shape[axis:]
    copies = jnp.broadcast_to(jnp.expand_dims(block, axis), spread)
    arrived = lax.all_to_all(copies, BATCH, axis, axis, tiled=False)
    return arrived.reshape(block.shape[:axis] + (count * block.shape[axis],) + block.shape[axis + 1 :])


def flash_step(query_ref, key_ref, value_ref, out_ref, peak_ref, total_ref, summed_ref):
    block = pl.program_id(1)

    @pl.when(block == 0)
    def _():
        peak_ref[...] = jnp.full(peak_ref.shape, -jnp.inf, jnp.float32)
        total_ref[...] = jnp.zeros(total_ref.shape, jnp.float32)
        summed_ref[...] = jnp.zeros(summed_ref.shape, jnp.float32)

    query = query_ref[0]
    pieces = [
        jnp.dot(query, key_ref[0, part, 0], preferred_element_type=jnp.float32)
        for part in range(key_ref.shape[1])
    ]
    old_peak = peak_ref[...]
    new_peak = old_peak
    for scores in pieces:
        new_peak = jnp.maximum(new_peak, jnp.max(scores, axis=1, keepdims=True))
    rescale = jnp.exp(old_peak - new_peak)
    total = total_ref[...] * rescale
    summed = summed_ref[...] * rescale
    for part, scores in enumerate(pieces):
        weights = jnp.exp(scores - new_peak)
        total = total + jnp.sum(weights, axis=1, keepdims=True)
        summed = summed + lax.dot_general(
            weights.astype(jnp.bfloat16),
            value_ref[0, part, 0],
            (((1,), (1,)), ((), ())),
            preferred_element_type=jnp.float32,
        )
    total_ref[...] = total
    summed_ref[...] = summed
    peak_ref[...] = new_peak

    @pl.when(block == pl.num_programs(1) - 1)
    def _():
        finished = (summed_ref[...] / total_ref[...]).astype(out_ref.dtype)
        out_ref[:, 0] = finished.reshape(out_ref.shape[0], out_ref.shape[2], out_ref.shape[3])


def flash_attention(queries, kv_tile, peers, sources_per_step=8):
    sample_count, query_count, head_width = queries.shape
    _, source_count, _, _, source_rows = kv_tile.shape
    sources_per_step = math.gcd(source_count, sources_per_step)
    return pl.pallas_call(
        flash_step,
        grid=(sample_count, source_count // sources_per_step),
        in_specs=[
            pl.BlockSpec((1, query_count, head_width), lambda s, k: (s, 0, 0)),
            pl.BlockSpec(
                (1, sources_per_step, 1, head_width, source_rows), lambda s, k: (0, k, s, 0, 0)
            ),
            pl.BlockSpec(
                (1, sources_per_step, 1, head_width, source_rows), lambda s, k: (1, k, s, 0, 0)
            ),
        ],
        out_specs=pl.BlockSpec(
            (peers, 1, query_count // peers, head_width), lambda s, k: (0, s, 0, 0)
        ),
        out_shape=jax.ShapeDtypeStruct(
            (peers, sample_count, query_count // peers, head_width), jnp.bfloat16
        ),
        scratch_shapes=[
            pltpu.VMEM((query_count, 1), jnp.float32),
            pltpu.VMEM((query_count, 1), jnp.float32),
            pltpu.VMEM((query_count, head_width), jnp.float32),
        ],
        compiler_params=pltpu.CompilerParams(dimension_semantics=("parallel", "arbitrary")),
    )(queries, kv_tile, kv_tile)


def normalize(rows_in, gain):
    values = rows_in.astype(jnp.float32)
    scale = lax.rsqrt(jnp.mean(values * values, axis=-1, keepdims=True) + 1e-06)
    return values * scale * gain


def shards(
    activations,
    conv_gain,
    conv_weight,
    attention_gain,
    query_weight,
    key_weight,
    value_weight,
    output_weight,
):
    sample_count, own_rows, full_width = activations.shape
    tap_count, local_out, _ = conv_weight.shape
    flank_rows = tap_count // 2
    mine = lax.axis_index("core")
    half_width = full_width // 2
    own_half = lax.all_gather(
        lax.dynamic_slice_in_dim(output_weight, mine * half_width, half_width, 1),
        BATCH,
        axis=0,
        tiled=True,
    )
    gathered_in = gather_batch(activations, 1)
    seq_rows = gathered_in.shape[1]
    active = lax.optimization_barrier(
        jax.nn.gelu(normalize(gathered_in, conv_gain)).astype(jnp.bfloat16)
    )
    framed = with_halo(active, ((SEQ, 1),), flank_rows)
    conv_sum = jnp.zeros((sample_count, local_out, seq_rows), jnp.float32)
    for offset in range(tap_count):
        conv_sum = conv_sum + jnp.einsum(
            "std,ed->set",
            framed[:, offset : offset + seq_rows],
            conv_weight[offset],
            preferred_element_type=jnp.float32,
        )
    column_start = lax.axis_index(BATCH) * local_out
    own_columns = lax.dynamic_slice_in_dim(gathered_in, column_start, local_out, 2)
    residual = jnp.transpose(own_columns, (0, 2, 1)).astype(jnp.float32)
    hidden_part = (residual + conv_sum).astype(jnp.bfloat16)
    hidden_full, own_half = lax.optimization_barrier((gather_batch(hidden_part, 1), own_half))
    hidden_float = hidden_full.astype(jnp.float32)
    norm_scale = lax.rsqrt(jnp.mean(hidden_float * hidden_float, axis=1, keepdims=True) + 1e-06)
    normed = (hidden_float * norm_scale * attention_gain[None, :, None]).astype(jnp.bfloat16)
    queries = (
        jnp.einsum("sdt,ed->ste", normed, query_weight, preferred_element_type=jnp.float32)
        * HD ** (-0.5)
    ).astype(jnp.bfloat16)
    kv_rows = jnp.einsum(
        "sdt,ked->kset",
        normed,
        jnp.stack([key_weight, value_weight]),
        preferred_element_type=jnp.float32,
    ).astype(jnp.bfloat16)
    kv_tile = lax.all_gather(kv_rows, SEQ, axis=1)
    batch_count = lax.axis_size(BATCH)
    attended = flash_attention(queries, kv_tile, batch_count)
    row_start = lax.axis_index(BATCH) * own_rows
    own_hidden = jnp.transpose(
        lax.dynamic_slice_in_dim(hidden_full, row_start, own_rows, 2), (0, 2, 1)
    ).astype(jnp.float32)
    head_width = attended.shape[3]
    arrived = lax.all_to_all(attended, BATCH, 0, 0, tiled=False)
    other_half = lax.ppermute(own_half, "core", [(0, 1), (1, 0)])
    own_part = jnp.einsum(
        "hstd,hdf->stf",
        arrived,
        own_half.reshape(batch_count, head_width, -1),
        preferred_element_type=jnp.float32,
    )
    other_part = jnp.einsum(
        "hstd,hdf->stf",
        arrived,
        other_half.reshape(batch_count, head_width, -1),
        preferred_element_type=jnp.float32,
    )
    branch_rows = jnp.where(
        mine == 0,
        jnp.concatenate([own_part, other_part], axis=2),
        jnp.concatenate([other_part, own_part], axis=2),
    )
    result = own_hidden + branch_rows
    return result.astype(jnp.bfloat16)


def solution(mesh):
    fine = jax.sharding.Mesh(
        mesh.devices.reshape(2, mesh.shape["seq"] // 4, 2, mesh.shape["batch"] // 2, 2),
        SEQ + BATCH,
    )
    placed = (
        P(None, SEQ + BATCH, None),
        P(),
        P(None, BATCH, None),
        P(),
        P(BATCH, None),
        P(BATCH, None),
        P(BATCH, None),
        P(BATCH, None),
    )
    return jax.shard_map(
        shards,
        mesh=fine,
        in_specs=placed,
        out_specs=P(None, SEQ + BATCH, None),
        check_vma=False,
    )
```

```python
import math

import jax
import jax.numpy as jnp
from jax import lax
from jax.experimental import pallas as pl
from jax.experimental.pallas import tpu as pltpu
from jax.sharding import PartitionSpec as P

HD = 192
SEQ = ("chip_x", "chip_z", "core")
BATCH = ("peer_y", "peer_x")


def with_halo(cells, raw, activate, axis, width):
    count = lax.axis_size(axis)
    ends = count - 1
    head = raw[:, :width]
    tail = raw[:, raw.shape[1] - width :]
    before = lax.ppermute(tail, axis, [(i, (i + 1) % count) for i in range(ends)])
    after = lax.ppermute(head, axis, [((i + 1) % count, i) for i in range(ends)])
    return jnp.concatenate([activate(before), cells, activate(after)], axis=1)


def gather_batch(block, axis):
    count = lax.axis_size(BATCH)
    spread = block.shape[:axis] + (count,) + block.shape[axis:]
    copies = jnp.broadcast_to(jnp.expand_dims(block, axis), spread)
    arrived = lax.all_to_all(copies, BATCH, axis, axis, tiled=False)
    return arrived.reshape(block.shape[:axis] + (count * block.shape[axis],) + block.shape[axis + 1 :])


def flash_step(query_ref, key_ref, value_ref, out_ref, peak_ref, total_ref, summed_ref):
    block = pl.program_id(1)

    @pl.when(block == 0)
    def _():
        peak_ref[...] = jnp.full(peak_ref.shape, -jnp.inf, jnp.float32)
        total_ref[...] = jnp.zeros(total_ref.shape, jnp.float32)
        summed_ref[...] = jnp.zeros(summed_ref.shape, jnp.float32)

    query = query_ref[0]
    pieces = [
        jnp.dot(query, key_ref[0, part, 0], preferred_element_type=jnp.float32)
        for part in range(key_ref.shape[1])
    ]
    old_peak = peak_ref[...]
    new_peak = old_peak
    for scores in pieces:
        new_peak = jnp.maximum(new_peak, jnp.max(scores, axis=1, keepdims=True))
    rescale = jnp.exp(old_peak - new_peak)
    total = total_ref[...] * rescale
    summed = summed_ref[...] * rescale
    for part, scores in enumerate(pieces):
        weights = jnp.exp(scores - new_peak)
        total = total + jnp.sum(weights, axis=1, keepdims=True)
        summed = summed + lax.dot_general(
            weights.astype(jnp.bfloat16),
            value_ref[0, part, 0],
            (((1,), (1,)), ((), ())),
            preferred_element_type=jnp.float32,
        )
    total_ref[...] = total
    summed_ref[...] = summed
    peak_ref[...] = new_peak

    @pl.when(block == pl.num_programs(1) - 1)
    def _():
        finished = (summed_ref[...] / total_ref[...]).astype(out_ref.dtype)
        out_ref[:, 0] = finished.reshape(out_ref.shape[0], out_ref.shape[2], out_ref.shape[3])


def flash_attention(queries, kv_tile, peers, sources_per_step=8):
    sample_count, query_count, head_width = queries.shape
    _, source_count, _, _, source_rows = kv_tile.shape
    sources_per_step = math.gcd(source_count, sources_per_step)
    return pl.pallas_call(
        flash_step,
        grid=(sample_count, source_count // sources_per_step),
        in_specs=[
            pl.BlockSpec((1, query_count, head_width), lambda s, k: (s, 0, 0)),
            pl.BlockSpec(
                (1, sources_per_step, 1, head_width, source_rows), lambda s, k: (0, k, s, 0, 0)
            ),
            pl.BlockSpec(
                (1, sources_per_step, 1, head_width, source_rows), lambda s, k: (1, k, s, 0, 0)
            ),
        ],
        out_specs=pl.BlockSpec(
            (peers, 1, query_count // peers, head_width), lambda s, k: (0, s, 0, 0)
        ),
        out_shape=jax.ShapeDtypeStruct(
            (peers, sample_count, query_count // peers, head_width), jnp.bfloat16
        ),
        scratch_shapes=[
            pltpu.VMEM((query_count, 1), jnp.float32),
            pltpu.VMEM((query_count, 1), jnp.float32),
            pltpu.VMEM((query_count, head_width), jnp.float32),
        ],
        compiler_params=pltpu.CompilerParams(dimension_semantics=("parallel", "arbitrary")),
    )(queries, kv_tile, kv_tile)


def normalize(rows_in, gain):
    values = rows_in.astype(jnp.float32)
    scale = lax.rsqrt(jnp.mean(values * values, axis=-1, keepdims=True) + 1e-06)
    return values * scale * gain


def shards(
    activations,
    conv_gain,
    conv_weight,
    attention_gain,
    query_weight,
    key_weight,
    value_weight,
    output_weight,
):
    sample_count, own_rows, full_width = activations.shape
    tap_count, local_out, _ = conv_weight.shape
    flank_rows = tap_count // 2
    mine = lax.axis_index("core")
    half_width = full_width // 2
    own_half = lax.all_gather(
        lax.dynamic_slice_in_dim(output_weight, mine * half_width, half_width, 1),
        BATCH,
        axis=0,
        tiled=True,
    )
    gathered_in = gather_batch(activations, 1)
    seq_rows = gathered_in.shape[1]
    def activate(rows_in):
        return jax.nn.gelu(normalize(rows_in, conv_gain)).astype(jnp.bfloat16)

    active = lax.optimization_barrier(activate(gathered_in))
    framed = with_halo(active, gathered_in, activate, SEQ, flank_rows)
    conv_sum = jnp.zeros((sample_count, local_out, seq_rows), jnp.float32)
    for offset in range(tap_count):
        conv_sum = conv_sum + jnp.einsum(
            "std,ed->set",
            framed[:, offset : offset + seq_rows],
            conv_weight[offset],
            preferred_element_type=jnp.float32,
        )
    column_start = lax.axis_index(BATCH) * local_out
    own_columns = lax.dynamic_slice_in_dim(gathered_in, column_start, local_out, 2)
    residual = jnp.transpose(own_columns, (0, 2, 1)).astype(jnp.float32)
    hidden_part = (residual + conv_sum).astype(jnp.bfloat16)
    hidden_full, own_half = lax.optimization_barrier((gather_batch(hidden_part, 1), own_half))
    hidden_float = hidden_full.astype(jnp.float32)
    norm_scale = lax.rsqrt(jnp.mean(hidden_float * hidden_float, axis=1, keepdims=True) + 1e-06)
    normed = (hidden_float * norm_scale * attention_gain[None, :, None]).astype(jnp.bfloat16)
    queries = (
        jnp.einsum("sdt,ed->ste", normed, query_weight, preferred_element_type=jnp.float32)
        * HD ** (-0.5)
    ).astype(jnp.bfloat16)
    kv_rows = jnp.einsum(
        "sdt,ked->kset",
        normed,
        jnp.stack([key_weight, value_weight]),
        preferred_element_type=jnp.float32,
    ).astype(jnp.bfloat16)
    kv_tile = lax.all_gather(kv_rows, SEQ, axis=1)
    batch_count = lax.axis_size(BATCH)
    attended = flash_attention(queries, kv_tile, batch_count)
    row_start = lax.axis_index(BATCH) * own_rows
    own_hidden = jnp.transpose(
        lax.dynamic_slice_in_dim(hidden_full, row_start, own_rows, 2), (0, 2, 1)
    ).astype(jnp.float32)
    head_width = attended.shape[3]
    arrived = lax.all_to_all(attended, BATCH, 0, 0, tiled=False)
    other_half = lax.ppermute(own_half, "core", [(0, 1), (1, 0)])
    full_output_weight = jnp.where(
        mine == 0,
        jnp.concatenate([own_half, other_half], axis=1),
        jnp.concatenate([other_half, own_half], axis=1),
    )
    branch_rows = jnp.einsum(
        "hstd,hdf->stf",
        arrived,
        full_output_weight.reshape(batch_count, head_width, -1),
        preferred_element_type=jnp.float32,
    )
    result = own_hidden + branch_rows
    return result.astype(jnp.bfloat16)


def solution(mesh):
    fine = jax.sharding.Mesh(
        mesh.devices.reshape(2, mesh.shape["seq"] // 4, 2, mesh.shape["batch"] // 2, 2),
        SEQ + BATCH,
    )
    placed = (
        P(None, SEQ + BATCH, None),
        P(),
        P(None, BATCH, None),
        P(),
        P(BATCH, None),
        P(BATCH, None),
        P(BATCH, None),
        P(BATCH, None),
    )
    return jax.shard_map(
        shards,
        mesh=fine,
        in_specs=placed,
        out_specs=P(None, SEQ + BATCH, None),
        check_vma=False,
    )
```
